32 devices in a mesh: dp: 4 (over y, x), expert: 8 (over z, core).
Axes of the slice: x: 2, y: 2, z: 4, core: 2. Of those that a mesh axis runs over, the one named last changes fastest.
Arguments:
- tokens: bfloat16 [4096, 7168], P(('dp', 'expert')), may hold values from -6 to 6
- steering: float32 [7168], replicated, may hold values from -6 to 6
- norm_gain: float32 [7168], replicated, may hold values from 0.1 to 1.9
- route_ids: int32 [4096, 8], P(('dp', 'expert')), may hold values from 0 to 255, as said below
- route_gates: int32 [4096, 8], P(('dp', 'expert')), may hold values from 1 to 65535
- gate_weight: bfloat16 [7168, 8192], P(None, 'expert'), may hold values from -0.0625 to 0.0625
- up_weight: bfloat16 [7168, 8192], P(None, 'expert'), may hold values from -0.0625 to 0.0625
- down_weight: bfloat16 [8192, 7168], P('expert'), may hold values from -0.125 to 0.125
- out_grad: bfloat16 [4096, 7168], P(('dp', 'expert')), may hold values from -6 to 6
Outputs:
- layer_out: bfloat16 [4096, 7168], P(('dp', 'expert'))
- in_grad: bfloat16 [4096, 7168], P(('dp', 'expert'))
- steer_grad: float32 [7168], replicated
The draws below stay inside these ranges and needn't reach their ends.
Inputs may be any that keep to these rules, and one draw needn't show every extreme that they name: `route_ids`: each row names 8 different experts. Among the 128 rows of one device no expert below 4 is named more than 8 times. One expert below 4, the same for every device, is named exactly 8 times by every device's rows, and on some devices every expert below 4 is named exactly 8 times.
All inputs are finite; a program needn't handle non-finite values.
Results may differ from the reference program's by a relative error of at most 0.0021.
Values may be sent and summed in bfloat16 or wider, within the bound.
No kernel may reach another device: no remote copies, remote signals or barrier semaphores. Data moves between devices by JAX's collectives and lax.ppermute only.
A program may use at most 128 MiB of HBM per device.

```python
from functools import partial
import jax
import jax.numpy as jnp
from jax import lax

D = 7168
EXPERTS = 256
FF = 2048
TOPK = 8
EXP_FLIGHT = 4
TOK_DEV = 128
GROUP = 2
HID_DEV = 1024
CAP = 8
TOKENS = 4096
N_DP = 4
N_EXPERT = 8


def draw_route_ids(key, part):
    sources = TOKENS // TOK_DEV
    key_hot = jax.random.fold_in(key, 11)
    key_count = jax.random.fold_in(key, 12)
    key_pick = jax.random.fold_in(key, 13)
    key_rest = jax.random.fold_in(key, 14)
    key_order = jax.random.fold_in(key, 15)
    key_full = jax.random.fold_in(key, 16)
    key_anchor = jax.random.fold_in(key, 17)
    hottest = jax.random.randint(key_hot, (), 0, EXP_FLIGHT)
    counts = jax.random.randint(key_count, (sources, EXP_FLIGHT), 0, CAP + 1)
    source_range = jnp.arange(sources, dtype=jnp.int32)
    anchor = jax.random.randint(key_anchor, (), 0, sources)
    full_sources = jax.random.randint(key_full, (sources,), 0, 4) == 0
    full_sources = jnp.logical_or(full_sources, source_range == anchor)
    counts = jnp.where(full_sources[:, None], CAP, counts)
    expert_range = jnp.arange(EXP_FLIGHT, dtype=jnp.int32)
    counts = jnp.where(expert_range[None, :] == hottest, CAP, counts)
    scores = jax.random.randint(key_pick, (sources, EXP_FLIGHT, TOK_DEV), 0, 1048576) * TOK_DEV + jnp.arange(TOK_DEV, dtype=jnp.int32)
    rank_of = jnp.argsort(jnp.argsort(scores, axis=-1, stable=True), axis=-1, stable=True)
    chosen = jnp.swapaxes(rank_of < counts[:, :, None], 1, 2)
    chosen = jnp.pad(chosen, ((0, 0), (0, 0), (0, TOPK - EXP_FLIGHT)))
    all_range = jnp.arange(EXPERTS, dtype=jnp.int32)
    other_scores = jax.random.randint(key_rest, (sources, TOK_DEV, EXPERTS), 0, 1048576) * EXPERTS + all_range
    other_scores = jnp.where(all_range < EXP_FLIGHT, -1, other_scores)
    others = lax.top_k(other_scores, TOPK)[1].astype(jnp.int32)
    slot_range = jnp.arange(TOPK, dtype=jnp.int32)
    named_ids = jnp.where(chosen, slot_range, others)
    order_scores = jax.random.randint(key_order, (sources, TOK_DEV, TOPK), 0, 1048576) * TOPK + slot_range
    reorder = jnp.argsort(order_scores, axis=-1, stable=True)
    named_ids = jnp.take_along_axis(named_ids, reorder, axis=-1)
    return named_ids.reshape(TOKENS, TOPK).astype(jnp.int32)


def with_ends(entries, stream_key, low, top_value):
    spot = [jax.random.randint(jax.random.fold_in(stream_key, axis), (), 0, length) for axis, length in enumerate(entries.shape)]
    main_axis = entries.shape.index(max(entries.shape))
    beside = spot[:main_axis] + [(spot[main_axis] + 1) % entries.shape[main_axis]] + spot[main_axis + 1:]
    return entries.at[tuple(spot)].set(low).at[tuple(beside)].set(top_value)


def spiked(result, rng, source, target, parts, factor):
    def block_of(dim):
        return (jnp.arange(result.shape[dim]) // (result.shape[dim] // parts)).reshape((-1,) + (1,) * (result.ndim - 1 - dim))

    one_side = jax.random.permutation(rng, parts)[block_of(target)]
    other_side = (block_of(target) + parts // 2) % parts
    return jnp.where((block_of(source) == one_side) | (block_of(source) == other_side), factor * result, result)


def steps_of(stream_key, shape, pieces, least, largest):
    def one(dim, parts):
        heights = jax.random.uniform(jax.random.fold_in(jax.random.fold_in(stream_key, 6), dim), (parts,), jnp.float32, least / len(pieces), largest / len(pieces))
        return jnp.repeat(jnp.exp(heights), shape[dim] // parts).reshape((-1,) + (1,) * (len(shape) - dim - 1))

    factor_of = one(*pieces[0])
    for cut in pieces[1:]:
        factor_of = factor_of * one(*cut)
    return factor_of


def centred(rng, extent, spread, reach, pieces=(), kind=jnp.bfloat16):
    factor_of = steps_of(rng, extent, pieces, -0.22, 0.18) if pieces else 1.0
    values = jax.random.normal(rng, extent, jnp.float32) * spread * factor_of
    return jnp.minimum(jnp.maximum(values, -reach), reach).astype(kind)


def heavy_noise(rng, dims, scale, most, shards, heavy, kind=jnp.bfloat16):
    drawn = scale * jax.random.normal(rng, dims, jnp.float32)
    if shards:
        drawn = drawn * steps_of(rng, dims, shards, -0.22, 0.18)
    return jnp.clip(spiked(drawn, jax.random.fold_in(rng, 3), *heavy), -most, most).astype(kind)


def setup_inputs(seed: int = 0) -> dict:
    splits = jax.random.split(jax.random.key(seed), 10)
    return {
        "tokens": centred(splits[0], (TOKENS, D), 1.0, 6.0, ((0, 32),)),
        "steering": centred(splits[1], (D,), 1.0, 6.0, (), jnp.float32),
        "norm_gain": jnp.clip(1.0 + 0.18 * jax.random.normal(splits[2], (D,), jnp.float32), 0.1, 1.9),
        "route_ids": draw_route_ids(jax.random.fold_in(splits[9], 71), 0),
        "route_gates": with_ends(jax.random.randint(splits[4], (TOKENS, TOPK), 1, 65536), jax.random.fold_in(splits[4], 1), 1, 65535).astype(jnp.int32),
        "gate_weight": centred(splits[5], (D, EXP_FLIGHT * FF), D ** -0.5, 0.0625, ((1, 8),)),
        "up_weight": centred(splits[6], (D, EXP_FLIGHT * FF), D ** -0.5, 0.0625, ((1, 8),)),
        "down_weight": centred(splits[7], (EXP_FLIGHT * FF, D), FF ** -0.5, 0.125, ((0, 8),)),
        "out_grad": heavy_noise(splits[8], (TOKENS, D), 1.0, 6.0, ((0, 32),), (0, 1, 32, 2.75)),
    }


EPSILON = 1e-06
GATE_UNIT = 1.0 / 65536.0

def slot_tables(route_ids, route_gates, flight, capacity):
    count_rows = route_ids.shape[0]
    expert_range = jnp.arange(flight, dtype=jnp.int32)
    hit_mask = route_ids[:, :, None] == expert_range[None, None, :]
    member = jnp.any(hit_mask, axis=1)
    scaled = route_gates.astype(jnp.float32) * GATE_UNIT
    weights = lax.optimization_barrier(jnp.sum(jnp.where(hit_mask, scaled[:, :, None], 0.0), axis=1))
    position = jnp.cumsum(member.astype(jnp.int32), axis=0).astype(jnp.int32) - 1
    slot_of = jnp.where(member, position, capacity)
    slot_range = jnp.arange(capacity, dtype=jnp.int32)
    matches = slot_of[:, :, None] == slot_range[None, None, :]
    row_range = jnp.arange(count_rows, dtype=jnp.int32)
    slot_table = lax.optimization_barrier(jnp.sum(jnp.where(matches, row_range[:, None, None], 0), axis=0)).astype(jnp.int32)
    filled = jnp.any(matches, axis=0)
    combine = jnp.where(matches, weights[:, :, None], 0.0).reshape(count_rows, flight * capacity)
    return (slot_table, filled, combine)

def dispatch_rows(values, slot_table, filled):
    picked = values[slot_table]
    return jnp.where(filled[:, :, None], picked, jnp.zeros((), values.dtype))

def normalize(tokens, steering, norm_gain):
    residual = tokens.astype(jnp.float32) + steering
    inverse = lax.rsqrt(lax.optimization_barrier(jnp.mean(residual * residual, axis=-1, keepdims=True)) + EPSILON)
    normed = (residual * inverse * norm_gain).astype(jnp.bfloat16)
    return (residual, inverse, normed)

def norm_backward(residual, inverse, norm_gain, back_normed, out_grad):
    scaled = back_normed * norm_gain
    inner_mean = lax.optimization_barrier(jnp.mean(scaled * residual, axis=-1, keepdims=True))
    cubed = inverse * inverse * inverse
    return out_grad.astype(jnp.float32) + inverse * scaled - residual * cubed * inner_mean

def share_forward(token_rows, gate_cols, up_cols, down_rows):
    gate_pre = jnp.dot(token_rows, gate_cols, preferred_element_type=jnp.float32)
    up_pre = jnp.dot(token_rows, up_cols, preferred_element_type=jnp.float32)
    hidden = (jax.nn.silu(gate_pre) * up_pre).astype(jnp.bfloat16)
    forward = jnp.dot(hidden, down_rows, preferred_element_type=jnp.float32).astype(jnp.bfloat16)
    return (forward, gate_pre, up_pre)

def share_backward(grad_rows, gate_pre, up_pre, gate_cols, up_cols, down_rows):
    contract = (((1,), (1,)), ((), ()))
    back_hidden = lax.dot_general(grad_rows, down_rows, contract, preferred_element_type=jnp.float32)
    sigmoid = jax.nn.sigmoid(gate_pre)
    back_up = (back_hidden * gate_pre * sigmoid).astype(jnp.bfloat16)
    back_gate = (back_hidden * up_pre * sigmoid * (1.0 + gate_pre * (1.0 - sigmoid))).astype(jnp.bfloat16)
    backward = lax.dot_general(back_gate, gate_cols, contract, preferred_element_type=jnp.float32)
    backward = backward + lax.dot_general(back_up, up_cols, contract, preferred_element_type=jnp.float32)
    return backward.astype(jnp.bfloat16)

def apply_combine(combine, partial_sums):
    return jnp.dot(combine, partial_sums, precision=lax.Precision.HIGHEST)

def reference(tokens, steering, norm_gain, route_ids, route_gates, gate_weight, up_weight, down_weight, out_grad):
    sources = TOKENS // TOK_DEV
    residual, inverse, normed = normalize(tokens, steering, norm_gain)
    tables = partial(slot_tables, flight=EXP_FLIGHT, capacity=CAP)
    slot_table, filled, combine = jax.vmap(tables)(route_ids.reshape(sources, TOK_DEV, TOPK), route_gates.reshape(sources, TOK_DEV, TOPK))
    rows = jax.vmap(dispatch_rows)(normed.reshape(sources, TOK_DEV, D), slot_table, filled)
    grads_all = jax.vmap(dispatch_rows)(out_grad.reshape(sources, TOK_DEV, D), slot_table, filled)
    rows = rows.reshape(N_DP, N_EXPERT, EXP_FLIGHT, CAP, D).transpose(0, 2, 1, 3, 4).reshape(N_DP * EXP_FLIGHT, N_EXPERT * CAP, D)
    grads_all = grads_all.reshape(N_DP, N_EXPERT, EXP_FLIGHT, CAP, D).transpose(0, 2, 1, 3, 4).reshape(N_DP * EXP_FLIGHT, N_EXPERT * CAP, D)
    expert_of = jnp.tile(jnp.arange(EXP_FLIGHT, dtype=jnp.int32), N_DP)

    def one_expert(operands):
        block_rows, block_grads, expert = operands

        def one_share(carry, share_index):
            first_col = ((expert * GROUP + share_index) * HID_DEV).astype(jnp.int32)
            gate_cols = lax.dynamic_slice_in_dim(gate_weight, first_col, HID_DEV, 1)
            up_cols = lax.dynamic_slice_in_dim(up_weight, first_col, HID_DEV, 1)
            down_rows = lax.dynamic_slice_in_dim(down_weight, first_col, HID_DEV, 0)
            forward, gate_pre, up_pre = share_forward(block_rows, gate_cols, up_cols, down_rows)
            backward = share_backward(block_grads, gate_pre, up_pre, gate_cols, up_cols, down_rows)
            return ((carry[0] + forward.astype(jnp.float32), carry[1] + backward.astype(jnp.float32)), None)
        zero_rows = jnp.zeros((N_EXPERT * CAP, D), jnp.float32)
        return lax.scan(one_share, (zero_rows, zero_rows), jnp.arange(GROUP, dtype=jnp.int32))[0]
    out_sums, grad_sums = lax.map(one_expert, (rows, grads_all, expert_of))
    out_sums = out_sums.reshape(N_DP, EXP_FLIGHT, N_EXPERT, CAP, D).transpose(0, 2, 1, 3, 4).reshape(sources, EXP_FLIGHT * CAP, D)
    grad_sums = grad_sums.reshape(N_DP, EXP_FLIGHT, N_EXPERT, CAP, D).transpose(0, 2, 1, 3, 4).reshape(sources, EXP_FLIGHT * CAP, D)
    mixture = jax.vmap(apply_combine)(combine, out_sums).reshape(TOKENS, D)
    back_normed = jax.vmap(apply_combine)(combine, grad_sums).reshape(TOKENS, D)
    layer_out = (residual + mixture).astype(jnp.bfloat16)
    total_grad = norm_backward(residual, inverse, norm_gain, back_normed, out_grad)
    return (layer_out, total_grad.astype(jnp.bfloat16), lax.optimization_barrier(jnp.sum(total_grad, axis=0)))
```

```python
import jax
import jax.numpy as jnp
from jax import lax
from jax.sharding import PartitionSpec as P
from jax.experimental import pallas as pl
from jax.experimental.pallas import tpu as pltpu

EXP_FLIGHT = 4
CAP = 8


EPSILON = 1e-06
GATE_UNIT = 1.0 / 65536.0


def slot_tables(route_ids, route_gates, flight, capacity):
    count_rows = route_ids.shape[0]
    expert_range = jnp.arange(flight, dtype=jnp.int32)
    hit_mask = route_ids[:, :, None] == expert_range[None, None, :]
    member = jnp.any(hit_mask, axis=1)
    scaled = route_gates.astype(jnp.float32) * GATE_UNIT
    weights = jnp.sum(jnp.where(hit_mask, scaled[:, :, None], 0.0), axis=1)
    position = jnp.cumsum(member.astype(jnp.int32), axis=0) - 1
    slot_of = jnp.where(member, position, capacity)
    slot_range = jnp.arange(capacity, dtype=jnp.int32)
    matches = slot_of[:, :, None] == slot_range[None, None, :]
    row_range = jnp.arange(count_rows, dtype=jnp.int32)
    slot_table = jnp.sum(jnp.where(matches, row_range[:, None, None], 0), axis=0)
    filled = jnp.any(matches, axis=0)
    combine = jnp.where(matches, weights[:, :, None], 0.0).reshape(count_rows, flight * capacity)
    return (slot_table, filled, combine)


def dispatch_rows(values, slot_table, filled):
    picked = values[slot_table]
    return jnp.where(filled[:, :, None], picked, jnp.zeros((), values.dtype))


def normalize(tokens, steering, norm_gain):
    residual = tokens.astype(jnp.float32) + steering
    inverse = lax.rsqrt(jnp.mean(residual * residual, axis=-1, keepdims=True) + EPSILON)
    normed = (residual * inverse * norm_gain).astype(jnp.bfloat16)
    return (residual, inverse, normed)


def norm_backward(residual, inverse, norm_gain, back_normed, out_grad):
    scaled = back_normed * norm_gain
    inner_mean = jnp.mean(scaled * residual, axis=-1, keepdims=True)
    cubed = inverse * inverse * inverse
    return out_grad.astype(jnp.float32) + inverse * scaled - residual * cubed * inner_mean


def share_forward(token_rows, gate_cols, up_cols, down_rows):
    gate_pre = jnp.dot(token_rows, gate_cols, preferred_element_type=jnp.float32)
    up_pre = jnp.dot(token_rows, up_cols, preferred_element_type=jnp.float32)
    hidden = (jax.nn.silu(gate_pre) * up_pre).astype(jnp.bfloat16)
    forward = jnp.dot(hidden, down_rows, preferred_element_type=jnp.float32).astype(jnp.bfloat16)
    return (forward, gate_pre, up_pre)


def share_backward(grad_rows, gate_pre, up_pre, gate_cols, up_cols, down_rows):
    contract = (((1,), (1,)), ((), ()))
    back_hidden = lax.dot_general(
        grad_rows, down_rows, contract, preferred_element_type=jnp.float32
    )
    sigmoid = jax.nn.sigmoid(gate_pre)
    back_up = (back_hidden * gate_pre * sigmoid).astype(jnp.bfloat16)
    back_gate = (back_hidden * up_pre * sigmoid * (1.0 + gate_pre * (1.0 - sigmoid))).astype(
        jnp.bfloat16
    )
    backward = lax.dot_general(back_gate, gate_cols, contract, preferred_element_type=jnp.float32)
    backward = backward + lax.dot_general(
        back_up, up_cols, contract, preferred_element_type=jnp.float32
    )
    return backward.astype(jnp.bfloat16)


def _expert_kernel(x_ref, y_ref, g_ref, u_ref, d_ref, out_ref, back_ref, acc_o, acc_b):
    j = pl.program_id(1)
    @pl.when(j == 0)
    def _():
        acc_o[...] = jnp.zeros_like(acc_o)
        acc_b[...] = jnp.zeros_like(acc_b)
    x = x_ref[...]
    y = y_ref[...]
    gw = g_ref[...]
    uw = u_ref[...]
    dw = d_ref[...]
    nt = (((1,), (1,)), ((), ()))
    g = jnp.dot(x, gw, preferred_element_type=jnp.float32)
    u = jnp.dot(x, uw, preferred_element_type=jnp.float32)
    sig = jax.nn.sigmoid(g)
    hidden = (g * sig * u).astype(jnp.bfloat16)
    bh = lax.dot_general(y, dw, nt, preferred_element_type=jnp.float32)
    back_up = (bh * g * sig).astype(jnp.bfloat16)
    back_gate = (bh * u * sig * (1.0 + g * (1.0 - sig))).astype(jnp.bfloat16)
    acc_o[...] += jnp.dot(hidden, dw, preferred_element_type=jnp.float32)
    acc_b[...] += (lax.dot_general(back_gate, gw, nt, preferred_element_type=jnp.float32)
                   + lax.dot_general(back_up, uw, nt, preferred_element_type=jnp.float32))
    @pl.when(j == pl.num_programs(1) - 1)
    def _():
        out_ref[...] = acc_o[...].astype(out_ref.dtype)
        back_ref[...] = acc_b[...].astype(back_ref.dtype)

def expert_share(x, y, gw, uw, dw):
    rows, feat = x.shape
    hid = gw.shape[1]
    rb = min(rows, 128)
    hb = min(hid, 256)
    return pl.pallas_call(
        _expert_kernel,
        grid=(rows // rb, hid // hb),
        in_specs=[
            pl.BlockSpec((rb, feat), lambda i, j: (i, 0)),
            pl.BlockSpec((rb, feat), lambda i, j: (i, 0)),
            pl.BlockSpec((feat, hb), lambda i, j: (0, j)),
            pl.BlockSpec((feat, hb), lambda i, j: (0, j)),
            pl.BlockSpec((hb, feat), lambda i, j: (j, 0)),
        ],
        out_specs=[
            pl.BlockSpec((rb, feat), lambda i, j: (i, 0)),
            pl.BlockSpec((rb, feat), lambda i, j: (i, 0)),
        ],
        out_shape=[jax.ShapeDtypeStruct((rows, feat), jnp.bfloat16)] * 2,
        scratch_shapes=[pltpu.VMEM((rb, feat), jnp.float32)] * 2,
        compiler_params=pltpu.CompilerParams(
            dimension_semantics=("arbitrary", "arbitrary"), vmem_limit_bytes=56 * 1024 * 1024
        ),
    )(x, y, gw, uw, dw)


def apply_combine(combine, partial_sums):
    return jnp.dot(combine, partial_sums, precision=lax.Precision.HIGHEST)


def shards(
    tokens,
    steering,
    norm_gain,
    route_ids,
    route_gates,
    gate_weight,
    up_weight,
    down_weight,
    out_grad,
):
    expert_count = lax.axis_size("expert")
    flight = EXP_FLIGHT
    group_size = expert_count // flight
    capacity = CAP
    feature_count = tokens.shape[1]
    residual, inverse, normed = normalize(tokens, steering, norm_gain)
    slot_table, filled, combine = slot_tables(route_ids, route_gates, flight, capacity)
    packed = jnp.stack(
        [dispatch_rows(normed, slot_table, filled), dispatch_rows(out_grad, slot_table, filled)],
        axis=1,
    )
    sending = jnp.repeat(packed, group_size, axis=0)
    arrived = lax.all_to_all(sending, "expert", split_axis=0, concat_axis=0, tiled=True)
    local_rows = arrived[:, 0].reshape(expert_count * capacity, feature_count)
    local_grads = arrived[:, 1].reshape(expert_count * capacity, feature_count)
    forward, backward = expert_share(local_rows, local_grads, gate_weight, up_weight, down_weight)
    came_out = lax.all_to_all(
        forward.reshape(expert_count, capacity, feature_count),
        "expert",
        split_axis=0,
        concat_axis=0,
        tiled=True,
    )
    came_grad = lax.all_to_all(
        backward.reshape(expert_count, capacity, feature_count),
        "expert",
        split_axis=0,
        concat_axis=0,
        tiled=True,
    )
    out_sums = (
        came_out.reshape(flight, group_size, capacity, feature_count)
        .astype(jnp.float32)
        .sum(axis=1)
    )
    grad_sums = (
        came_grad.reshape(flight, group_size, capacity, feature_count)
        .astype(jnp.float32)
        .sum(axis=1)
    )
    mixture = apply_combine(combine, out_sums.reshape(flight * capacity, feature_count))
    back_normed = apply_combine(combine, grad_sums.reshape(flight * capacity, feature_count))
    layer_out = (residual + mixture).astype(jnp.bfloat16)
    total_grad = norm_backward(residual, inverse, norm_gain, back_normed, out_grad)
    steer_grad = lax.psum(jnp.sum(total_grad, axis=0), ("dp", "expert"))
    return (layer_out, total_grad.astype(jnp.bfloat16), steer_grad)


def solution(mesh):
    in_specs = (
        P(("dp", "expert"), None),
        P(),
        P(),
        P(("dp", "expert"), None),
        P(("dp", "expert"), None),
        P(None, "expert"),
        P(None, "expert"),
        P("expert", None),
        P(("dp", "expert"), None),
    )
    out_specs = (P(("dp", "expert"), None), P(("dp", "expert"), None), P())
    return jax.shard_map(shards, mesh=mesh, in_specs=in_specs, out_specs=out_specs, check_vma=False)
```

```python
import jax
import jax.numpy as jnp
from jax import lax
from jax.sharding import PartitionSpec as P
from jax.experimental import pallas as pl
from jax.experimental.pallas import tpu as pltpu

EXP_FLIGHT = 4
CAP = 8


EPSILON = 1e-06
GATE_UNIT = 1.0 / 65536.0


def slot_tables(route_ids, route_gates, flight, capacity):
    count_rows = route_ids.shape[0]
    expert_range = jnp.arange(flight, dtype=jnp.int32)
    hit_mask = route_ids[:, :, None] == expert_range[None, None, :]
    member = jnp.any(hit_mask, axis=1)
    scaled = route_gates.astype(jnp.float32) * GATE_UNIT
    weights = jnp.sum(jnp.where(hit_mask, scaled[:, :, None], 0.0), axis=1)
    position = jnp.cumsum(member.astype(jnp.int32), axis=0) - 1
    slot_of = jnp.where(member, position, capacity)
    slot_range = jnp.arange(capacity, dtype=jnp.int32)
    matches = slot_of[:, :, None] == slot_range[None, None, :]
    row_range = jnp.arange(count_rows, dtype=jnp.int32)
    slot_table = jnp.sum(jnp.where(matches, row_range[:, None, None], 0), axis=0)
    filled = jnp.any(matches, axis=0)
    combine = jnp.where(matches, weights[:, :, None], 0.0).reshape(count_rows, flight * capacity)
    return (slot_table, filled, combine)


def dispatch_rows(values, slot_table, filled):
    picked = values[slot_table]
    return jnp.where(filled[:, :, None], picked, jnp.zeros((), values.dtype))


def normalize(tokens, steering, norm_gain):
    residual = tokens.astype(jnp.float32) + steering
    inverse = lax.rsqrt(jnp.mean(residual * residual, axis=-1, keepdims=True) + EPSILON)
    normed = (residual * inverse * norm_gain).astype(jnp.bfloat16)
    return (residual, inverse, normed)


def norm_backward(residual, inverse, norm_gain, back_normed, out_grad):
    scaled = back_normed * norm_gain
    inner_mean = jnp.mean(scaled * residual, axis=-1, keepdims=True)
    cubed = inverse * inverse * inverse
    return out_grad.astype(jnp.float32) + inverse * scaled - residual * cubed * inner_mean


def share_forward(token_rows, gate_cols, up_cols, down_rows):
    gate_pre = jnp.dot(token_rows, gate_cols, preferred_element_type=jnp.float32)
    up_pre = jnp.dot(token_rows, up_cols, preferred_element_type=jnp.float32)
    hidden = (jax.nn.silu(gate_pre) * up_pre).astype(jnp.bfloat16)
    forward = jnp.dot(hidden, down_rows, preferred_element_type=jnp.float32).astype(jnp.bfloat16)
    return (forward, gate_pre, up_pre)


def share_backward(grad_rows, gate_pre, up_pre, gate_cols, up_cols, down_rows):
    contract = (((1,), (1,)), ((), ()))
    back_hidden = lax.dot_general(
        grad_rows, down_rows, contract, preferred_element_type=jnp.float32
    )
    sigmoid = jax.nn.sigmoid(gate_pre)
    back_up = (back_hidden * gate_pre * sigmoid).astype(jnp.bfloat16)
    back_gate = (back_hidden * up_pre * sigmoid * (1.0 + gate_pre * (1.0 - sigmoid))).astype(
        jnp.bfloat16
    )
    backward = lax.dot_general(back_gate, gate_cols, contract, preferred_element_type=jnp.float32)
    backward = backward + lax.dot_general(
        back_up, up_cols, contract, preferred_element_type=jnp.float32
    )
    return backward.astype(jnp.bfloat16)


def _expert_kernel(x_ref, y_ref, g_ref, u_ref, d_ref, out_ref, back_ref, acc_o, acc_b):
    j = pl.program_id(1)
    @pl.when(j == 0)
    def _():
        acc_o[...] = jnp.zeros_like(acc_o)
        acc_b[...] = jnp.zeros_like(acc_b)
    x = x_ref[...]
    y = y_ref[...]
    gw = g_ref[...]
    uw = u_ref[...]
    dw = d_ref[...]
    nt = (((1,), (1,)), ((), ()))
    g = jnp.dot(x, gw, preferred_element_type=jnp.float32)
    u = jnp.dot(x, uw, preferred_element_type=jnp.float32)
    sig = jax.nn.sigmoid(g)
    hidden = (g * sig * u).astype(jnp.bfloat16)
    bh = lax.dot_general(y, dw, nt, preferred_element_type=jnp.float32)
    back_up = (bh * g * sig).astype(jnp.bfloat16)
    back_gate = (bh * u * sig * (1.0 + g * (1.0 - sig))).astype(jnp.bfloat16)
    acc_o[...] += jnp.dot(hidden, dw, preferred_element_type=jnp.float32)
    acc_b[...] += (lax.dot_general(back_gate, gw, nt, preferred_element_type=jnp.float32)
                   + lax.dot_general(back_up, uw, nt, preferred_element_type=jnp.float32))
    @pl.when(j == pl.num_programs(1) - 1)
    def _():
        out_ref[...] = acc_o[...].astype(out_ref.dtype)
        back_ref[...] = acc_b[...].astype(back_ref.dtype)

def expert_share(x, y, gw, uw, dw):
    rows, feat = x.shape
    hid = gw.shape[1]
    rb = min(rows, 128)
    hb = min(hid, 256)
    return pl.pallas_call(
        _expert_kernel,
        grid=(rows // rb, hid // hb),
        in_specs=[
            pl.BlockSpec((rb, feat), lambda i, j: (i, 0)),
            pl.BlockSpec((rb, feat), lambda i, j: (i, 0)),
            pl.BlockSpec((feat, hb), lambda i, j: (0, j)),
            pl.BlockSpec((feat, hb), lambda i, j: (0, j)),
            pl.BlockSpec((hb, feat), lambda i, j: (j, 0)),
        ],
        out_specs=[
            pl.BlockSpec((rb, feat), lambda i, j: (i, 0)),
            pl.BlockSpec((rb, feat), lambda i, j: (i, 0)),
        ],
        out_shape=[jax.ShapeDtypeStruct((rows, feat), jnp.bfloat16)] * 2,
        scratch_shapes=[pltpu.VMEM((rb, feat), jnp.float32)] * 2,
        compiler_params=pltpu.CompilerParams(
            dimension_semantics=("arbitrary", "arbitrary"), vmem_limit_bytes=56 * 1024 * 1024
        ),
    )(x, y, gw, uw, dw)


def apply_combine(combine, partial_sums):
    return jnp.dot(combine, partial_sums, precision=lax.Precision.HIGHEST)


def group_perm(expert_count, group_size, shift):
    return [
        (d, (d // group_size) * group_size + (d % group_size + shift) % group_size)
        for d in range(expert_count)
    ]


def group_gather(piece, member, expert_count, group_size):
    got = [piece]
    for shift in range(1, group_size):
        got.append(lax.ppermute(piece, "expert", group_perm(expert_count, group_size, shift)))
    stacked = jnp.stack(got)
    order = (member - jnp.arange(group_size, dtype=jnp.int32)) % group_size
    return jnp.take(stacked, order, axis=0)


def group_reduce_scatter(pieces, member, expert_count, group_size, axis):
    total = lax.dynamic_index_in_dim(pieces, member, axis, keepdims=False).astype(jnp.float32)
    for shift in range(1, group_size):
        target = (member + shift) % group_size
        part = lax.dynamic_index_in_dim(pieces, target, axis, keepdims=False)
        moved = lax.ppermute(part, "expert", group_perm(expert_count, group_size, shift))
        total = total + moved.astype(jnp.float32)
    return total


def shards(
    tokens,
    steering,
    norm_gain,
    route_ids,
    route_gates,
    gate_weight,
    up_weight,
    down_weight,
    out_grad,
):
    expert_count = lax.axis_size("expert")
    flight = EXP_FLIGHT
    group_size = expert_count // flight
    capacity = CAP
    feature_count = tokens.shape[1]
    piece = feature_count // group_size
    member = lax.axis_index("expert") % group_size
    residual, inverse, normed = normalize(tokens, steering, norm_gain)
    slot_table, filled, combine = slot_tables(route_ids, route_gates, flight, capacity)
    packed = jnp.stack(
        [dispatch_rows(normed, slot_table, filled), dispatch_rows(out_grad, slot_table, filled)],
        axis=1,
    )
    sending = (
        packed.reshape(flight, 2, capacity, group_size, piece)
        .transpose(0, 3, 1, 2, 4)
        .reshape(expert_count, 2, capacity, piece)
    )
    arrived = lax.all_to_all(sending, "expert", split_axis=0, concat_axis=0, tiled=True)
    whole = group_gather(arrived, member, expert_count, group_size)
    rows = whole.transpose(1, 2, 3, 0, 4).reshape(expert_count, 2, capacity, feature_count)
    local_rows = rows[:, 0].reshape(expert_count * capacity, feature_count)
    local_grads = rows[:, 1].reshape(expert_count * capacity, feature_count)
    forward, backward = expert_share(local_rows, local_grads, gate_weight, up_weight, down_weight)
    both = jnp.stack(
        [
            forward.reshape(expert_count, capacity, feature_count),
            backward.reshape(expert_count, capacity, feature_count),
        ],
        axis=1,
    ).reshape(expert_count, 2, capacity, group_size, piece)
    summed = group_reduce_scatter(both, member, expert_count, group_size, 3)
    came = lax.all_to_all(
        summed.astype(jnp.bfloat16), "expert", split_axis=0, concat_axis=0, tiled=True
    )
    sums = (
        came.reshape(flight, group_size, 2, capacity, piece)
        .transpose(0, 2, 3, 1, 4)
        .reshape(flight, 2, capacity * feature_count)
        .astype(jnp.float32)
    )
    out_sums = sums[:, 0].reshape(flight * capacity, feature_count)
    grad_sums = sums[:, 1].reshape(flight * capacity, feature_count)
    mixture = apply_combine(combine, out_sums)
    back_normed = apply_combine(combine, grad_sums)
    layer_out = (residual + mixture).astype(jnp.bfloat16)
    total_grad = norm_backward(residual, inverse, norm_gain, back_normed, out_grad)
    steer_grad = lax.psum(jnp.sum(total_grad, axis=0), ("dp", "expert"))
    return (layer_out, total_grad.astype(jnp.bfloat16), steer_grad)


def solution(mesh):
    in_specs = (
        P(("dp", "expert"), None),
        P(),
        P(),
        P(("dp", "expert"), None),
        P(("dp", "expert"), None),
        P(None, "expert"),
        P(None, "expert"),
        P("expert", None),
        P(("dp", "expert"), None),
    )
    out_specs = (P(("dp", "expert"), None), P(("dp", "expert"), None), P())
    return jax.shard_map(shards, mesh=mesh, in_specs=in_specs, out_specs=out_specs, check_vma=False)
```

```python
import jax
import jax.numpy as jnp
from jax import lax
from jax.sharding import PartitionSpec as P
from jax.experimental import pallas as pl
from jax.experimental.pallas import tpu as pltpu

EXP_FLIGHT = 4
CAP = 8


EPSILON = 1e-06
GATE_UNIT = 1.0 / 65536.0


def slot_tables(route_ids, route_gates, flight, capacity):
    count_rows = route_ids.shape[0]
    expert_range = jnp.arange(flight, dtype=jnp.int32)
    hit_mask = route_ids[:, :, None] == expert_range[None, None, :]
    member = jnp.any(hit_mask, axis=1)
    scaled = route_gates.astype(jnp.float32) * GATE_UNIT
    weights = jnp.sum(jnp.where(hit_mask, scaled[:, :, None], 0.0), axis=1)
    position = jnp.cumsum(member.astype(jnp.int32), axis=0) - 1
    slot_of = jnp.where(member, position, capacity)
    slot_range = jnp.arange(capacity, dtype=jnp.int32)
    matches = slot_of[:, :, None] == slot_range[None, None, :]
    row_range = jnp.arange(count_rows, dtype=jnp.int32)
    slot_table = jnp.sum(jnp.where(matches, row_range[:, None, None], 0), axis=0)
    filled = jnp.any(matches, axis=0)
    combine = jnp.where(matches, weights[:, :, None], 0.0).reshape(count_rows, flight * capacity)
    return (slot_table, filled, combine)


def dispatch_rows(values, slot_table, filled):
    picked = values[slot_table]
    return jnp.where(filled[:, :, None], picked, jnp.zeros((), values.dtype))


def normalize(tokens, steering, norm_gain):
    residual = tokens.astype(jnp.float32) + steering
    inverse = lax.rsqrt(jnp.mean(residual * residual, axis=-1, keepdims=True) + EPSILON)
    normed = (residual * inverse * norm_gain).astype(jnp.bfloat16)
    return (residual, inverse, normed)


def norm_backward(residual, inverse, norm_gain, back_normed, out_grad):
    scaled = back_normed * norm_gain
    inner_mean = jnp.mean(scaled * residual, axis=-1, keepdims=True)
    cubed = inverse * inverse * inverse
    return out_grad.astype(jnp.float32) + inverse * scaled - residual * cubed * inner_mean


def share_forward(token_rows, gate_cols, up_cols, down_rows):
    gate_pre = jnp.dot(token_rows, gate_cols, preferred_element_type=jnp.float32)
    up_pre = jnp.dot(token_rows, up_cols, preferred_element_type=jnp.float32)
    hidden = (jax.nn.silu(gate_pre) * up_pre).astype(jnp.bfloat16)
    forward = jnp.dot(hidden, down_rows, preferred_element_type=jnp.float32).astype(jnp.bfloat16)
    return (forward, gate_pre, up_pre)


def share_backward(grad_rows, gate_pre, up_pre, gate_cols, up_cols, down_rows):
    contract = (((1,), (1,)), ((), ()))
    back_hidden = lax.dot_general(
        grad_rows, down_rows, contract, preferred_element_type=jnp.float32
    )
    sigmoid = jax.nn.sigmoid(gate_pre)
    back_up = (back_hidden * gate_pre * sigmoid).astype(jnp.bfloat16)
    back_gate = (back_hidden * up_pre * sigmoid * (1.0 + gate_pre * (1.0 - sigmoid))).astype(
        jnp.bfloat16
    )
    backward = lax.dot_general(back_gate, gate_cols, contract, preferred_element_type=jnp.float32)
    backward = backward + lax.dot_general(
        back_up, up_cols, contract, preferred_element_type=jnp.float32
    )
    return backward.astype(jnp.bfloat16)


def _expert_kernel(x_ref, y_ref, g_ref, u_ref, d_ref, out_ref, back_ref, acc_o, acc_b):
    j = pl.program_id(1)
    @pl.when(j == 0)
    def _():
        acc_o[...] = jnp.zeros_like(acc_o)
        acc_b[...] = jnp.zeros_like(acc_b)
    x = x_ref[...]
    y = y_ref[...]
    gw = g_ref[...]
    uw = u_ref[...]
    dw = d_ref[...]
    nt = (((1,), (1,)), ((), ()))
    g = jnp.dot(x, gw, preferred_element_type=jnp.float32)
    u = jnp.dot(x, uw, preferred_element_type=jnp.float32)
    sig = jax.nn.sigmoid(g)
    hidden = (g * sig * u).astype(jnp.bfloat16)
    bh = lax.dot_general(y, dw, nt, preferred_element_type=jnp.float32)
    back_up = (bh * g * sig).astype(jnp.bfloat16)
    back_gate = (bh * u * sig * (1.0 + g * (1.0 - sig))).astype(jnp.bfloat16)
    acc_o[...] += jnp.dot(hidden, dw, preferred_element_type=jnp.float32)
    acc_b[...] += (lax.dot_general(back_gate, gw, nt, preferred_element_type=jnp.float32)
                   + lax.dot_general(back_up, uw, nt, preferred_element_type=jnp.float32))
    @pl.when(j == pl.num_programs(1) - 1)
    def _():
        out_ref[...] = acc_o[...].astype(out_ref.dtype)
        back_ref[...] = acc_b[...].astype(back_ref.dtype)

def expert_share(x, y, gw, uw, dw):
    rows, feat = x.shape
    hid = gw.shape[1]
    rb = min(rows, 128)
    hb = min(hid, 256)
    return pl.pallas_call(
        _expert_kernel,
        grid=(rows // rb, hid // hb),
        in_specs=[
            pl.BlockSpec((rb, feat), lambda i, j: (i, 0)),
            pl.BlockSpec((rb, feat), lambda i, j: (i, 0)),
            pl.BlockSpec((feat, hb), lambda i, j: (0, j)),
            pl.BlockSpec((feat, hb), lambda i, j: (0, j)),
            pl.BlockSpec((hb, feat), lambda i, j: (j, 0)),
        ],
        out_specs=[
            pl.BlockSpec((rb, feat), lambda i, j: (i, 0)),
            pl.BlockSpec((rb, feat), lambda i, j: (i, 0)),
        ],
        out_shape=[jax.ShapeDtypeStruct((rows, feat), jnp.bfloat16)] * 2,
        scratch_shapes=[pltpu.VMEM((rb, feat), jnp.float32)] * 2,
        compiler_params=pltpu.CompilerParams(
            dimension_semantics=("arbitrary", "arbitrary"), vmem_limit_bytes=56 * 1024 * 1024
        ),
    )(x, y, gw, uw, dw)


def apply_combine(combine, partial_sums):
    return jnp.dot(combine, partial_sums, precision=lax.Precision.HIGHEST)


def group_perm(expert_count, group_size, shift):
    return [
        (d, (d // group_size) * group_size + (d % group_size + shift) % group_size)
        for d in range(expert_count)
    ]


def group_gather(piece, member, expert_count, group_size):
    got = [piece]
    for shift in range(1, group_size):
        got.append(lax.ppermute(piece, "expert", group_perm(expert_count, group_size, shift)))
    stacked = jnp.stack(got)
    order = (member - jnp.arange(group_size, dtype=jnp.int32)) % group_size
    return jnp.take(stacked, order, axis=0)


def group_reduce_scatter(pieces, member, expert_count, group_size, axis):
    total = lax.dynamic_index_in_dim(pieces, member, axis, keepdims=False).astype(jnp.float32)
    for shift in range(1, group_size):
        target = (member + shift) % group_size
        part = lax.dynamic_index_in_dim(pieces, target, axis, keepdims=False)
        moved = lax.ppermute(part, "expert", group_perm(expert_count, group_size, shift))
        total = total + moved.astype(jnp.float32)
    return total


def butterfly_sum(value, axes):
    for axis in axes:
        size = lax.axis_size(axis)
        if size & (size - 1):
            value = lax.psum(value, axis)
            continue
        bit = 1
        while bit < size:
            value = value + lax.ppermute(value, axis, [(i, i ^ bit) for i in range(size)])
            bit *= 2
    return value


def shards(
    tokens,
    steering,
    norm_gain,
    route_ids,
    route_gates,
    gate_weight,
    up_weight,
    down_weight,
    out_grad,
):
    expert_count = lax.axis_size("expert")
    flight = EXP_FLIGHT
    group_size = expert_count // flight
    capacity = CAP
    feature_count = tokens.shape[1]
    piece = feature_count // group_size
    member = lax.axis_index("expert") % group_size
    residual, inverse, normed = normalize(tokens, steering, norm_gain)
    slot_table, filled, combine = slot_tables(route_ids, route_gates, flight, capacity)
    packed = jnp.stack(
        [dispatch_rows(normed, slot_table, filled), dispatch_rows(out_grad, slot_table, filled)],
        axis=1,
    )
    sending = (
        packed.reshape(flight, 2, capacity, group_size, piece)
        .transpose(0, 3, 1, 2, 4)
        .reshape(expert_count, 2, capacity, piece)
    )
    arrived = lax.all_to_all(sending, "expert", split_axis=0, concat_axis=0, tiled=True)
    whole = group_gather(arrived, member, expert_count, group_size)
    rows = whole.transpose(1, 2, 3, 0, 4).reshape(expert_count, 2, capacity, feature_count)
    local_rows = rows[:, 0].reshape(expert_count * capacity, feature_count)
    local_grads = rows[:, 1].reshape(expert_count * capacity, feature_count)
    forward, backward = expert_share(local_rows, local_grads, gate_weight, up_weight, down_weight)
    both = jnp.stack(
        [
            forward.reshape(expert_count, capacity, feature_count),
            backward.reshape(expert_count, capacity, feature_count),
        ],
        axis=1,
    ).reshape(expert_count, 2, capacity, group_size, piece)
    summed = group_reduce_scatter(both, member, expert_count, group_size, 3)
    came = lax.all_to_all(
        summed.astype(jnp.bfloat16), "expert", split_axis=0, concat_axis=0, tiled=True
    )
    sums = (
        came.reshape(flight, group_size, 2, capacity, piece)
        .transpose(0, 2, 3, 1, 4)
        .reshape(flight, 2, capacity * feature_count)
        .astype(jnp.float32)
    )
    out_sums = sums[:, 0].reshape(flight * capacity, feature_count)
    grad_sums = sums[:, 1].reshape(flight * capacity, feature_count)
    mixture = apply_combine(combine, out_sums)
    back_normed = apply_combine(combine, grad_sums)
    layer_out = (residual + mixture).astype(jnp.bfloat16)
    total_grad = norm_backward(residual, inverse, norm_gain, back_normed, out_grad)
    steer_grad = butterfly_sum(jnp.sum(total_grad, axis=0), ("expert", "dp"))
    return (layer_out, total_grad.astype(jnp.bfloat16), steer_grad)


def solution(mesh):
    in_specs = (
        P(("dp", "expert"), None),
        P(),
        P(),
        P(("dp", "expert"), None),
        P(("dp", "expert"), None),
        P(None, "expert"),
        P(None, "expert"),
        P("expert", None),
        P(("dp", "expert"), None),
    )
    out_specs = (P(("dp", "expert"), None), P(("dp", "expert"), None), P())
    return jax.shard_map(shards, mesh=mesh, in_specs=in_specs, out_specs=out_specs, check_vma=False)
```

```python
import jax
import jax.numpy as jnp
from jax import lax
from jax.sharding import PartitionSpec as P
from jax.experimental import pallas as pl
from jax.experimental.pallas import tpu as pltpu

EXP_FLIGHT = 4
CAP = 8


EPSILON = 1e-06
GATE_UNIT = 1.0 / 65536.0


def slot_tables(route_ids, route_gates, flight, capacity):
    count_rows = route_ids.shape[0]
    expert_range = jnp.arange(flight, dtype=jnp.int32)
    hit_mask = route_ids[:, :, None] == expert_range[None, None, :]
    member = jnp.any(hit_mask, axis=1)
    scaled = route_gates.astype(jnp.float32) * GATE_UNIT
    weights = jnp.sum(jnp.where(hit_mask, scaled[:, :, None], 0.0), axis=1)
    position = jnp.cumsum(member.astype(jnp.int32), axis=0) - 1
    slot_of = jnp.where(member, position, capacity)
    slot_range = jnp.arange(capacity, dtype=jnp.int32)
    matches = slot_of[:, :, None] == slot_range[None, None, :]
    row_range = jnp.arange(count_rows, dtype=jnp.int32)
    slot_table = jnp.sum(jnp.where(matches, row_range[:, None, None], 0), axis=0)
    filled = jnp.any(matches, axis=0)
    combine = jnp.where(matches, weights[:, :, None], 0.0).reshape(count_rows, flight * capacity)
    return (slot_table, filled, combine)


def dispatch_rows(values, slot_table, filled):
    picked = values[slot_table]
    return jnp.where(filled[:, :, None], picked, jnp.zeros((), values.dtype))


def normalize(tokens, steering, norm_gain):
    residual = tokens.astype(jnp.float32) + steering
    inverse = lax.rsqrt(jnp.mean(residual * residual, axis=-1, keepdims=True) + EPSILON)
    normed = (residual * inverse * norm_gain).astype(jnp.bfloat16)
    return (residual, inverse, normed)


def norm_backward(residual, inverse, norm_gain, back_normed, out_grad):
    scaled = back_normed * norm_gain
    inner_mean = jnp.mean(scaled * residual, axis=-1, keepdims=True)
    cubed = inverse * inverse * inverse
    return out_grad.astype(jnp.float32) + inverse * scaled - residual * cubed * inner_mean


def share_forward(token_rows, gate_cols, up_cols, down_rows):
    gate_pre = jnp.dot(token_rows, gate_cols, preferred_element_type=jnp.float32)
    up_pre = jnp.dot(token_rows, up_cols, preferred_element_type=jnp.float32)
    hidden = (jax.nn.silu(gate_pre) * up_pre).astype(jnp.bfloat16)
    forward = jnp.dot(hidden, down_rows, preferred_element_type=jnp.float32).astype(jnp.bfloat16)
    return (forward, gate_pre, up_pre)


def share_backward(grad_rows, gate_pre, up_pre, gate_cols, up_cols, down_rows):
    contract = (((1,), (1,)), ((), ()))
    back_hidden = lax.dot_general(
        grad_rows, down_rows, contract, preferred_element_type=jnp.float32
    )
    sigmoid = jax.nn.sigmoid(gate_pre)
    back_up = (back_hidden * gate_pre * sigmoid).astype(jnp.bfloat16)
    back_gate = (back_hidden * up_pre * sigmoid * (1.0 + gate_pre * (1.0 - sigmoid))).astype(
        jnp.bfloat16
    )
    backward = lax.dot_general(back_gate, gate_cols, contract, preferred_element_type=jnp.float32)
    backward = backward + lax.dot_general(
        back_up, up_cols, contract, preferred_element_type=jnp.float32
    )
    return backward.astype(jnp.bfloat16)


def _expert_kernel(x_ref, y_ref, g_ref, u_ref, d_ref, out_ref, back_ref, acc_o, acc_b):
    j = pl.program_id(1)
    @pl.when(j == 0)
    def _():
        acc_o[...] = jnp.zeros_like(acc_o)
        acc_b[...] = jnp.zeros_like(acc_b)
    x = x_ref[...]
    y = y_ref[...]
    gw = g_ref[...]
    uw = u_ref[...]
    dw = d_ref[...]
    nt = (((1,), (1,)), ((), ()))
    g = jnp.dot(x, gw, preferred_element_type=jnp.float32)
    u = jnp.dot(x, uw, preferred_element_type=jnp.float32)
    sig = jax.nn.sigmoid(g)
    hidden = (g * sig * u).astype(jnp.bfloat16)
    bh = lax.dot_general(y, dw, nt, preferred_element_type=jnp.float32)
    back_up = (bh * g * sig).astype(jnp.bfloat16)
    back_gate = (bh * u * sig * (1.0 + g * (1.0 - sig))).astype(jnp.bfloat16)
    acc_o[...] += jnp.dot(hidden, dw, preferred_element_type=jnp.float32)
    acc_b[...] += (lax.dot_general(back_gate, gw, nt, preferred_element_type=jnp.float32)
                   + lax.dot_general(back_up, uw, nt, preferred_element_type=jnp.float32))
    @pl.when(j == pl.num_programs(1) - 1)
    def _():
        out_ref[...] = acc_o[...].astype(out_ref.dtype)
        back_ref[...] = acc_b[...].astype(back_ref.dtype)

def expert_share(x, y, gw, uw, dw):
    rows, feat = x.shape
    hid = gw.shape[1]
    rb = min(rows, 128)
    hb = min(hid, 256)
    return pl.pallas_call(
        _expert_kernel,
        grid=(rows // rb, hid // hb),
        in_specs=[
            pl.BlockSpec((rb, feat), lambda i, j: (i, 0)),
            pl.BlockSpec((rb, feat), lambda i, j: (i, 0)),
            pl.BlockSpec((feat, hb), lambda i, j: (0, j)),
            pl.BlockSpec((feat, hb), lambda i, j: (0, j)),
            pl.BlockSpec((hb, feat), lambda i, j: (j, 0)),
        ],
        out_specs=[
            pl.BlockSpec((rb, feat), lambda i, j: (i, 0)),
            pl.BlockSpec((rb, feat), lambda i, j: (i, 0)),
        ],
        out_shape=[jax.ShapeDtypeStruct((rows, feat), jnp.bfloat16)] * 2,
        scratch_shapes=[pltpu.VMEM((rb, feat), jnp.float32)] * 2,
        compiler_params=pltpu.CompilerParams(
            dimension_semantics=("arbitrary", "arbitrary"), vmem_limit_bytes=56 * 1024 * 1024
        ),
    )(x, y, gw, uw, dw)


def apply_combine(combine, partial_sums):
    return jnp.dot(combine, partial_sums, precision=lax.Precision.HIGHEST)


def group_perm(expert_count, group_size, shift):
    return [
        (d, (d // group_size) * group_size + (d % group_size + shift) % group_size)
        for d in range(expert_count)
    ]


def group_gather(piece, member, expert_count, group_size):
    got = [piece]
    for shift in range(1, group_size):
        got.append(lax.ppermute(piece, "expert", group_perm(expert_count, group_size, shift)))
    stacked = jnp.stack(got)
    order = (member - jnp.arange(group_size, dtype=jnp.int32)) % group_size
    return jnp.take(stacked, order, axis=0)


def group_reduce_scatter(pieces, member, expert_count, group_size, axis):
    total = lax.dynamic_index_in_dim(pieces, member, axis, keepdims=False).astype(jnp.float32)
    for shift in range(1, group_size):
        target = (member + shift) % group_size
        part = lax.dynamic_index_in_dim(pieces, target, axis, keepdims=False)
        moved = lax.ppermute(part, "expert", group_perm(expert_count, group_size, shift))
        total = total + moved.astype(jnp.float32)
    return total


def butterfly_sum(value, axes):
    for axis in axes:
        size = lax.axis_size(axis)
        if size & (size - 1):
            value = lax.psum(value, axis)
            continue
        bit = 1
        while bit < size:
            value = value + lax.ppermute(value, axis, [(i, i ^ bit) for i in range(size)])
            bit *= 2
    return value


def by_features(
    normed, out_grad, slot_table, filled, gate_weight, up_weight, down_weight,
    member, expert_count, group_size,
):
    flight, capacity = slot_table.shape
    feature_count = normed.shape[1]
    piece = feature_count // group_size
    packed = jnp.stack(
        [dispatch_rows(normed, slot_table, filled), dispatch_rows(out_grad, slot_table, filled)],
        axis=1,
    )
    sending = (
        packed.reshape(flight, 2, capacity, group_size, piece)
        .transpose(0, 3, 1, 2, 4)
        .reshape(expert_count, 2, capacity, piece)
    )
    arrived = lax.all_to_all(sending, "expert", split_axis=0, concat_axis=0, tiled=True)
    whole = group_gather(arrived, member, expert_count, group_size)
    rows = whole.transpose(1, 2, 3, 0, 4).reshape(expert_count, 2, capacity, feature_count)
    local_rows = rows[:, 0].reshape(expert_count * capacity, feature_count)
    local_grads = rows[:, 1].reshape(expert_count * capacity, feature_count)
    forward, backward = expert_share(local_rows, local_grads, gate_weight, up_weight, down_weight)
    both = jnp.stack(
        [
            forward.reshape(expert_count, capacity, feature_count),
            backward.reshape(expert_count, capacity, feature_count),
        ],
        axis=1,
    ).reshape(expert_count, 2, capacity, group_size, piece)
    summed = group_reduce_scatter(both, member, expert_count, group_size, 3)
    came = lax.all_to_all(
        summed.astype(jnp.bfloat16), "expert", split_axis=0, concat_axis=0, tiled=True
    )
    sums = (
        came.reshape(flight, group_size, 2, capacity, piece)
        .transpose(0, 2, 3, 1, 4)
        .reshape(flight, 2, capacity * feature_count)
        .astype(jnp.float32)
    )
    out_sums = sums[:, 0].reshape(flight * capacity, feature_count)
    grad_sums = sums[:, 1].reshape(flight * capacity, feature_count)
    return out_sums, grad_sums


def by_slots(
    normed, out_grad, slot_table, filled, gate_weight, up_weight, down_weight,
    member, expert_count, group_size,
):
    flight, capacity = slot_table.shape
    feature_count = normed.shape[1]
    half = capacity // group_size
    sending = jnp.stack(
        [dispatch_rows(normed, slot_table, filled), dispatch_rows(out_grad, slot_table, filled)],
        axis=1,
    )
    sending = (
        sending.reshape(flight, 2, group_size, half, feature_count)
        .transpose(0, 2, 1, 3, 4)
        .reshape(expert_count, 2, half, feature_count)
    )
    arrived = lax.all_to_all(sending, "expert", split_axis=0, concat_axis=0, tiled=True)
    got = [arrived]
    for shift in range(1, group_size):
        got.append(lax.ppermute(arrived, "expert", group_perm(expert_count, group_size, shift)))
    rows = jnp.stack(got, axis=1)
    local_rows = rows[:, :, 0].reshape(expert_count * group_size * half, feature_count)
    local_grads = rows[:, :, 1].reshape(expert_count * group_size * half, feature_count)
    forward, backward = expert_share(local_rows, local_grads, gate_weight, up_weight, down_weight)
    both = jnp.stack(
        [
            forward.reshape(expert_count, group_size, half, feature_count),
            backward.reshape(expert_count, group_size, half, feature_count),
        ],
        axis=2,
    )
    total = both[:, 0].astype(jnp.float32)
    for shift in range(1, group_size):
        back_shift = (group_size - shift) % group_size
        moved = lax.ppermute(
            both[:, shift], "expert", group_perm(expert_count, group_size, back_shift)
        )
        total = total + moved.astype(jnp.float32)
    came = lax.all_to_all(
        total.astype(jnp.bfloat16), "expert", split_axis=0, concat_axis=0, tiled=True
    )
    sums = (
        came.reshape(flight, group_size, 2, half, feature_count)
        .transpose(0, 2, 1, 3, 4)
        .reshape(flight, 2, capacity * feature_count)
        .astype(jnp.float32)
    )
    out_sums = sums[:, 0].reshape(flight * capacity, feature_count)
    grad_sums = sums[:, 1].reshape(flight * capacity, feature_count)
    return out_sums, grad_sums


def shards(
    tokens,
    steering,
    norm_gain,
    route_ids,
    route_gates,
    gate_weight,
    up_weight,
    down_weight,
    out_grad,
):
    expert_count = lax.axis_size("expert")
    flight = EXP_FLIGHT
    group_size = expert_count // flight
    capacity = CAP
    feature_count = tokens.shape[1]
    piece = feature_count // group_size
    member = lax.axis_index("expert") % group_size
    residual, inverse, normed = normalize(tokens, steering, norm_gain)
    slot_table, filled, combine = slot_tables(route_ids, route_gates, flight, capacity)
    if capacity % group_size == 0:
        out_sums, grad_sums = by_slots(
            normed, out_grad, slot_table, filled, gate_weight, up_weight, down_weight,
            member, expert_count, group_size,
        )
    else:
        out_sums, grad_sums = by_features(
            normed, out_grad, slot_table, filled, gate_weight, up_weight, down_weight,
            member, expert_count, group_size,
        )
    mixture = apply_combine(combine, out_sums)
    back_normed = apply_combine(combine, grad_sums)
    layer_out = (residual + mixture).astype(jnp.bfloat16)
    total_grad = norm_backward(residual, inverse, norm_gain, back_normed, out_grad)
    steer_grad = butterfly_sum(jnp.sum(total_grad, axis=0), ("expert", "dp"))
    return (layer_out, total_grad.astype(jnp.bfloat16), steer_grad)


def solution(mesh):
    in_specs = (
        P(("dp", "expert"), None),
        P(),
        P(),
        P(("dp", "expert"), None),
        P(("dp", "expert"), None),
        P(None, "expert"),
        P(None, "expert"),
        P("expert", None),
        P(("dp", "expert"), None),
    )
    out_specs = (P(("dp", "expert"), None), P(("dp", "expert"), None), P())
    return jax.shard_map(shards, mesh=mesh, in_specs=in_specs, out_specs=out_specs, check_vma=False)
```

```python
import jax
import jax.numpy as jnp
from jax import lax
from jax.sharding import PartitionSpec as P
from jax.experimental import pallas as pl
from jax.experimental.pallas import tpu as pltpu

EXP_FLIGHT = 4
CAP = 8


EPSILON = 1e-06
GATE_UNIT = 1.0 / 65536.0


def slot_tables(route_ids, route_gates, flight, capacity):
    count_rows = route_ids.shape[0]
    expert_range = jnp.arange(flight, dtype=jnp.int32)
    hit_mask = route_ids[:, :, None] == expert_range[None, None, :]
    member = jnp.any(hit_mask, axis=1)
    scaled = route_gates.astype(jnp.float32) * GATE_UNIT
    weights = jnp.sum(jnp.where(hit_mask, scaled[:, :, None], 0.0), axis=1)
    position = jnp.cumsum(member.astype(jnp.int32), axis=0) - 1
    slot_of = jnp.where(member, position, capacity)
    slot_range = jnp.arange(capacity, dtype=jnp.int32)
    matches = slot_of[:, :, None] == slot_range[None, None, :]
    row_range = jnp.arange(count_rows, dtype=jnp.int32)
    slot_table = jnp.sum(jnp.where(matches, row_range[:, None, None], 0), axis=0)
    filled = jnp.any(matches, axis=0)
    combine = jnp.where(matches, weights[:, :, None], 0.0).reshape(count_rows, flight * capacity)
    return (slot_table, filled, combine)


def dispatch_rows(values, slot_table, filled):
    picked = values[slot_table]
    return jnp.where(filled[:, :, None], picked, jnp.zeros((), values.dtype))


def normalize(tokens, steering, norm_gain):
    residual = tokens.astype(jnp.float32) + steering
    inverse = lax.rsqrt(jnp.mean(residual * residual, axis=-1, keepdims=True) + EPSILON)
    normed = (residual * inverse * norm_gain).astype(jnp.bfloat16)
    return (residual, inverse, normed)


def norm_backward(residual, inverse, norm_gain, back_normed, out_grad):
    scaled = back_normed * norm_gain
    inner_mean = jnp.mean(scaled * residual, axis=-1, keepdims=True)
    cubed = inverse * inverse * inverse
    return out_grad.astype(jnp.float32) + inverse * scaled - residual * cubed * inner_mean


def share_forward(token_rows, gate_cols, up_cols, down_rows):
    gate_pre = jnp.dot(token_rows, gate_cols, preferred_element_type=jnp.float32)
    up_pre = jnp.dot(token_rows, up_cols, preferred_element_type=jnp.float32)
    hidden = (jax.nn.silu(gate_pre) * up_pre).astype(jnp.bfloat16)
    forward = jnp.dot(hidden, down_rows, preferred_element_type=jnp.float32).astype(jnp.bfloat16)
    return (forward, gate_pre, up_pre)


def share_backward(grad_rows, gate_pre, up_pre, gate_cols, up_cols, down_rows):
    contract = (((1,), (1,)), ((), ()))
    back_hidden = lax.dot_general(
        grad_rows, down_rows, contract, preferred_element_type=jnp.float32
    )
    sigmoid = jax.nn.sigmoid(gate_pre)
    back_up = (back_hidden * gate_pre * sigmoid).astype(jnp.bfloat16)
    back_gate = (back_hidden * up_pre * sigmoid * (1.0 + gate_pre * (1.0 - sigmoid))).astype(
        jnp.bfloat16
    )
    backward = lax.dot_general(back_gate, gate_cols, contract, preferred_element_type=jnp.float32)
    backward = backward + lax.dot_general(
        back_up, up_cols, contract, preferred_element_type=jnp.float32
    )
    return backward.astype(jnp.bfloat16)


def _expert_kernel(x_ref, y_ref, g_ref, u_ref, d_ref, out_ref, back_ref, acc_o, acc_b):
    j = pl.program_id(1)
    @pl.when(j == 0)
    def _():
        acc_o[...] = jnp.zeros_like(acc_o)
        acc_b[...] = jnp.zeros_like(acc_b)
    x = x_ref[...]
    y = y_ref[...]
    gw = g_ref[...]
    uw = u_ref[...]
    dw = d_ref[...]
    nt = (((1,), (1,)), ((), ()))
    g = jnp.dot(x, gw, preferred_element_type=jnp.float32)
    u = jnp.dot(x, uw, preferred_element_type=jnp.float32)
    sig = jax.nn.sigmoid(g)
    hidden = (g * sig * u).astype(jnp.bfloat16)
    bh = lax.dot_general(y, dw, nt, preferred_element_type=jnp.float32)
    back_up = (bh * g * sig).astype(jnp.bfloat16)
    back_gate = (bh * u * sig * (1.0 + g * (1.0 - sig))).astype(jnp.bfloat16)
    acc_o[...] += jnp.dot(hidden, dw, preferred_element_type=jnp.float32)
    acc_b[...] += (lax.dot_general(back_gate, gw, nt, preferred_element_type=jnp.float32)
                   + lax.dot_general(back_up, uw, nt, preferred_element_type=jnp.float32))
    @pl.when(j == pl.num_programs(1) - 1)
    def _():
        out_ref[...] = acc_o[...].astype(out_ref.dtype)
        back_ref[...] = acc_b[...].astype(back_ref.dtype)

def expert_share(x, y, gw, uw, dw):
    rows, feat = x.shape
    hid = gw.shape[1]
    rb = min(rows, 128)
    hb = min(hid, 256)
    return pl.pallas_call(
        _expert_kernel,
        grid=(rows // rb, hid // hb),
        in_specs=[
            pl.BlockSpec((rb, feat), lambda i, j: (i, 0)),
            pl.BlockSpec((rb, feat), lambda i, j: (i, 0)),
            pl.BlockSpec((feat, hb), lambda i, j: (0, j)),
            pl.BlockSpec((feat, hb), lambda i, j: (0, j)),
            pl.BlockSpec((hb, feat), lambda i, j: (j, 0)),
        ],
        out_specs=[
            pl.BlockSpec((rb, feat), lambda i, j: (i, 0)),
            pl.BlockSpec((rb, feat), lambda i, j: (i, 0)),
        ],
        out_shape=[jax.ShapeDtypeStruct((rows, feat), jnp.bfloat16)] * 2,
        scratch_shapes=[pltpu.VMEM((rb, feat), jnp.float32)] * 2,
        compiler_params=pltpu.CompilerParams(
            dimension_semantics=("arbitrary", "arbitrary"), vmem_limit_bytes=56 * 1024 * 1024
        ),
    )(x, y, gw, uw, dw)


def apply_combine(combine, partial_sums):
    return jnp.dot(combine, partial_sums, precision=lax.Precision.HIGHEST)


def group_perm(expert_count, group_size, shift):
    return [
        (d, (d // group_size) * group_size + (d % group_size + shift) % group_size)
        for d in range(expert_count)
    ]


def group_gather(piece, member, expert_count, group_size):
    got = [piece]
    for shift in range(1, group_size):
        got.append(lax.ppermute(piece, "expert", group_perm(expert_count, group_size, shift)))
    stacked = jnp.stack(got)
    order = (member - jnp.arange(group_size, dtype=jnp.int32)) % group_size
    return jnp.take(stacked, order, axis=0)


def group_reduce_scatter(pieces, member, expert_count, group_size, axis):
    total = lax.dynamic_index_in_dim(pieces, member, axis, keepdims=False).astype(jnp.float32)
    for shift in range(1, group_size):
        target = (member + shift) % group_size
        part = lax.dynamic_index_in_dim(pieces, target, axis, keepdims=False)
        moved = lax.ppermute(part, "expert", group_perm(expert_count, group_size, shift))
        total = total + moved.astype(jnp.float32)
    return total


def butterfly_sum(value, axes):
    for axis in axes:
        size = lax.axis_size(axis)
        if size & (size - 1):
            value = lax.psum(value, axis)
            continue
        bit = 1
        while bit < size:
            value = value + lax.ppermute(value, axis, [(i, i ^ bit) for i in range(size)])
            bit *= 2
    return value


def by_features(
    normed, out_grad, slot_table, filled, gate_weight, up_weight, down_weight,
    member, expert_count, group_size,
):
    flight, capacity = slot_table.shape
    feature_count = normed.shape[1]
    piece = feature_count // group_size
    packed = jnp.stack(
        [dispatch_rows(normed, slot_table, filled), dispatch_rows(out_grad, slot_table, filled)],
        axis=1,
    )
    sending = (
        packed.reshape(flight, 2, capacity, group_size, piece)
        .transpose(0, 3, 1, 2, 4)
        .reshape(expert_count, 2, capacity, piece)
    )
    arrived = lax.all_to_all(sending, "expert", split_axis=0, concat_axis=0, tiled=True)
    whole = group_gather(arrived, member, expert_count, group_size)
    rows = whole.transpose(1, 2, 3, 0, 4).reshape(expert_count, 2, capacity, feature_count)
    local_rows = rows[:, 0].reshape(expert_count * capacity, feature_count)
    local_grads = rows[:, 1].reshape(expert_count * capacity, feature_count)
    forward, backward = expert_share(local_rows, local_grads, gate_weight, up_weight, down_weight)
    both = jnp.stack(
        [
            forward.reshape(expert_count, capacity, feature_count),
            backward.reshape(expert_count, capacity, feature_count),
        ],
        axis=1,
    ).reshape(expert_count, 2, capacity, group_size, piece)
    summed = group_reduce_scatter(both, member, expert_count, group_size, 3)
    came = lax.all_to_all(
        summed.astype(jnp.bfloat16), "expert", split_axis=0, concat_axis=0, tiled=True
    )
    sums = (
        came.reshape(flight, group_size, 2, capacity, piece)
        .transpose(0, 2, 3, 1, 4)
        .reshape(flight, 2, capacity * feature_count)
        .astype(jnp.float32)
    )
    out_sums = sums[:, 0].reshape(flight * capacity, feature_count)
    grad_sums = sums[:, 1].reshape(flight * capacity, feature_count)
    return out_sums, grad_sums


def by_pair(
    normed, out_grad, slot_table, filled, gate_weight, up_weight, down_weight,
    member, expert_count, group_size,
):
    flight, capacity = slot_table.shape
    feature_count = normed.shape[1]
    sending = jnp.stack(
        [dispatch_rows(normed, slot_table, filled), dispatch_rows(out_grad, slot_table, filled)],
        axis=1,
    ).reshape(expert_count, capacity, feature_count)
    arrived = lax.all_to_all(sending, "expert", split_axis=0, concat_axis=0, tiled=True)
    swap = group_perm(expert_count, group_size, 1)
    partner = lax.ppermute(arrived, "expert", swap)
    first = member == 0
    local_rows = jnp.where(first, arrived, partner).reshape(expert_count * capacity, feature_count)
    local_grads = jnp.where(first, partner, arrived).reshape(expert_count * capacity, feature_count)
    forward, backward = expert_share(local_rows, local_grads, gate_weight, up_weight, down_weight)
    keep = jnp.where(first, forward, backward)
    give = jnp.where(first, backward, forward)
    total = keep.astype(jnp.float32) + lax.ppermute(give, "expert", swap).astype(jnp.float32)
    came = lax.all_to_all(
        total.astype(jnp.bfloat16).reshape(expert_count, capacity, feature_count),
        "expert", split_axis=0, concat_axis=0, tiled=True,
    ).reshape(flight, 2, capacity, feature_count)
    out_sums = came[:, 0].reshape(flight * capacity, feature_count).astype(jnp.float32)
    grad_sums = came[:, 1].reshape(flight * capacity, feature_count).astype(jnp.float32)
    return out_sums, grad_sums


def shards(
    tokens,
    steering,
    norm_gain,
    route_ids,
    route_gates,
    gate_weight,
    up_weight,
    down_weight,
    out_grad,
):
    expert_count = lax.axis_size("expert")
    flight = EXP_FLIGHT
    group_size = expert_count // flight
    capacity = CAP
    feature_count = tokens.shape[1]
    piece = feature_count // group_size
    member = lax.axis_index("expert") % group_size
    residual, inverse, normed = normalize(tokens, steering, norm_gain)
    slot_table, filled, combine = slot_tables(route_ids, route_gates, flight, capacity)
    if group_size == 2:
        out_sums, grad_sums = by_pair(
            normed, out_grad, slot_table, filled, gate_weight, up_weight, down_weight,
            member, expert_count, group_size,
        )
    else:
        out_sums, grad_sums = by_features(
            normed, out_grad, slot_table, filled, gate_weight, up_weight, down_weight,
            member, expert_count, group_size,
        )
    mixture = apply_combine(combine, out_sums)
    back_normed = apply_combine(combine, grad_sums)
    layer_out = (residual + mixture).astype(jnp.bfloat16)
    total_grad = norm_backward(residual, inverse, norm_gain, back_normed, out_grad)
    steer_grad = butterfly_sum(jnp.sum(total_grad, axis=0), ("expert", "dp"))
    return (layer_out, total_grad.astype(jnp.bfloat16), steer_grad)


def solution(mesh):
    in_specs = (
        P(("dp", "expert"), None),
        P(),
        P(),
        P(("dp", "expert"), None),
        P(("dp", "expert"), None),
        P(None, "expert"),
        P(None, "expert"),
        P("expert", None),
        P(("dp", "expert"), None),
    )
    out_specs = (P(("dp", "expert"), None), P(("dp", "expert"), None), P())
    return jax.shard_map(shards, mesh=mesh, in_specs=in_specs, out_specs=out_specs, check_vma=False)
```

```python
import jax
import jax.numpy as jnp
from jax import lax
from jax.sharding import PartitionSpec as P
from jax.experimental import pallas as pl
from jax.experimental.pallas import tpu as pltpu

EXP_FLIGHT = 4
CAP = 8


EPSILON = 1e-06
GATE_UNIT = 1.0 / 65536.0


def slot_tables(route_ids, route_gates, flight, capacity):
    count_rows = route_ids.shape[0]
    expert_range = jnp.arange(flight, dtype=jnp.int32)
    hit_mask = route_ids[:, :, None] == expert_range[None, None, :]
    member = jnp.any(hit_mask, axis=1)
    scaled = route_gates.astype(jnp.float32) * GATE_UNIT
    weights = jnp.sum(jnp.where(hit_mask, scaled[:, :, None], 0.0), axis=1)
    position = jnp.cumsum(member.astype(jnp.int32), axis=0) - 1
    slot_of = jnp.where(member, position, capacity)
    slot_range = jnp.arange(capacity, dtype=jnp.int32)
    matches = slot_of[:, :, None] == slot_range[None, None, :]
    row_range = jnp.arange(count_rows, dtype=jnp.int32)
    slot_table = jnp.sum(jnp.where(matches, row_range[:, None, None], 0), axis=0)
    filled = jnp.any(matches, axis=0)
    combine = jnp.where(matches, weights[:, :, None], 0.0).reshape(count_rows, flight * capacity)
    return (slot_table, filled, combine)


def dispatch_rows(values, slot_table, filled):
    picked = values[slot_table]
    return jnp.where(filled[:, :, None], picked, jnp.zeros((), values.dtype))


def normalize(tokens, steering, norm_gain):
    residual = tokens.astype(jnp.float32) + steering
    inverse = lax.rsqrt(jnp.mean(residual * residual, axis=-1, keepdims=True) + EPSILON)
    normed = (residual * inverse * norm_gain).astype(jnp.bfloat16)
    return (residual, inverse, normed)


def norm_backward(residual, inverse, norm_gain, back_normed, out_grad):
    scaled = back_normed * norm_gain
    inner_mean = jnp.mean(scaled * residual, axis=-1, keepdims=True)
    cubed = inverse * inverse * inverse
    return out_grad.astype(jnp.float32) + inverse * scaled - residual * cubed * inner_mean


def share_forward(token_rows, gate_cols, up_cols, down_rows):
    gate_pre = jnp.dot(token_rows, gate_cols, preferred_element_type=jnp.float32)
    up_pre = jnp.dot(token_rows, up_cols, preferred_element_type=jnp.float32)
    hidden = (jax.nn.silu(gate_pre) * up_pre).astype(jnp.bfloat16)
    forward = jnp.dot(hidden, down_rows, preferred_element_type=jnp.float32).astype(jnp.bfloat16)
    return (forward, gate_pre, up_pre)


def share_backward(grad_rows, gate_pre, up_pre, gate_cols, up_cols, down_rows):
    contract = (((1,), (1,)), ((), ()))
    back_hidden = lax.dot_general(
        grad_rows, down_rows, contract, preferred_element_type=jnp.float32
    )
    sigmoid = jax.nn.sigmoid(gate_pre)
    back_up = (back_hidden * gate_pre * sigmoid).astype(jnp.bfloat16)
    back_gate = (back_hidden * up_pre * sigmoid * (1.0 + gate_pre * (1.0 - sigmoid))).astype(
        jnp.bfloat16
    )
    backward = lax.dot_general(back_gate, gate_cols, contract, preferred_element_type=jnp.float32)
    backward = backward + lax.dot_general(
        back_up, up_cols, contract, preferred_element_type=jnp.float32
    )
    return backward.astype(jnp.bfloat16)


def _expert_kernel(x_ref, y_ref, g_ref, u_ref, d_ref, out_ref, back_ref, acc_o, acc_b):
    j = pl.program_id(1)
    @pl.when(j == 0)
    def _():
        acc_o[...] = jnp.zeros_like(acc_o)
        acc_b[...] = jnp.zeros_like(acc_b)
    x = x_ref[...]
    y = y_ref[...]
    gw = g_ref[...]
    uw = u_ref[...]
    dw = d_ref[...]
    nt = (((1,), (1,)), ((), ()))
    g = jnp.dot(x, gw, preferred_element_type=jnp.float32)
    u = jnp.dot(x, uw, preferred_element_type=jnp.float32)
    sig = jax.nn.sigmoid(g)
    hidden = (g * sig * u).astype(jnp.bfloat16)
    bh = lax.dot_general(y, dw, nt, preferred_element_type=jnp.float32)
    back_up = (bh * g * sig).astype(jnp.bfloat16)
    back_gate = (bh * u * sig * (1.0 + g * (1.0 - sig))).astype(jnp.bfloat16)
    acc_o[...] += jnp.dot(hidden, dw, preferred_element_type=jnp.float32)
    acc_b[...] += (lax.dot_general(back_gate, gw, nt, preferred_element_type=jnp.float32)
                   + lax.dot_general(back_up, uw, nt, preferred_element_type=jnp.float32))
    @pl.when(j == pl.num_programs(1) - 1)
    def _():
        out_ref[...] = acc_o[...].astype(out_ref.dtype)
        back_ref[...] = acc_b[...].astype(back_ref.dtype)

def expert_share(x, y, gw, uw, dw):
    rows, feat = x.shape
    hid = gw.shape[1]
    rb = min(rows, 128)
    hb = min(hid, 256)
    return pl.pallas_call(
        _expert_kernel,
        grid=(rows // rb, hid // hb),
        in_specs=[
            pl.BlockSpec((rb, feat), lambda i, j: (i, 0)),
            pl.BlockSpec((rb, feat), lambda i, j: (i, 0)),
            pl.BlockSpec((feat, hb), lambda i, j: (0, j)),
            pl.BlockSpec((feat, hb), lambda i, j: (0, j)),
            pl.BlockSpec((hb, feat), lambda i, j: (j, 0)),
        ],
        out_specs=[
            pl.BlockSpec((rb, feat), lambda i, j: (i, 0)),
            pl.BlockSpec((rb, feat), lambda i, j: (i, 0)),
        ],
        out_shape=[jax.ShapeDtypeStruct((rows, feat), jnp.bfloat16)] * 2,
        scratch_shapes=[pltpu.VMEM((rb, feat), jnp.float32)] * 2,
        compiler_params=pltpu.CompilerParams(
            dimension_semantics=("arbitrary", "arbitrary"), vmem_limit_bytes=56 * 1024 * 1024
        ),
    )(x, y, gw, uw, dw)


def apply_combine(combine, partial_sums):
    return jnp.dot(combine, partial_sums, precision=lax.Precision.HIGHEST)


def group_perm(expert_count, group_size, shift):
    return [
        (d, (d // group_size) * group_size + (d % group_size + shift) % group_size)
        for d in range(expert_count)
    ]


def group_gather(piece, member, expert_count, group_size):
    got = [piece]
    for shift in range(1, group_size):
        got.append(lax.ppermute(piece, "expert", group_perm(expert_count, group_size, shift)))
    stacked = jnp.stack(got)
    order = (member - jnp.arange(group_size, dtype=jnp.int32)) % group_size
    return jnp.take(stacked, order, axis=0)


def group_reduce_scatter(pieces, member, expert_count, group_size, axis):
    total = lax.dynamic_index_in_dim(pieces, member, axis, keepdims=False).astype(jnp.float32)
    for shift in range(1, group_size):
        target = (member + shift) % group_size
        part = lax.dynamic_index_in_dim(pieces, target, axis, keepdims=False)
        moved = lax.ppermute(part, "expert", group_perm(expert_count, group_size, shift))
        total = total + moved.astype(jnp.float32)
    return total


def butterfly_sum(value, axes):
    for axis in axes:
        size = lax.axis_size(axis)
        if size & (size - 1):
            value = lax.psum(value, axis)
            continue
        bit = 1
        while bit < size:
            value = value + lax.ppermute(value, axis, [(i, i ^ bit) for i in range(size)])
            bit *= 2
    return value


def by_features(
    normed, out_grad, slot_table, filled, gate_weight, up_weight, down_weight,
    member, expert_count, group_size,
):
    flight, capacity = slot_table.shape
    feature_count = normed.shape[1]
    piece = feature_count // group_size
    packed = jnp.stack(
        [dispatch_rows(normed, slot_table, filled), dispatch_rows(out_grad, slot_table, filled)],
        axis=1,
    )
    sending = (
        packed.reshape(flight, 2, capacity, group_size, piece)
        .transpose(0, 3, 1, 2, 4)
        .reshape(expert_count, 2, capacity, piece)
    )
    arrived = lax.all_to_all(sending, "expert", split_axis=0, concat_axis=0, tiled=True)
    whole = group_gather(arrived, member, expert_count, group_size)
    rows = whole.transpose(1, 2, 3, 0, 4).reshape(expert_count, 2, capacity, feature_count)
    local_rows = rows[:, 0].reshape(expert_count * capacity, feature_count)
    local_grads = rows[:, 1].reshape(expert_count * capacity, feature_count)
    forward, backward = expert_share(local_rows, local_grads, gate_weight, up_weight, down_weight)
    both = jnp.stack(
        [
            forward.reshape(expert_count, capacity, feature_count),
            backward.reshape(expert_count, capacity, feature_count),
        ],
        axis=1,
    ).reshape(expert_count, 2, capacity, group_size, piece)
    summed = group_reduce_scatter(both, member, expert_count, group_size, 3)
    came = lax.all_to_all(
        summed.astype(jnp.bfloat16), "expert", split_axis=0, concat_axis=0, tiled=True
    )
    sums = (
        came.reshape(flight, group_size, 2, capacity, piece)
        .transpose(0, 2, 3, 1, 4)
        .reshape(flight, 2, capacity * feature_count)
        .astype(jnp.float32)
    )
    out_sums = sums[:, 0].reshape(flight * capacity, feature_count)
    grad_sums = sums[:, 1].reshape(flight * capacity, feature_count)
    return out_sums, grad_sums


def exchange(chunks, axis):
    size = lax.axis_size(axis)
    me = lax.axis_index(axis)
    moved = [lax.dynamic_index_in_dim(chunks, me, 0, keepdims=False)]
    for shift in range(1, size):
        part = lax.dynamic_index_in_dim(chunks, (me + shift) % size, 0, keepdims=False)
        moved.append(lax.ppermute(part, axis, [(i, (i + shift) % size) for i in range(size)]))
    stacked = jnp.stack(moved)
    order = (me - jnp.arange(size, dtype=jnp.int32)) % size
    return jnp.take(stacked, order, axis=0)


def pick_rows(values, slot_table, filled):
    token_range = jnp.arange(values.shape[0], dtype=jnp.int32)
    onehot = (slot_table[:, :, None] == token_range[None, None, :]) & filled[:, :, None]
    picked = jnp.einsum(
        "fct,td->fcd", onehot.astype(values.dtype), values, preferred_element_type=jnp.float32
    )
    return picked.astype(values.dtype)


def by_pair(
    normed, out_grad, slot_table, filled, gate_weight, up_weight, down_weight,
    member, expert_count, group_size,
):
    flight, capacity = slot_table.shape
    feature_count = normed.shape[1]
    sending = jnp.stack(
        [pick_rows(normed, slot_table, filled), pick_rows(out_grad, slot_table, filled)],
        axis=1,
    ).reshape(expert_count, capacity, feature_count)
    arrived = exchange(sending, "expert")
    swap = group_perm(expert_count, group_size, 1)
    partner = lax.ppermute(arrived, "expert", swap)
    first = member == 0
    local_rows = jnp.where(first, arrived, partner).reshape(expert_count * capacity, feature_count)
    local_grads = jnp.where(first, partner, arrived).reshape(expert_count * capacity, feature_count)
    forward, backward = expert_share(local_rows, local_grads, gate_weight, up_weight, down_weight)
    keep = jnp.where(first, forward, backward)
    give = jnp.where(first, backward, forward)
    total = keep.astype(jnp.float32) + lax.ppermute(give, "expert", swap).astype(jnp.float32)
    came = exchange(
        total.astype(jnp.bfloat16).reshape(expert_count, capacity, feature_count), "expert"
    ).reshape(flight, 2, capacity, feature_count)
    out_sums = came[:, 0].reshape(flight * capacity, feature_count).astype(jnp.float32)
    grad_sums = came[:, 1].reshape(flight * capacity, feature_count).astype(jnp.float32)
    return out_sums, grad_sums


def shards(
    tokens,
    steering,
    norm_gain,
    route_ids,
    route_gates,
    gate_weight,
    up_weight,
    down_weight,
    out_grad,
):
    expert_count = lax.axis_size("expert")
    flight = EXP_FLIGHT
    group_size = expert_count // flight
    capacity = CAP
    feature_count = tokens.shape[1]
    piece = feature_count // group_size
    member = lax.axis_index("expert") % group_size
    residual, inverse, normed = normalize(tokens, steering, norm_gain)
    slot_table, filled, combine = slot_tables(route_ids, route_gates, flight, capacity)
    if group_size == 2:
        out_sums, grad_sums = by_pair(
            normed, out_grad, slot_table, filled, gate_weight, up_weight, down_weight,
            member, expert_count, group_size,
        )
    else:
        out_sums, grad_sums = by_features(
            normed, out_grad, slot_table, filled, gate_weight, up_weight, down_weight,
            member, expert_count, group_size,
        )
    mixture = apply_combine(combine, out_sums)
    back_normed = apply_combine(combine, grad_sums)
    layer_out = (residual + mixture).astype(jnp.bfloat16)
    total_grad = norm_backward(residual, inverse, norm_gain, back_normed, out_grad)
    steer_grad = butterfly_sum(jnp.sum(total_grad, axis=0), ("expert", "dp"))
    return (layer_out, total_grad.astype(jnp.bfloat16), steer_grad)


def solution(mesh):
    in_specs = (
        P(("dp", "expert"), None),
        P(),
        P(),
        P(("dp", "expert"), None),
        P(("dp", "expert"), None),
        P(None, "expert"),
        P(None, "expert"),
        P("expert", None),
        P(("dp", "expert"), None),
    )
    out_specs = (P(("dp", "expert"), None), P(("dp", "expert"), None), P())
    return jax.shard_map(shards, mesh=mesh, in_specs=in_specs, out_specs=out_specs, check_vma=False)
```

```python
import jax
import jax.numpy as jnp
from jax import lax
from jax.sharding import PartitionSpec as P
from jax.experimental import pallas as pl
from jax.experimental.pallas import tpu as pltpu

EXP_FLIGHT = 4
CAP = 8


EPSILON = 1e-06
GATE_UNIT = 1.0 / 65536.0


def slot_tables(route_ids, route_gates, flight, capacity):
    count_rows = route_ids.shape[0]
    expert_range = jnp.arange(flight, dtype=jnp.int32)
    hit_mask = route_ids[:, :, None] == expert_range[None, None, :]
    member = jnp.any(hit_mask, axis=1)
    scaled = route_gates.astype(jnp.float32) * GATE_UNIT
    weights = jnp.sum(jnp.where(hit_mask, scaled[:, :, None], 0.0), axis=1)
    position = jnp.cumsum(member.astype(jnp.int32), axis=0) - 1
    slot_of = jnp.where(member, position, capacity)
    slot_range = jnp.arange(capacity, dtype=jnp.int32)
    matches = slot_of[:, :, None] == slot_range[None, None, :]
    row_range = jnp.arange(count_rows, dtype=jnp.int32)
    slot_table = jnp.sum(jnp.where(matches, row_range[:, None, None], 0), axis=0)
    filled = jnp.any(matches, axis=0)
    combine = jnp.where(matches, weights[:, :, None], 0.0).reshape(count_rows, flight * capacity)
    return (slot_table, filled, combine)


def dispatch_rows(values, slot_table, filled):
    picked = values[slot_table]
    return jnp.where(filled[:, :, None], picked, jnp.zeros((), values.dtype))


def normalize(tokens, steering, norm_gain):
    residual = tokens.astype(jnp.float32) + steering
    inverse = lax.rsqrt(jnp.mean(residual * residual, axis=-1, keepdims=True) + EPSILON)
    normed = (residual * inverse * norm_gain).astype(jnp.bfloat16)
    return (residual, inverse, normed)


def norm_backward(residual, inverse, norm_gain, back_normed, out_grad):
    scaled = back_normed * norm_gain
    inner_mean = jnp.mean(scaled * residual, axis=-1, keepdims=True)
    cubed = inverse * inverse * inverse
    return out_grad.astype(jnp.float32) + inverse * scaled - residual * cubed * inner_mean


def share_forward(token_rows, gate_cols, up_cols, down_rows):
    gate_pre = jnp.dot(token_rows, gate_cols, preferred_element_type=jnp.float32)
    up_pre = jnp.dot(token_rows, up_cols, preferred_element_type=jnp.float32)
    hidden = (jax.nn.silu(gate_pre) * up_pre).astype(jnp.bfloat16)
    forward = jnp.dot(hidden, down_rows, preferred_element_type=jnp.float32).astype(jnp.bfloat16)
    return (forward, gate_pre, up_pre)


def share_backward(grad_rows, gate_pre, up_pre, gate_cols, up_cols, down_rows):
    contract = (((1,), (1,)), ((), ()))
    back_hidden = lax.dot_general(
        grad_rows, down_rows, contract, preferred_element_type=jnp.float32
    )
    sigmoid = jax.nn.sigmoid(gate_pre)
    back_up = (back_hidden * gate_pre * sigmoid).astype(jnp.bfloat16)
    back_gate = (back_hidden * up_pre * sigmoid * (1.0 + gate_pre * (1.0 - sigmoid))).astype(
        jnp.bfloat16
    )
    backward = lax.dot_general(back_gate, gate_cols, contract, preferred_element_type=jnp.float32)
    backward = backward + lax.dot_general(
        back_up, up_cols, contract, preferred_element_type=jnp.float32
    )
    return backward.astype(jnp.bfloat16)


def _expert_kernel(x_ref, y_ref, g_ref, u_ref, d_ref, out_ref, back_ref, acc_o, acc_b):
    j = pl.program_id(1)
    @pl.when(j == 0)
    def _():
        acc_o[...] = jnp.zeros_like(acc_o)
        acc_b[...] = jnp.zeros_like(acc_b)
    x = x_ref[...]
    y = y_ref[...]
    gw = g_ref[...]
    uw = u_ref[...]
    dw = d_ref[...]
    nt = (((1,), (1,)), ((), ()))
    g = jnp.dot(x, gw, preferred_element_type=jnp.float32)
    u = jnp.dot(x, uw, preferred_element_type=jnp.float32)
    sig = jax.nn.sigmoid(g)
    hidden = (g * sig * u).astype(jnp.bfloat16)
    bh = lax.dot_general(y, dw, nt, preferred_element_type=jnp.float32)
    back_up = (bh * g * sig).astype(jnp.bfloat16)
    back_gate = (bh * u * sig * (1.0 + g * (1.0 - sig))).astype(jnp.bfloat16)
    acc_o[...] += jnp.dot(hidden, dw, preferred_element_type=jnp.float32)
    acc_b[...] += (lax.dot_general(back_gate, gw, nt, preferred_element_type=jnp.float32)
                   + lax.dot_general(back_up, uw, nt, preferred_element_type=jnp.float32))
    @pl.when(j == pl.num_programs(1) - 1)
    def _():
        out_ref[...] = acc_o[...].astype(out_ref.dtype)
        back_ref[...] = acc_b[...].astype(back_ref.dtype)

def expert_share(x, y, gw, uw, dw):
    rows, feat = x.shape
    hid = gw.shape[1]
    rb = min(rows, 128)
    hb = min(hid, 256)
    return pl.pallas_call(
        _expert_kernel,
        grid=(rows // rb, hid // hb),
        in_specs=[
            pl.BlockSpec((rb, feat), lambda i, j: (i, 0)),
            pl.BlockSpec((rb, feat), lambda i, j: (i, 0)),
            pl.BlockSpec((feat, hb), lambda i, j: (0, j)),
            pl.BlockSpec((feat, hb), lambda i, j: (0, j)),
            pl.BlockSpec((hb, feat), lambda i, j: (j, 0)),
        ],
        out_specs=[
            pl.BlockSpec((rb, feat), lambda i, j: (i, 0)),
            pl.BlockSpec((rb, feat), lambda i, j: (i, 0)),
        ],
        out_shape=[jax.ShapeDtypeStruct((rows, feat), jnp.bfloat16)] * 2,
        scratch_shapes=[pltpu.VMEM((rb, feat), jnp.float32)] * 2,
        compiler_params=pltpu.CompilerParams(
            dimension_semantics=("arbitrary", "arbitrary"), vmem_limit_bytes=56 * 1024 * 1024
        ),
    )(x, y, gw, uw, dw)


def apply_combine(combine, partial_sums):
    return jnp.dot(combine, partial_sums, precision=lax.Precision.HIGHEST)


def group_perm(expert_count, group_size, shift):
    return [
        (d, (d // group_size) * group_size + (d % group_size + shift) % group_size)
        for d in range(expert_count)
    ]


def group_gather(piece, member, expert_count, group_size):
    got = [piece]
    for shift in range(1, group_size):
        got.append(lax.ppermute(piece, "expert", group_perm(expert_count, group_size, shift)))
    stacked = jnp.stack(got)
    order = (member - jnp.arange(group_size, dtype=jnp.int32)) % group_size
    return jnp.take(stacked, order, axis=0)


def group_reduce_scatter(pieces, member, expert_count, group_size, axis):
    total = lax.dynamic_index_in_dim(pieces, member, axis, keepdims=False).astype(jnp.float32)
    for shift in range(1, group_size):
        target = (member + shift) % group_size
        part = lax.dynamic_index_in_dim(pieces, target, axis, keepdims=False)
        moved = lax.ppermute(part, "expert", group_perm(expert_count, group_size, shift))
        total = total + moved.astype(jnp.float32)
    return total


def butterfly_sum(value, axes):
    for axis in axes:
        size = lax.axis_size(axis)
        if size & (size - 1):
            value = lax.psum(value, axis)
            continue
        bit = 1
        while bit < size:
            value = value + lax.ppermute(value, axis, [(i, i ^ bit) for i in range(size)])
            bit *= 2
    return value


def by_features(
    normed, out_grad, slot_table, filled, gate_weight, up_weight, down_weight,
    member, expert_count, group_size,
):
    flight, capacity = slot_table.shape
    feature_count = normed.shape[1]
    piece = feature_count // group_size
    packed = jnp.stack(
        [dispatch_rows(normed, slot_table, filled), dispatch_rows(out_grad, slot_table, filled)],
        axis=1,
    )
    sending = (
        packed.reshape(flight, 2, capacity, group_size, piece)
        .transpose(0, 3, 1, 2, 4)
        .reshape(expert_count, 2, capacity, piece)
    )
    arrived = lax.all_to_all(sending, "expert", split_axis=0, concat_axis=0, tiled=True)
    whole = group_gather(arrived, member, expert_count, group_size)
    rows = whole.transpose(1, 2, 3, 0, 4).reshape(expert_count, 2, capacity, feature_count)
    local_rows = rows[:, 0].reshape(expert_count * capacity, feature_count)
    local_grads = rows[:, 1].reshape(expert_count * capacity, feature_count)
    forward, backward = expert_share(local_rows, local_grads, gate_weight, up_weight, down_weight)
    both = jnp.stack(
        [
            forward.reshape(expert_count, capacity, feature_count),
            backward.reshape(expert_count, capacity, feature_count),
        ],
        axis=1,
    ).reshape(expert_count, 2, capacity, group_size, piece)
    summed = group_reduce_scatter(both, member, expert_count, group_size, 3)
    came = lax.all_to_all(
        summed.astype(jnp.bfloat16), "expert", split_axis=0, concat_axis=0, tiled=True
    )
    sums = (
        came.reshape(flight, group_size, 2, capacity, piece)
        .transpose(0, 2, 3, 1, 4)
        .reshape(flight, 2, capacity * feature_count)
        .astype(jnp.float32)
    )
    out_sums = sums[:, 0].reshape(flight * capacity, feature_count)
    grad_sums = sums[:, 1].reshape(flight * capacity, feature_count)
    return out_sums, grad_sums


def exchange(chunks, axis):
    size = lax.axis_size(axis)
    me = lax.axis_index(axis)
    moved = [lax.dynamic_index_in_dim(chunks, me, 0, keepdims=False)]
    for shift in range(1, size):
        part = lax.dynamic_index_in_dim(chunks, (me + shift) % size, 0, keepdims=False)
        moved.append(lax.ppermute(part, axis, [(i, (i + shift) % size) for i in range(size)]))
    stacked = jnp.stack(moved)
    order = (me - jnp.arange(size, dtype=jnp.int32)) % size
    return jnp.take(stacked, order, axis=0)


def pick_rows(values, slot_table, filled):
    token_range = jnp.arange(values.shape[0], dtype=jnp.int32)
    onehot = (slot_table[:, :, None] == token_range[None, None, :]) & filled[:, :, None]
    picked = jnp.einsum(
        "fct,td->fcd", onehot.astype(values.dtype), values, preferred_element_type=jnp.float32
    )
    return picked.astype(values.dtype)


def collect(chunks, kind, flight, group_size):
    size = lax.axis_size("expert")
    me = lax.axis_index("expert")
    own = jnp.where(me % group_size == kind, chunks[me % size], jnp.zeros_like(chunks[0]))
    moved = [own]
    for shift in range(1, size):
        part = lax.dynamic_index_in_dim(chunks, (me + shift) % size, 0, keepdims=False)
        pairs = [(i, (i + shift) % size) for i in range(size) if i % group_size == kind]
        moved.append(lax.ppermute(part, "expert", pairs))
    stacked = jnp.stack(moved)
    senders = jnp.arange(flight, dtype=jnp.int32) * group_size + kind
    order = (me - senders) % size
    picked = jnp.take(stacked, order, axis=0)
    return picked.reshape(flight * chunks.shape[1], chunks.shape[2])


def by_pair(
    normed, out_grad, slot_table, filled, gate_weight, up_weight, down_weight,
    member, expert_count, group_size,
):
    flight, capacity = slot_table.shape
    feature_count = normed.shape[1]
    sending = jnp.stack(
        [pick_rows(normed, slot_table, filled), pick_rows(out_grad, slot_table, filled)],
        axis=1,
    ).reshape(expert_count, capacity, feature_count)
    arrived = exchange(sending, "expert")
    swap = group_perm(expert_count, group_size, 1)
    partner = lax.ppermute(arrived, "expert", swap)
    first = member == 0
    local_rows = jnp.where(first, arrived, partner).reshape(expert_count * capacity, feature_count)
    local_grads = jnp.where(first, partner, arrived).reshape(expert_count * capacity, feature_count)
    forward, backward = expert_share(local_rows, local_grads, gate_weight, up_weight, down_weight)
    keep = jnp.where(first, forward, backward)
    give = jnp.where(first, backward, forward)
    total = keep.astype(jnp.float32) + lax.ppermute(give, "expert", swap).astype(jnp.float32)
    total = total.astype(jnp.bfloat16).reshape(expert_count, capacity, feature_count)
    grad_sums = collect(total, 1, flight, group_size).astype(jnp.float32)
    out_sums = collect(total, 0, flight, group_size).astype(jnp.float32)
    return out_sums, grad_sums


def shards(
    tokens,
    steering,
    norm_gain,
    route_ids,
    route_gates,
    gate_weight,
    up_weight,
    down_weight,
    out_grad,
):
    expert_count = lax.axis_size("expert")
    flight = EXP_FLIGHT
    group_size = expert_count // flight
    capacity = CAP
    feature_count = tokens.shape[1]
    piece = feature_count // group_size
    member = lax.axis_index("expert") % group_size
    residual, inverse, normed = normalize(tokens, steering, norm_gain)
    slot_table, filled, combine = slot_tables(route_ids, route_gates, flight, capacity)
    if group_size == 2:
        out_sums, grad_sums = by_pair(
            normed, out_grad, slot_table, filled, gate_weight, up_weight, down_weight,
            member, expert_count, group_size,
        )
    else:
        out_sums, grad_sums = by_features(
            normed, out_grad, slot_table, filled, gate_weight, up_weight, down_weight,
            member, expert_count, group_size,
        )
    mixture = apply_combine(combine, out_sums)
    back_normed = apply_combine(combine, grad_sums)
    layer_out = (residual + mixture).astype(jnp.bfloat16)
    total_grad = norm_backward(residual, inverse, norm_gain, back_normed, out_grad)
    steer_grad = butterfly_sum(jnp.sum(total_grad, axis=0), ("expert", "dp"))
    return (layer_out, total_grad.astype(jnp.bfloat16), steer_grad)


def solution(mesh):
    in_specs = (
        P(("dp", "expert"), None),
        P(),
        P(),
        P(("dp", "expert"), None),
        P(("dp", "expert"), None),
        P(None, "expert"),
        P(None, "expert"),
        P("expert", None),
        P(("dp", "expert"), None),
    )
    out_specs = (P(("dp", "expert"), None), P(("dp", "expert"), None), P())
    return jax.shard_map(shards, mesh=mesh, in_specs=in_specs, out_specs=out_specs, check_vma=False)
```

```python
import jax
import jax.numpy as jnp
from jax import lax
from jax.sharding import PartitionSpec as P
from jax.experimental import pallas as pl
from jax.experimental.pallas import tpu as pltpu

EXP_FLIGHT = 4
CAP = 8


EPSILON = 1e-06
GATE_UNIT = 1.0 / 65536.0


def slot_tables(route_ids, route_gates, flight, capacity):
    count_rows = route_ids.shape[0]
    expert_range = jnp.arange(flight, dtype=jnp.int32)
    hit_mask = route_ids[:, :, None] == expert_range[None, None, :]
    member = jnp.any(hit_mask, axis=1)
    scaled = route_gates.astype(jnp.float32) * GATE_UNIT
    weights = jnp.sum(jnp.where(hit_mask, scaled[:, :, None], 0.0), axis=1)
    position = jnp.cumsum(member.astype(jnp.int32), axis=0) - 1
    slot_of = jnp.where(member, position, capacity)
    slot_range = jnp.arange(capacity, dtype=jnp.int32)
    matches = slot_of[:, :, None] == slot_range[None, None, :]
    row_range = jnp.arange(count_rows, dtype=jnp.int32)
    slot_table = jnp.sum(jnp.where(matches, row_range[:, None, None], 0), axis=0)
    filled = jnp.any(matches, axis=0)
    combine = jnp.where(matches, weights[:, :, None], 0.0).reshape(count_rows, flight * capacity)
    return (slot_table, filled, combine)


def dispatch_rows(values, slot_table, filled):
    picked = values[slot_table]
    return jnp.where(filled[:, :, None], picked, jnp.zeros((), values.dtype))


def normalize(tokens, steering, norm_gain):
    residual = tokens.astype(jnp.float32) + steering
    inverse = lax.rsqrt(jnp.mean(residual * residual, axis=-1, keepdims=True) + EPSILON)
    normed = (residual * inverse * norm_gain).astype(jnp.bfloat16)
    return (residual, inverse, normed)


def norm_backward(residual, inverse, norm_gain, back_normed, out_grad):
    scaled = back_normed * norm_gain
    inner_mean = jnp.mean(scaled * residual, axis=-1, keepdims=True)
    cubed = inverse * inverse * inverse
    return out_grad.astype(jnp.float32) + inverse * scaled - residual * cubed * inner_mean


def share_forward(token_rows, gate_cols, up_cols, down_rows):
    gate_pre = jnp.dot(token_rows, gate_cols, preferred_element_type=jnp.float32)
    up_pre = jnp.dot(token_rows, up_cols, preferred_element_type=jnp.float32)
    hidden = (jax.nn.silu(gate_pre) * up_pre).astype(jnp.bfloat16)
    forward = jnp.dot(hidden, down_rows, preferred_element_type=jnp.float32).astype(jnp.bfloat16)
    return (forward, gate_pre, up_pre)


def share_backward(grad_rows, gate_pre, up_pre, gate_cols, up_cols, down_rows):
    contract = (((1,), (1,)), ((), ()))
    back_hidden = lax.dot_general(
        grad_rows, down_rows, contract, preferred_element_type=jnp.float32
    )
    sigmoid = jax.nn.sigmoid(gate_pre)
    back_up = (back_hidden * gate_pre * sigmoid).astype(jnp.bfloat16)
    back_gate = (back_hidden * up_pre * sigmoid * (1.0 + gate_pre * (1.0 - sigmoid))).astype(
        jnp.bfloat16
    )
    backward = lax.dot_general(back_gate, gate_cols, contract, preferred_element_type=jnp.float32)
    backward = backward + lax.dot_general(
        back_up, up_cols, contract, preferred_element_type=jnp.float32
    )
    return backward.astype(jnp.bfloat16)


def _expert_kernel(x_ref, y_ref, g_ref, u_ref, d_ref, out_ref, back_ref, acc_o, acc_b):
    j = pl.program_id(1)
    @pl.when(j == 0)
    def _():
        acc_o[...] = jnp.zeros_like(acc_o)
        acc_b[...] = jnp.zeros_like(acc_b)
    x = x_ref[...]
    y = y_ref[...]
    gw = g_ref[...]
    uw = u_ref[...]
    dw = d_ref[...]
    nt = (((1,), (1,)), ((), ()))
    g = jnp.dot(x, gw, preferred_element_type=jnp.float32)
    u = jnp.dot(x, uw, preferred_element_type=jnp.float32)
    sig = jax.nn.sigmoid(g)
    hidden = (g * sig * u).astype(jnp.bfloat16)
    bh = lax.dot_general(y, dw, nt, preferred_element_type=jnp.float32)
    back_up = (bh * g * sig).astype(jnp.bfloat16)
    back_gate = (bh * u * sig * (1.0 + g * (1.0 - sig))).astype(jnp.bfloat16)
    acc_o[...] += jnp.dot(hidden, dw, preferred_element_type=jnp.float32)
    acc_b[...] += (lax.dot_general(back_gate, gw, nt, preferred_element_type=jnp.float32)
                   + lax.dot_general(back_up, uw, nt, preferred_element_type=jnp.float32))
    @pl.when(j == pl.num_programs(1) - 1)
    def _():
        out_ref[...] = acc_o[...].astype(out_ref.dtype)
        back_ref[...] = acc_b[...].astype(back_ref.dtype)

def expert_share(x, y, gw, uw, dw):
    rows, feat = x.shape
    hid = gw.shape[1]
    rb = min(rows, 128)
    hb = min(hid, 256)
    return pl.pallas_call(
        _expert_kernel,
        grid=(rows // rb, hid // hb),
        in_specs=[
            pl.BlockSpec((rb, feat), lambda i, j: (i, 0)),
            pl.BlockSpec((rb, feat), lambda i, j: (i, 0)),
            pl.BlockSpec((feat, hb), lambda i, j: (0, j)),
            pl.BlockSpec((feat, hb), lambda i, j: (0, j)),
            pl.BlockSpec((hb, feat), lambda i, j: (j, 0)),
        ],
        out_specs=[
            pl.BlockSpec((rb, feat), lambda i, j: (i, 0)),
            pl.BlockSpec((rb, feat), lambda i, j: (i, 0)),
        ],
        out_shape=[jax.ShapeDtypeStruct((rows, feat), jnp.bfloat16)] * 2,
        scratch_shapes=[pltpu.VMEM((rb, feat), jnp.float32)] * 2,
        compiler_params=pltpu.CompilerParams(
            dimension_semantics=("arbitrary", "arbitrary"), vmem_limit_bytes=56 * 1024 * 1024
        ),
    )(x, y, gw, uw, dw)


def _pair_kernel(
    first_ref, a_ref, p_ref, g_ref, u_ref, d_ref, keep_ref, give_ref, xs, ys, acc_o, acc_b
):
    j = pl.program_id(0)
    first = first_ref[0] == 1

    @pl.when(j == 0)
    def _():
        xs[...] = jnp.where(first, a_ref[...], p_ref[...])
        ys[...] = jnp.where(first, p_ref[...], a_ref[...])
        acc_o[...] = jnp.zeros_like(acc_o)
        acc_b[...] = jnp.zeros_like(acc_b)

    x = xs[...]
    y = ys[...]
    gw = g_ref[...]
    uw = u_ref[...]
    dw = d_ref[...]
    nt = (((1,), (1,)), ((), ()))
    g = jnp.dot(x, gw, preferred_element_type=jnp.float32)
    u = jnp.dot(x, uw, preferred_element_type=jnp.float32)
    sig = jax.nn.sigmoid(g)
    hidden = (g * sig * u).astype(jnp.bfloat16)
    bh = lax.dot_general(y, dw, nt, preferred_element_type=jnp.float32)
    back_up = (bh * g * sig).astype(jnp.bfloat16)
    back_gate = (bh * u * sig * (1.0 + g * (1.0 - sig))).astype(jnp.bfloat16)
    acc_o[...] += jnp.dot(hidden, dw, preferred_element_type=jnp.float32)
    acc_b[...] += lax.dot_general(
        back_gate, gw, nt, preferred_element_type=jnp.float32
    ) + lax.dot_general(back_up, uw, nt, preferred_element_type=jnp.float32)

    @pl.when(j == pl.num_programs(0) - 1)
    def _():
        out = acc_o[...].astype(keep_ref.dtype)
        back = acc_b[...].astype(keep_ref.dtype)
        keep_ref[...] = jnp.where(first, out, back)
        give_ref[...] = jnp.where(first, back, out)


def expert_pair(first, arrived, partner, gw, uw, dw):
    rows, feat = arrived.shape
    hid = gw.shape[1]
    hb = min(hid, 256)
    full = pl.BlockSpec((rows, feat), lambda j, f: (0, 0))
    grid_spec = pltpu.PrefetchScalarGridSpec(
        num_scalar_prefetch=1,
        grid=(hid // hb,),
        in_specs=[
            full,
            full,
            pl.BlockSpec((feat, hb), lambda j, f: (0, j)),
            pl.BlockSpec((feat, hb), lambda j, f: (0, j)),
            pl.BlockSpec((hb, feat), lambda j, f: (j, 0)),
        ],
        out_specs=[full, full],
        scratch_shapes=[pltpu.VMEM((rows, feat), arrived.dtype)] * 2
        + [pltpu.VMEM((rows, feat), jnp.float32)] * 2,
    )
    return pl.pallas_call(
        _pair_kernel,
        grid_spec=grid_spec,
        out_shape=[jax.ShapeDtypeStruct((rows, feat), jnp.bfloat16)] * 2,
        compiler_params=pltpu.CompilerParams(
            dimension_semantics=("arbitrary",), vmem_limit_bytes=56 * 1024 * 1024
        ),
    )(first, arrived, partner, gw, uw, dw)


def apply_combine(combine, partial_sums):
    return jnp.dot(combine, partial_sums, precision=lax.Precision.HIGHEST)


def group_perm(expert_count, group_size, shift):
    return [
        (d, (d // group_size) * group_size + (d % group_size + shift) % group_size)
        for d in range(expert_count)
    ]


def group_gather(piece, member, expert_count, group_size):
    got = [piece]
    for shift in range(1, group_size):
        got.append(lax.ppermute(piece, "expert", group_perm(expert_count, group_size, shift)))
    stacked = jnp.stack(got)
    order = (member - jnp.arange(group_size, dtype=jnp.int32)) % group_size
    return jnp.take(stacked, order, axis=0)


def group_reduce_scatter(pieces, member, expert_count, group_size, axis):
    total = lax.dynamic_index_in_dim(pieces, member, axis, keepdims=False).astype(jnp.float32)
    for shift in range(1, group_size):
        target = (member + shift) % group_size
        part = lax.dynamic_index_in_dim(pieces, target, axis, keepdims=False)
        moved = lax.ppermute(part, "expert", group_perm(expert_count, group_size, shift))
        total = total + moved.astype(jnp.float32)
    return total


def butterfly_sum(value, axes):
    for axis in axes:
        size = lax.axis_size(axis)
        if size & (size - 1):
            value = lax.psum(value, axis)
            continue
        bit = 1
        while bit < size:
            value = value + lax.ppermute(value, axis, [(i, i ^ bit) for i in range(size)])
            bit *= 2
    return value


def by_features(
    normed, out_grad, slot_table, filled, gate_weight, up_weight, down_weight,
    member, expert_count, group_size,
):
    flight, capacity = slot_table.shape
    feature_count = normed.shape[1]
    piece = feature_count // group_size
    packed = jnp.stack(
        [dispatch_rows(normed, slot_table, filled), dispatch_rows(out_grad, slot_table, filled)],
        axis=1,
    )
    sending = (
        packed.reshape(flight, 2, capacity, group_size, piece)
        .transpose(0, 3, 1, 2, 4)
        .reshape(expert_count, 2, capacity, piece)
    )
    arrived = lax.all_to_all(sending, "expert", split_axis=0, concat_axis=0, tiled=True)
    whole = group_gather(arrived, member, expert_count, group_size)
    rows = whole.transpose(1, 2, 3, 0, 4).reshape(expert_count, 2, capacity, feature_count)
    local_rows = rows[:, 0].reshape(expert_count * capacity, feature_count)
    local_grads = rows[:, 1].reshape(expert_count * capacity, feature_count)
    forward, backward = expert_share(local_rows, local_grads, gate_weight, up_weight, down_weight)
    both = jnp.stack(
        [
            forward.reshape(expert_count, capacity, feature_count),
            backward.reshape(expert_count, capacity, feature_count),
        ],
        axis=1,
    ).reshape(expert_count, 2, capacity, group_size, piece)
    summed = group_reduce_scatter(both, member, expert_count, group_size, 3)
    came = lax.all_to_all(
        summed.astype(jnp.bfloat16), "expert", split_axis=0, concat_axis=0, tiled=True
    )
    sums = (
        came.reshape(flight, group_size, 2, capacity, piece)
        .transpose(0, 2, 3, 1, 4)
        .reshape(flight, 2, capacity * feature_count)
        .astype(jnp.float32)
    )
    out_sums = sums[:, 0].reshape(flight * capacity, feature_count)
    grad_sums = sums[:, 1].reshape(flight * capacity, feature_count)
    return out_sums, grad_sums


def exchange(chunks, axis):
    size = lax.axis_size(axis)
    me = lax.axis_index(axis)
    moved = [lax.dynamic_index_in_dim(chunks, me, 0, keepdims=False)]
    for shift in range(1, size):
        part = lax.dynamic_index_in_dim(chunks, (me + shift) % size, 0, keepdims=False)
        moved.append(lax.ppermute(part, axis, [(i, (i + shift) % size) for i in range(size)]))
    stacked = jnp.stack(moved)
    order = (me - jnp.arange(size, dtype=jnp.int32)) % size
    return jnp.take(stacked, order, axis=0)


def pick_rows(values, slot_table, filled):
    token_range = jnp.arange(values.shape[0], dtype=jnp.int32)
    onehot = (slot_table[:, :, None] == token_range[None, None, :]) & filled[:, :, None]
    picked = jnp.einsum(
        "fct,td->fcd", onehot.astype(values.dtype), values, preferred_element_type=jnp.float32
    )
    return picked.astype(values.dtype)


def by_pair(
    normed, out_grad, slot_table, filled, gate_weight, up_weight, down_weight,
    member, expert_count, group_size,
):
    flight, capacity = slot_table.shape
    feature_count = normed.shape[1]
    sending = jnp.stack(
        [pick_rows(normed, slot_table, filled), pick_rows(out_grad, slot_table, filled)],
        axis=1,
    ).reshape(expert_count, capacity, feature_count)
    arrived = exchange(sending, "expert")
    swap = group_perm(expert_count, group_size, 1)
    partner = lax.ppermute(arrived, "expert", swap)
    first = (member == 0).astype(jnp.int32).reshape(1)
    keep, give = expert_pair(
        first,
        arrived.reshape(expert_count * capacity, feature_count),
        partner.reshape(expert_count * capacity, feature_count),
        gate_weight,
        up_weight,
        down_weight,
    )
    total = keep.astype(jnp.float32) + lax.ppermute(give, "expert", swap).astype(jnp.float32)
    came = exchange(
        total.astype(jnp.bfloat16).reshape(expert_count, capacity, feature_count), "expert"
    ).reshape(flight, 2, capacity, feature_count)
    out_sums = came[:, 0].reshape(flight * capacity, feature_count).astype(jnp.float32)
    grad_sums = came[:, 1].reshape(flight * capacity, feature_count).astype(jnp.float32)
    return out_sums, grad_sums


def shards(
    tokens,
    steering,
    norm_gain,
    route_ids,
    route_gates,
    gate_weight,
    up_weight,
    down_weight,
    out_grad,
):
    expert_count = lax.axis_size("expert")
    flight = EXP_FLIGHT
    group_size = expert_count // flight
    capacity = CAP
    feature_count = tokens.shape[1]
    piece = feature_count // group_size
    member = lax.axis_index("expert") % group_size
    residual, inverse, normed = normalize(tokens, steering, norm_gain)
    slot_table, filled, combine = slot_tables(route_ids, route_gates, flight, capacity)
    if group_size == 2:
        out_sums, grad_sums = by_pair(
            normed, out_grad, slot_table, filled, gate_weight, up_weight, down_weight,
            member, expert_count, group_size,
        )
    else:
        out_sums, grad_sums = by_features(
            normed, out_grad, slot_table, filled, gate_weight, up_weight, down_weight,
            member, expert_count, group_size,
        )
    mixture = apply_combine(combine, out_sums)
    back_normed = apply_combine(combine, grad_sums)
    layer_out = (residual + mixture).astype(jnp.bfloat16)
    total_grad = norm_backward(residual, inverse, norm_gain, back_normed, out_grad)
    steer_grad = butterfly_sum(jnp.sum(total_grad, axis=0), ("expert", "dp"))
    return (layer_out, total_grad.astype(jnp.bfloat16), steer_grad)


def solution(mesh):
    in_specs = (
        P(("dp", "expert"), None),
        P(),
        P(),
        P(("dp", "expert"), None),
        P(("dp", "expert"), None),
        P(None, "expert"),
        P(None, "expert"),
        P("expert", None),
        P(("dp", "expert"), None),
    )
    out_specs = (P(("dp", "expert"), None), P(("dp", "expert"), None), P())
    return jax.shard_map(shards, mesh=mesh, in_specs=in_specs, out_specs=out_specs, check_vma=False)
```

```python
import jax
import jax.numpy as jnp
from jax import lax
from jax.sharding import PartitionSpec as P
from jax.experimental import pallas as pl
from jax.experimental.pallas import tpu as pltpu

EXP_FLIGHT = 4
CAP = 8


EPSILON = 1e-06
GATE_UNIT = 1.0 / 65536.0


def slot_tables(route_ids, route_gates, flight, capacity):
    count_rows = route_ids.shape[0]
    expert_range = jnp.arange(flight, dtype=jnp.int32)
    hit_mask = route_ids[:, :, None] == expert_range[None, None, :]
    member = jnp.any(hit_mask, axis=1)
    scaled = route_gates.astype(jnp.float32) * GATE_UNIT
    weights = jnp.sum(jnp.where(hit_mask, scaled[:, :, None], 0.0), axis=1)
    position = jnp.cumsum(member.astype(jnp.int32), axis=0) - 1
    slot_of = jnp.where(member, position, capacity)
    slot_range = jnp.arange(capacity, dtype=jnp.int32)
    matches = slot_of[:, :, None] == slot_range[None, None, :]
    row_range = jnp.arange(count_rows, dtype=jnp.int32)
    slot_table = jnp.sum(jnp.where(matches, row_range[:, None, None], 0), axis=0)
    filled = jnp.any(matches, axis=0)
    combine = jnp.where(matches, weights[:, :, None], 0.0).reshape(count_rows, flight * capacity)
    return (slot_table, filled, combine)


def dispatch_rows(values, slot_table, filled):
    picked = values[slot_table]
    return jnp.where(filled[:, :, None], picked, jnp.zeros((), values.dtype))


def normalize(tokens, steering, norm_gain):
    residual = tokens.astype(jnp.float32) + steering
    inverse = lax.rsqrt(jnp.mean(residual * residual, axis=-1, keepdims=True) + EPSILON)
    normed = (residual * inverse * norm_gain).astype(jnp.bfloat16)
    return (residual, inverse, normed)


def norm_backward(residual, inverse, norm_gain, back_normed, out_grad):
    scaled = back_normed * norm_gain
    inner_mean = jnp.mean(scaled * residual, axis=-1, keepdims=True)
    cubed = inverse * inverse * inverse
    return out_grad.astype(jnp.float32) + inverse * scaled - residual * cubed * inner_mean


def share_forward(token_rows, gate_cols, up_cols, down_rows):
    gate_pre = jnp.dot(token_rows, gate_cols, preferred_element_type=jnp.float32)
    up_pre = jnp.dot(token_rows, up_cols, preferred_element_type=jnp.float32)
    hidden = (jax.nn.silu(gate_pre) * up_pre).astype(jnp.bfloat16)
    forward = jnp.dot(hidden, down_rows, preferred_element_type=jnp.float32).astype(jnp.bfloat16)
    return (forward, gate_pre, up_pre)


def share_backward(grad_rows, gate_pre, up_pre, gate_cols, up_cols, down_rows):
    contract = (((1,), (1,)), ((), ()))
    back_hidden = lax.dot_general(
        grad_rows, down_rows, contract, preferred_element_type=jnp.float32
    )
    sigmoid = jax.nn.sigmoid(gate_pre)
    back_up = (back_hidden * gate_pre * sigmoid).astype(jnp.bfloat16)
    back_gate = (back_hidden * up_pre * sigmoid * (1.0 + gate_pre * (1.0 - sigmoid))).astype(
        jnp.bfloat16
    )
    backward = lax.dot_general(back_gate, gate_cols, contract, preferred_element_type=jnp.float32)
    backward = backward + lax.dot_general(
        back_up, up_cols, contract, preferred_element_type=jnp.float32
    )
    return backward.astype(jnp.bfloat16)


def _expert_kernel(x_ref, y_ref, g_ref, u_ref, d_ref, out_ref, back_ref, acc_o, acc_b):
    j = pl.program_id(1)
    @pl.when(j == 0)
    def _():
        acc_o[...] = jnp.zeros_like(acc_o)
        acc_b[...] = jnp.zeros_like(acc_b)
    x = x_ref[...]
    y = y_ref[...]
    gw = g_ref[...]
    uw = u_ref[...]
    dw = d_ref[...]
    nt = (((1,), (1,)), ((), ()))
    g = jnp.dot(x, gw, preferred_element_type=jnp.float32)
    u = jnp.dot(x, uw, preferred_element_type=jnp.float32)
    sig = jax.nn.sigmoid(g)
    hidden = (g * sig * u).astype(jnp.bfloat16)
    bh = lax.dot_general(y, dw, nt, preferred_element_type=jnp.float32)
    back_up = (bh * g * sig).astype(jnp.bfloat16)
    back_gate = (bh * u * sig * (1.0 + g * (1.0 - sig))).astype(jnp.bfloat16)
    acc_o[...] += jnp.dot(hidden, dw, preferred_element_type=jnp.float32)
    acc_b[...] += (lax.dot_general(back_gate, gw, nt, preferred_element_type=jnp.float32)
                   + lax.dot_general(back_up, uw, nt, preferred_element_type=jnp.float32))
    @pl.when(j == pl.num_programs(1) - 1)
    def _():
        out_ref[...] = acc_o[...].astype(out_ref.dtype)
        back_ref[...] = acc_b[...].astype(back_ref.dtype)

def expert_share(x, y, gw, uw, dw):
    rows, feat = x.shape
    hid = gw.shape[1]
    rb = min(rows, 128)
    hb = min(hid, 256)
    return pl.pallas_call(
        _expert_kernel,
        grid=(rows // rb, hid // hb),
        in_specs=[
            pl.BlockSpec((rb, feat), lambda i, j: (i, 0)),
            pl.BlockSpec((rb, feat), lambda i, j: (i, 0)),
            pl.BlockSpec((feat, hb), lambda i, j: (0, j)),
            pl.BlockSpec((feat, hb), lambda i, j: (0, j)),
            pl.BlockSpec((hb, feat), lambda i, j: (j, 0)),
        ],
        out_specs=[
            pl.BlockSpec((rb, feat), lambda i, j: (i, 0)),
            pl.BlockSpec((rb, feat), lambda i, j: (i, 0)),
        ],
        out_shape=[jax.ShapeDtypeStruct((rows, feat), jnp.bfloat16)] * 2,
        scratch_shapes=[pltpu.VMEM((rb, feat), jnp.float32)] * 2,
        compiler_params=pltpu.CompilerParams(
            dimension_semantics=("arbitrary", "arbitrary"), vmem_limit_bytes=56 * 1024 * 1024
        ),
    )(x, y, gw, uw, dw)


def _pair_kernel(
    first_ref, a_ref, p_ref, g_ref, u_ref, d_ref, both_ref, xs, ys, acc_o, acc_b
):
    j = pl.program_id(0)
    first = first_ref[0] == 1

    @pl.when(j == 0)
    def _():
        xs[...] = jnp.where(first, a_ref[...], p_ref[...])
        ys[...] = jnp.where(first, p_ref[...], a_ref[...])
        acc_o[...] = jnp.zeros_like(acc_o)
        acc_b[...] = jnp.zeros_like(acc_b)

    x = xs[...]
    y = ys[...]
    gw = g_ref[...]
    uw = u_ref[...]
    dw = d_ref[...]
    nt = (((1,), (1,)), ((), ()))
    g = jnp.dot(x, gw, preferred_element_type=jnp.float32)
    u = jnp.dot(x, uw, preferred_element_type=jnp.float32)
    sig = jax.nn.sigmoid(g)
    hidden = (g * sig * u).astype(jnp.bfloat16)
    bh = lax.dot_general(y, dw, nt, preferred_element_type=jnp.float32)
    back_up = (bh * g * sig).astype(jnp.bfloat16)
    back_gate = (bh * u * sig * (1.0 + g * (1.0 - sig))).astype(jnp.bfloat16)
    acc_o[...] += jnp.dot(hidden, dw, preferred_element_type=jnp.float32)
    acc_b[...] += lax.dot_general(
        back_gate, gw, nt, preferred_element_type=jnp.float32
    ) + lax.dot_general(back_up, uw, nt, preferred_element_type=jnp.float32)

    @pl.when(j == pl.num_programs(0) - 1)
    def _():
        both_ref[0] = acc_o[...].astype(both_ref.dtype)
        both_ref[1] = acc_b[...].astype(both_ref.dtype)


def expert_pair(first, arrived, partner, gw, uw, dw):
    rows, feat = arrived.shape
    hid = gw.shape[1]
    hb = min(hid, 256)
    full = pl.BlockSpec((rows, feat), lambda j, f: (0, 0))
    grid_spec = pltpu.PrefetchScalarGridSpec(
        num_scalar_prefetch=1,
        grid=(hid // hb,),
        in_specs=[
            full,
            full,
            pl.BlockSpec((feat, hb), lambda j, f: (0, j)),
            pl.BlockSpec((feat, hb), lambda j, f: (0, j)),
            pl.BlockSpec((hb, feat), lambda j, f: (j, 0)),
        ],
        out_specs=pl.BlockSpec((2, rows, feat), lambda j, f: (0, 0, 0)),
        scratch_shapes=[pltpu.VMEM((rows, feat), arrived.dtype)] * 2
        + [pltpu.VMEM((rows, feat), jnp.float32)] * 2,
    )
    return pl.pallas_call(
        _pair_kernel,
        grid_spec=grid_spec,
        out_shape=jax.ShapeDtypeStruct((2, rows, feat), jnp.bfloat16),
        compiler_params=pltpu.CompilerParams(
            dimension_semantics=("arbitrary",), vmem_limit_bytes=56 * 1024 * 1024
        ),
    )(first, arrived, partner, gw, uw, dw)


def apply_combine(combine, partial_sums):
    return jnp.dot(combine, partial_sums, precision=lax.Precision.HIGHEST)


def group_perm(expert_count, group_size, shift):
    return [
        (d, (d // group_size) * group_size + (d % group_size + shift) % group_size)
        for d in range(expert_count)
    ]


def group_gather(piece, member, expert_count, group_size):
    got = [piece]
    for shift in range(1, group_size):
        got.append(lax.ppermute(piece, "expert", group_perm(expert_count, group_size, shift)))
    stacked = jnp.stack(got)
    order = (member - jnp.arange(group_size, dtype=jnp.int32)) % group_size
    return jnp.take(stacked, order, axis=0)


def group_reduce_scatter(pieces, member, expert_count, group_size, axis):
    total = lax.dynamic_index_in_dim(pieces, member, axis, keepdims=False).astype(jnp.float32)
    for shift in range(1, group_size):
        target = (member + shift) % group_size
        part = lax.dynamic_index_in_dim(pieces, target, axis, keepdims=False)
        moved = lax.ppermute(part, "expert", group_perm(expert_count, group_size, shift))
        total = total + moved.astype(jnp.float32)
    return total


def butterfly_sum(value, axes):
    for axis in axes:
        size = lax.axis_size(axis)
        if size & (size - 1):
            value = lax.psum(value, axis)
            continue
        bit = 1
        while bit < size:
            value = value + lax.ppermute(value, axis, [(i, i ^ bit) for i in range(size)])
            bit *= 2
    return value


def by_features(
    normed, out_grad, slot_table, filled, gate_weight, up_weight, down_weight,
    member, expert_count, group_size,
):
    flight, capacity = slot_table.shape
    feature_count = normed.shape[1]
    piece = feature_count // group_size
    packed = jnp.stack(
        [dispatch_rows(normed, slot_table, filled), dispatch_rows(out_grad, slot_table, filled)],
        axis=1,
    )
    sending = (
        packed.reshape(flight, 2, capacity, group_size, piece)
        .transpose(0, 3, 1, 2, 4)
        .reshape(expert_count, 2, capacity, piece)
    )
    arrived = lax.all_to_all(sending, "expert", split_axis=0, concat_axis=0, tiled=True)
    whole = group_gather(arrived, member, expert_count, group_size)
    rows = whole.transpose(1, 2, 3, 0, 4).reshape(expert_count, 2, capacity, feature_count)
    local_rows = rows[:, 0].reshape(expert_count * capacity, feature_count)
    local_grads = rows[:, 1].reshape(expert_count * capacity, feature_count)
    forward, backward = expert_share(local_rows, local_grads, gate_weight, up_weight, down_weight)
    both = jnp.stack(
        [
            forward.reshape(expert_count, capacity, feature_count),
            backward.reshape(expert_count, capacity, feature_count),
        ],
        axis=1,
    ).reshape(expert_count, 2, capacity, group_size, piece)
    summed = group_reduce_scatter(both, member, expert_count, group_size, 3)
    came = lax.all_to_all(
        summed.astype(jnp.bfloat16), "expert", split_axis=0, concat_axis=0, tiled=True
    )
    sums = (
        came.reshape(flight, group_size, 2, capacity, piece)
        .transpose(0, 2, 3, 1, 4)
        .reshape(flight, 2, capacity * feature_count)
        .astype(jnp.float32)
    )
    out_sums = sums[:, 0].reshape(flight * capacity, feature_count)
    grad_sums = sums[:, 1].reshape(flight * capacity, feature_count)
    return out_sums, grad_sums


def exchange(chunks, axis):
    size = lax.axis_size(axis)
    me = lax.axis_index(axis)
    moved = [lax.dynamic_index_in_dim(chunks, me, 0, keepdims=False)]
    for shift in range(1, size):
        part = lax.dynamic_index_in_dim(chunks, (me + shift) % size, 0, keepdims=False)
        moved.append(lax.ppermute(part, axis, [(i, (i + shift) % size) for i in range(size)]))
    stacked = jnp.stack(moved)
    order = (me - jnp.arange(size, dtype=jnp.int32)) % size
    return jnp.take(stacked, order, axis=0)


def pick_rows(values, slot_table, filled):
    token_range = jnp.arange(values.shape[0], dtype=jnp.int32)
    onehot = (slot_table[:, :, None] == token_range[None, None, :]) & filled[:, :, None]
    picked = jnp.einsum(
        "fct,td->fcd", onehot.astype(values.dtype), values, preferred_element_type=jnp.float32
    )
    return picked.astype(values.dtype)


def by_parity(chunks, odd, flight, group_size):
    size = lax.axis_size("expert")
    me = lax.axis_index("expert")
    moved = []
    for shift in range(odd, size, group_size):
        part = lax.dynamic_index_in_dim(chunks, (me + shift) % size, 0, keepdims=False)
        if shift == 0:
            moved.append(part)
        else:
            moved.append(lax.ppermute(part, "expert", [(i, (i + shift) % size) for i in range(size)]))
    stacked = jnp.stack(moved)
    chip = me // group_size
    order = (chip - jnp.arange(flight, dtype=jnp.int32) + odd * (me % group_size - 1)) % flight
    picked = jnp.take(stacked, order, axis=0)
    return picked.reshape(flight * chunks.shape[1], chunks.shape[2])


def by_pair(
    normed, out_grad, slot_table, filled, gate_weight, up_weight, down_weight,
    member, expert_count, group_size,
):
    flight, capacity = slot_table.shape
    feature_count = normed.shape[1]
    sending = jnp.stack(
        [pick_rows(normed, slot_table, filled), pick_rows(out_grad, slot_table, filled)],
        axis=1,
    ).reshape(expert_count, capacity, feature_count)
    arrived = exchange(sending, "expert")
    swap = group_perm(expert_count, group_size, 1)
    partner = lax.ppermute(arrived, "expert", swap)
    first = (member == 0).astype(jnp.int32).reshape(1)
    both = expert_pair(
        first,
        arrived.reshape(expert_count * capacity, feature_count),
        partner.reshape(expert_count * capacity, feature_count),
        gate_weight,
        up_weight,
        down_weight,
    )
    sums = both.astype(jnp.float32) + lax.ppermute(both, "expert", swap).astype(jnp.float32)
    sums = sums.astype(jnp.bfloat16).reshape(2, expert_count, capacity, feature_count)
    grad_sums = by_parity(sums[1], 0, flight, group_size).astype(jnp.float32)
    out_sums = by_parity(sums[0], 1, flight, group_size).astype(jnp.float32)
    return out_sums, grad_sums


def shards(
    tokens,
    steering,
    norm_gain,
    route_ids,
    route_gates,
    gate_weight,
    up_weight,
    down_weight,
    out_grad,
):
    expert_count = lax.axis_size("expert")
    flight = EXP_FLIGHT
    group_size = expert_count // flight
    capacity = CAP
    feature_count = tokens.shape[1]
    piece = feature_count // group_size
    member = lax.axis_index("expert") % group_size
    residual, inverse, normed = normalize(tokens, steering, norm_gain)
    slot_table, filled, combine = slot_tables(route_ids, route_gates, flight, capacity)
    if group_size == 2:
        out_sums, grad_sums = by_pair(
            normed, out_grad, slot_table, filled, gate_weight, up_weight, down_weight,
            member, expert_count, group_size,
        )
    else:
        out_sums, grad_sums = by_features(
            normed, out_grad, slot_table, filled, gate_weight, up_weight, down_weight,
            member, expert_count, group_size,
        )
    mixture = apply_combine(combine, out_sums)
    back_normed = apply_combine(combine, grad_sums)
    layer_out = (residual + mixture).astype(jnp.bfloat16)
    total_grad = norm_backward(residual, inverse, norm_gain, back_normed, out_grad)
    steer_grad = butterfly_sum(jnp.sum(total_grad, axis=0), ("expert", "dp"))
    return (layer_out, total_grad.astype(jnp.bfloat16), steer_grad)


def solution(mesh):
    in_specs = (
        P(("dp", "expert"), None),
        P(),
        P(),
        P(("dp", "expert"), None),
        P(("dp", "expert"), None),
        P(None, "expert"),
        P(None, "expert"),
        P("expert", None),
        P(("dp", "expert"), None),
    )
    out_specs = (P(("dp", "expert"), None), P(("dp", "expert"), None), P())
    return jax.shard_map(shards, mesh=mesh, in_specs=in_specs, out_specs=out_specs, check_vma=False)
```

```python
import jax
import jax.numpy as jnp
from jax import lax
from jax.sharding import PartitionSpec as P
from jax.experimental import pallas as pl
from jax.experimental.pallas import tpu as pltpu

EXP_FLIGHT = 4
CAP = 8


EPSILON = 1e-06
GATE_UNIT = 1.0 / 65536.0


def slot_tables(route_ids, route_gates, flight, capacity):
    count_rows = route_ids.shape[0]
    expert_range = jnp.arange(flight, dtype=jnp.int32)
    hit_mask = route_ids[:, :, None] == expert_range[None, None, :]
    member = jnp.any(hit_mask, axis=1)
    scaled = route_gates.astype(jnp.float32) * GATE_UNIT
    weights = jnp.sum(jnp.where(hit_mask, scaled[:, :, None], 0.0), axis=1)
    position = jnp.cumsum(member.astype(jnp.int32), axis=0) - 1
    slot_of = jnp.where(member, position, capacity)
    slot_range = jnp.arange(capacity, dtype=jnp.int32)
    matches = slot_of[:, :, None] == slot_range[None, None, :]
    row_range = jnp.arange(count_rows, dtype=jnp.int32)
    slot_table = jnp.sum(jnp.where(matches, row_range[:, None, None], 0), axis=0)
    filled = jnp.any(matches, axis=0)
    combine = jnp.where(matches, weights[:, :, None], 0.0).reshape(count_rows, flight * capacity)
    return (slot_table, filled, combine)


def dispatch_rows(values, slot_table, filled):
    picked = values[slot_table]
    return jnp.where(filled[:, :, None], picked, jnp.zeros((), values.dtype))


def normalize(tokens, steering, norm_gain):
    residual = tokens.astype(jnp.float32) + steering
    inverse = lax.rsqrt(jnp.mean(residual * residual, axis=-1, keepdims=True) + EPSILON)
    normed = (residual * inverse * norm_gain).astype(jnp.bfloat16)
    return (residual, inverse, normed)


def norm_backward(residual, inverse, norm_gain, back_normed, out_grad):
    scaled = back_normed * norm_gain
    inner_mean = jnp.mean(scaled * residual, axis=-1, keepdims=True)
    cubed = inverse * inverse * inverse
    return out_grad.astype(jnp.float32) + inverse * scaled - residual * cubed * inner_mean


def share_forward(token_rows, gate_cols, up_cols, down_rows):
    gate_pre = jnp.dot(token_rows, gate_cols, preferred_element_type=jnp.float32)
    up_pre = jnp.dot(token_rows, up_cols, preferred_element_type=jnp.float32)
    hidden = (jax.nn.silu(gate_pre) * up_pre).astype(jnp.bfloat16)
    forward = jnp.dot(hidden, down_rows, preferred_element_type=jnp.float32).astype(jnp.bfloat16)
    return (forward, gate_pre, up_pre)


def share_backward(grad_rows, gate_pre, up_pre, gate_cols, up_cols, down_rows):
    contract = (((1,), (1,)), ((), ()))
    back_hidden = lax.dot_general(
        grad_rows, down_rows, contract, preferred_element_type=jnp.float32
    )
    sigmoid = jax.nn.sigmoid(gate_pre)
    back_up = (back_hidden * gate_pre * sigmoid).astype(jnp.bfloat16)
    back_gate = (back_hidden * up_pre * sigmoid * (1.0 + gate_pre * (1.0 - sigmoid))).astype(
        jnp.bfloat16
    )
    backward = lax.dot_general(back_gate, gate_cols, contract, preferred_element_type=jnp.float32)
    backward = backward + lax.dot_general(
        back_up, up_cols, contract, preferred_element_type=jnp.float32
    )
    return backward.astype(jnp.bfloat16)


def _expert_kernel(x_ref, y_ref, g_ref, u_ref, d_ref, out_ref, back_ref, acc_o, acc_b):
    j = pl.program_id(1)
    @pl.when(j == 0)
    def _():
        acc_o[...] = jnp.zeros_like(acc_o)
        acc_b[...] = jnp.zeros_like(acc_b)
    x = x_ref[...]
    y = y_ref[...]
    gw = g_ref[...]
    uw = u_ref[...]
    dw = d_ref[...]
    nt = (((1,), (1,)), ((), ()))
    g = jnp.dot(x, gw, preferred_element_type=jnp.float32)
    u = jnp.dot(x, uw, preferred_element_type=jnp.float32)
    sig = jax.nn.sigmoid(g)
    hidden = (g * sig * u).astype(jnp.bfloat16)
    bh = lax.dot_general(y, dw, nt, preferred_element_type=jnp.float32)
    back_up = (bh * g * sig).astype(jnp.bfloat16)
    back_gate = (bh * u * sig * (1.0 + g * (1.0 - sig))).astype(jnp.bfloat16)
    acc_o[...] += jnp.dot(hidden, dw, preferred_element_type=jnp.float32)
    acc_b[...] += (lax.dot_general(back_gate, gw, nt, preferred_element_type=jnp.float32)
                   + lax.dot_general(back_up, uw, nt, preferred_element_type=jnp.float32))
    @pl.when(j == pl.num_programs(1) - 1)
    def _():
        out_ref[...] = acc_o[...].astype(out_ref.dtype)
        back_ref[...] = acc_b[...].astype(back_ref.dtype)

def expert_share(x, y, gw, uw, dw):
    rows, feat = x.shape
    hid = gw.shape[1]
    rb = min(rows, 128)
    hb = min(hid, 256)
    return pl.pallas_call(
        _expert_kernel,
        grid=(rows // rb, hid // hb),
        in_specs=[
            pl.BlockSpec((rb, feat), lambda i, j: (i, 0)),
            pl.BlockSpec((rb, feat), lambda i, j: (i, 0)),
            pl.BlockSpec((feat, hb), lambda i, j: (0, j)),
            pl.BlockSpec((feat, hb), lambda i, j: (0, j)),
            pl.BlockSpec((hb, feat), lambda i, j: (j, 0)),
        ],
        out_specs=[
            pl.BlockSpec((rb, feat), lambda i, j: (i, 0)),
            pl.BlockSpec((rb, feat), lambda i, j: (i, 0)),
        ],
        out_shape=[jax.ShapeDtypeStruct((rows, feat), jnp.bfloat16)] * 2,
        scratch_shapes=[pltpu.VMEM((rb, feat), jnp.float32)] * 2,
        compiler_params=pltpu.CompilerParams(
            dimension_semantics=("arbitrary", "arbitrary"), vmem_limit_bytes=56 * 1024 * 1024
        ),
    )(x, y, gw, uw, dw)


def _pair_kernel(
    first_ref, a_ref, p_ref, g_ref, u_ref, d_ref, both_ref, xs, ys, acc_o, acc_b
):
    j = pl.program_id(0)
    first = first_ref[0] == 1

    @pl.when(j == 0)
    def _():
        xs[...] = jnp.where(first, a_ref[...], p_ref[...])
        ys[...] = jnp.where(first, p_ref[...], a_ref[...])
        acc_o[...] = jnp.zeros_like(acc_o)
        acc_b[...] = jnp.zeros_like(acc_b)

    x = xs[...]
    y = ys[...]
    gw = g_ref[...]
    uw = u_ref[...]
    dw = d_ref[...]
    nt = (((1,), (1,)), ((), ()))
    g = jnp.dot(x, gw, preferred_element_type=jnp.float32)
    u = jnp.dot(x, uw, preferred_element_type=jnp.float32)
    sig = jax.nn.sigmoid(g)
    hidden = (g * sig * u).astype(jnp.bfloat16)
    bh = lax.dot_general(y, dw, nt, preferred_element_type=jnp.float32)
    back_up = (bh * g * sig).astype(jnp.bfloat16)
    back_gate = (bh * u * sig * (1.0 + g * (1.0 - sig))).astype(jnp.bfloat16)
    acc_o[...] += jnp.dot(hidden, dw, preferred_element_type=jnp.float32)
    acc_b[...] += lax.dot_general(
        back_gate, gw, nt, preferred_element_type=jnp.float32
    ) + lax.dot_general(back_up, uw, nt, preferred_element_type=jnp.float32)

    @pl.when(j == pl.num_programs(0) - 1)
    def _():
        both_ref[0] = acc_o[...].astype(both_ref.dtype)
        both_ref[1] = acc_b[...].astype(both_ref.dtype)


def expert_pair(first, arrived, partner, gw, uw, dw):
    rows, feat = arrived.shape
    hid = gw.shape[1]
    hb = min(hid, 256)
    full = pl.BlockSpec((rows, feat), lambda j, f: (0, 0))
    grid_spec = pltpu.PrefetchScalarGridSpec(
        num_scalar_prefetch=1,
        grid=(hid // hb,),
        in_specs=[
            full,
            full,
            pl.BlockSpec((feat, hb), lambda j, f: (0, j)),
            pl.BlockSpec((feat, hb), lambda j, f: (0, j)),
            pl.BlockSpec((hb, feat), lambda j, f: (j, 0)),
        ],
        out_specs=pl.BlockSpec((2, rows, feat), lambda j, f: (0, 0, 0)),
        scratch_shapes=[pltpu.VMEM((rows, feat), arrived.dtype)] * 2
        + [pltpu.VMEM((rows, feat), jnp.float32)] * 2,
    )
    return pl.pallas_call(
        _pair_kernel,
        grid_spec=grid_spec,
        out_shape=jax.ShapeDtypeStruct((2, rows, feat), jnp.bfloat16),
        compiler_params=pltpu.CompilerParams(
            dimension_semantics=("arbitrary",), vmem_limit_bytes=56 * 1024 * 1024
        ),
    )(first, arrived, partner, gw, uw, dw)


def apply_combine(combine, partial_sums):
    return jnp.dot(combine, partial_sums, precision=lax.Precision.HIGHEST)


def group_perm(expert_count, group_size, shift):
    return [
        (d, (d // group_size) * group_size + (d % group_size + shift) % group_size)
        for d in range(expert_count)
    ]


def group_gather(piece, member, expert_count, group_size):
    got = [piece]
    for shift in range(1, group_size):
        got.append(lax.ppermute(piece, "expert", group_perm(expert_count, group_size, shift)))
    stacked = jnp.stack(got)
    order = (member - jnp.arange(group_size, dtype=jnp.int32)) % group_size
    return jnp.take(stacked, order, axis=0)


def group_reduce_scatter(pieces, member, expert_count, group_size, axis):
    total = lax.dynamic_index_in_dim(pieces, member, axis, keepdims=False).astype(jnp.float32)
    for shift in range(1, group_size):
        target = (member + shift) % group_size
        part = lax.dynamic_index_in_dim(pieces, target, axis, keepdims=False)
        moved = lax.ppermute(part, "expert", group_perm(expert_count, group_size, shift))
        total = total + moved.astype(jnp.float32)
    return total


def butterfly_sum(value, axes):
    for axis in axes:
        size = lax.axis_size(axis)
        if size & (size - 1):
            value = lax.psum(value, axis)
            continue
        bit = 1
        while bit < size:
            value = value + lax.ppermute(value, axis, [(i, i ^ bit) for i in range(size)])
            bit *= 2
    return value


def by_features(
    normed, out_grad, slot_table, filled, gate_weight, up_weight, down_weight,
    member, expert_count, group_size,
):
    flight, capacity = slot_table.shape
    feature_count = normed.shape[1]
    piece = feature_count // group_size
    packed = jnp.stack(
        [dispatch_rows(normed, slot_table, filled), dispatch_rows(out_grad, slot_table, filled)],
        axis=1,
    )
    sending = (
        packed.reshape(flight, 2, capacity, group_size, piece)
        .transpose(0, 3, 1, 2, 4)
        .reshape(expert_count, 2, capacity, piece)
    )
    arrived = lax.all_to_all(sending, "expert", split_axis=0, concat_axis=0, tiled=True)
    whole = group_gather(arrived, member, expert_count, group_size)
    rows = whole.transpose(1, 2, 3, 0, 4).reshape(expert_count, 2, capacity, feature_count)
    local_rows = rows[:, 0].reshape(expert_count * capacity, feature_count)
    local_grads = rows[:, 1].reshape(expert_count * capacity, feature_count)
    forward, backward = expert_share(local_rows, local_grads, gate_weight, up_weight, down_weight)
    both = jnp.stack(
        [
            forward.reshape(expert_count, capacity, feature_count),
            backward.reshape(expert_count, capacity, feature_count),
        ],
        axis=1,
    ).reshape(expert_count, 2, capacity, group_size, piece)
    summed = group_reduce_scatter(both, member, expert_count, group_size, 3)
    came = lax.all_to_all(
        summed.astype(jnp.bfloat16), "expert", split_axis=0, concat_axis=0, tiled=True
    )
    sums = (
        came.reshape(flight, group_size, 2, capacity, piece)
        .transpose(0, 2, 3, 1, 4)
        .reshape(flight, 2, capacity * feature_count)
        .astype(jnp.float32)
    )
    out_sums = sums[:, 0].reshape(flight * capacity, feature_count)
    grad_sums = sums[:, 1].reshape(flight * capacity, feature_count)
    return out_sums, grad_sums


def exchange(chunks, axis):
    size = lax.axis_size(axis)
    me = lax.axis_index(axis)
    moved = [lax.dynamic_index_in_dim(chunks, me, 0, keepdims=False)]
    for shift in range(1, size):
        part = lax.dynamic_index_in_dim(chunks, (me + shift) % size, 0, keepdims=False)
        moved.append(lax.ppermute(part, axis, [(i, (i + shift) % size) for i in range(size)]))
    stacked = jnp.stack(moved)
    order = (me - jnp.arange(size, dtype=jnp.int32)) % size
    return jnp.take(stacked, order, axis=0)


def pick_rows(values, slot_table, filled):
    token_range = jnp.arange(values.shape[0], dtype=jnp.int32)
    onehot = (slot_table[:, :, None] == token_range[None, None, :]) & filled[:, :, None]
    picked = jnp.einsum(
        "fct,td->fcd", onehot.astype(values.dtype), values, preferred_element_type=jnp.float32
    )
    return picked.astype(values.dtype)


def exchange_relative(chunks, first):
    size = lax.axis_size("expert")
    me = lax.axis_index("expert")
    moved = [lax.dynamic_index_in_dim(chunks, me, 0, keepdims=False)]
    for shift in range(1, size):
        part = lax.dynamic_index_in_dim(chunks, (me + shift) % size, 0, keepdims=False)
        moved.append(lax.ppermute(part, "expert", [(i, (i + shift) % size) for i in range(size)]))
    return jnp.where(first, jnp.stack(moved), jnp.stack(moved[1:] + moved[:1]))


def by_parity(chunks, odd, flight, group_size):
    size = lax.axis_size("expert")
    me = lax.axis_index("expert")
    moved = []
    for shift in range(odd, size, group_size):
        block = (size - me % group_size - shift) % size
        part = lax.dynamic_index_in_dim(chunks, block, 0, keepdims=False)
        if shift == 0:
            moved.append(part)
        else:
            moved.append(lax.ppermute(part, "expert", [(i, (i + shift) % size) for i in range(size)]))
    stacked = jnp.stack(moved)
    chip = me // group_size
    order = (chip + odd * (me % group_size - 1) - jnp.arange(flight, dtype=jnp.int32)) % flight
    return stacked.reshape(flight * chunks.shape[1], chunks.shape[2]), order


def by_pair(
    normed, out_grad, slot_table, filled, gate_weight, up_weight, down_weight,
    member, expert_count, group_size,
):
    flight, capacity = slot_table.shape
    feature_count = normed.shape[1]
    sending = jnp.stack(
        [pick_rows(normed, slot_table, filled), pick_rows(out_grad, slot_table, filled)],
        axis=1,
    ).reshape(expert_count, capacity, feature_count)
    arrived = exchange_relative(sending, member == 0)
    swap = group_perm(expert_count, group_size, 1)
    partner = lax.ppermute(arrived, "expert", swap)
    first = (member == 0).astype(jnp.int32).reshape(1)
    both = expert_pair(
        first,
        arrived.reshape(expert_count * capacity, feature_count),
        partner.reshape(expert_count * capacity, feature_count),
        gate_weight,
        up_weight,
        down_weight,
    )
    sums = both.astype(jnp.float32) + lax.ppermute(both, "expert", swap).astype(jnp.float32)
    sums = sums.astype(jnp.bfloat16).reshape(2, expert_count, capacity, feature_count)
    grad_sums, grad_order = by_parity(sums[1], 0, flight, group_size)
    out_sums, out_order = by_parity(sums[0], 1, flight, group_size)
    return out_sums.astype(jnp.float32), grad_sums.astype(jnp.float32), out_order, grad_order


def shards(
    tokens,
    steering,
    norm_gain,
    route_ids,
    route_gates,
    gate_weight,
    up_weight,
    down_weight,
    out_grad,
):
    expert_count = lax.axis_size("expert")
    flight = EXP_FLIGHT
    group_size = expert_count // flight
    capacity = CAP
    feature_count = tokens.shape[1]
    piece = feature_count // group_size
    member = lax.axis_index("expert") % group_size
    residual, inverse, normed = normalize(tokens, steering, norm_gain)
    slot_table, filled, combine = slot_tables(route_ids, route_gates, flight, capacity)
    out_combine = combine
    grad_combine = combine
    if group_size == 2:
        out_sums, grad_sums, out_order, grad_order = by_pair(
            normed, out_grad, slot_table, filled, gate_weight, up_weight, down_weight,
            member, expert_count, group_size,
        )
        by_expert = combine.reshape(combine.shape[0], flight, capacity)
        out_combine = jnp.take(by_expert, out_order, axis=1).reshape(combine.shape)
        grad_combine = jnp.take(by_expert, grad_order, axis=1).reshape(combine.shape)
    else:
        out_sums, grad_sums = by_features(
            normed, out_grad, slot_table, filled, gate_weight, up_weight, down_weight,
            member, expert_count, group_size,
        )
    mixture = apply_combine(out_combine, out_sums)
    back_normed = apply_combine(grad_combine, grad_sums)
    layer_out = (residual + mixture).astype(jnp.bfloat16)
    total_grad = norm_backward(residual, inverse, norm_gain, back_normed, out_grad)
    steer_grad = butterfly_sum(jnp.sum(total_grad, axis=0), ("expert", "dp"))
    return (layer_out, total_grad.astype(jnp.bfloat16), steer_grad)


def solution(mesh):
    in_specs = (
        P(("dp", "expert"), None),
        P(),
        P(),
        P(("dp", "expert"), None),
        P(("dp", "expert"), None),
        P(None, "expert"),
        P(None, "expert"),
        P("expert", None),
        P(("dp", "expert"), None),
    )
    out_specs = (P(("dp", "expert"), None), P(("dp", "expert"), None), P())
    return jax.shard_map(shards, mesh=mesh, in_specs=in_specs, out_specs=out_specs, check_vma=False)
```

```python
import jax
import jax.numpy as jnp
from jax import lax
from jax.sharding import PartitionSpec as P
from jax.experimental import pallas as pl
from jax.experimental.pallas import tpu as pltpu

EXP_FLIGHT = 4
CAP = 8


EPSILON = 1e-06
GATE_UNIT = 1.0 / 65536.0


def slot_tables(route_ids, route_gates, flight, capacity):
    count_rows = route_ids.shape[0]
    expert_range = jnp.arange(flight, dtype=jnp.int32)
    hit_mask = route_ids[:, :, None] == expert_range[None, None, :]
    member = jnp.any(hit_mask, axis=1)
    scaled = route_gates.astype(jnp.float32) * GATE_UNIT
    weights = jnp.sum(jnp.where(hit_mask, scaled[:, :, None], 0.0), axis=1)
    position = jnp.cumsum(member.astype(jnp.int32), axis=0) - 1
    slot_of = jnp.where(member, position, capacity)
    slot_range = jnp.arange(capacity, dtype=jnp.int32)
    matches = slot_of[:, :, None] == slot_range[None, None, :]
    row_range = jnp.arange(count_rows, dtype=jnp.int32)
    slot_table = jnp.sum(jnp.where(matches, row_range[:, None, None], 0), axis=0)
    filled = jnp.any(matches, axis=0)
    combine = jnp.where(matches, weights[:, :, None], 0.0).reshape(count_rows, flight * capacity)
    return (slot_table, filled, combine)


def dispatch_rows(values, slot_table, filled):
    picked = values[slot_table]
    return jnp.where(filled[:, :, None], picked, jnp.zeros((), values.dtype))


def normalize(tokens, steering, norm_gain):
    residual = tokens.astype(jnp.float32) + steering
    inverse = lax.rsqrt(jnp.mean(residual * residual, axis=-1, keepdims=True) + EPSILON)
    normed = (residual * inverse * norm_gain).astype(jnp.bfloat16)
    return (residual, inverse, normed)


def norm_backward(residual, inverse, norm_gain, back_normed, out_grad):
    scaled = back_normed * norm_gain
    inner_mean = jnp.mean(scaled * residual, axis=-1, keepdims=True)
    cubed = inverse * inverse * inverse
    return out_grad.astype(jnp.float32) + inverse * scaled - residual * cubed * inner_mean


def share_forward(token_rows, gate_cols, up_cols, down_rows):
    gate_pre = jnp.dot(token_rows, gate_cols, preferred_element_type=jnp.float32)
    up_pre = jnp.dot(token_rows, up_cols, preferred_element_type=jnp.float32)
    hidden = (jax.nn.silu(gate_pre) * up_pre).astype(jnp.bfloat16)
    forward = jnp.dot(hidden, down_rows, preferred_element_type=jnp.float32).astype(jnp.bfloat16)
    return (forward, gate_pre, up_pre)


def share_backward(grad_rows, gate_pre, up_pre, gate_cols, up_cols, down_rows):
    contract = (((1,), (1,)), ((), ()))
    back_hidden = lax.dot_general(
        grad_rows, down_rows, contract, preferred_element_type=jnp.float32
    )
    sigmoid = jax.nn.sigmoid(gate_pre)
    back_up = (back_hidden * gate_pre * sigmoid).astype(jnp.bfloat16)
    back_gate = (back_hidden * up_pre * sigmoid * (1.0 + gate_pre * (1.0 - sigmoid))).astype(
        jnp.bfloat16
    )
    backward = lax.dot_general(back_gate, gate_cols, contract, preferred_element_type=jnp.float32)
    backward = backward + lax.dot_general(
        back_up, up_cols, contract, preferred_element_type=jnp.float32
    )
    return backward.astype(jnp.bfloat16)


def _expert_kernel(x_ref, y_ref, g_ref, u_ref, d_ref, out_ref, back_ref, acc_o, acc_b):
    j = pl.program_id(1)
    @pl.when(j == 0)
    def _():
        acc_o[...] = jnp.zeros_like(acc_o)
        acc_b[...] = jnp.zeros_like(acc_b)
    x = x_ref[...]
    y = y_ref[...]
    gw = g_ref[...]
    uw = u_ref[...]
    dw = d_ref[...]
    nt = (((1,), (1,)), ((), ()))
    g = jnp.dot(x, gw, preferred_element_type=jnp.float32)
    u = jnp.dot(x, uw, preferred_element_type=jnp.float32)
    sig = jax.nn.sigmoid(g)
    hidden = (g * sig * u).astype(jnp.bfloat16)
    bh = lax.dot_general(y, dw, nt, preferred_element_type=jnp.float32)
    back_up = (bh * g * sig).astype(jnp.bfloat16)
    back_gate = (bh * u * sig * (1.0 + g * (1.0 - sig))).astype(jnp.bfloat16)
    acc_o[...] += jnp.dot(hidden, dw, preferred_element_type=jnp.float32)
    acc_b[...] += (lax.dot_general(back_gate, gw, nt, preferred_element_type=jnp.float32)
                   + lax.dot_general(back_up, uw, nt, preferred_element_type=jnp.float32))
    @pl.when(j == pl.num_programs(1) - 1)
    def _():
        out_ref[...] = acc_o[...].astype(out_ref.dtype)
        back_ref[...] = acc_b[...].astype(back_ref.dtype)

def expert_share(x, y, gw, uw, dw):
    rows, feat = x.shape
    hid = gw.shape[1]
    rb = min(rows, 128)
    hb = min(hid, 256)
    return pl.pallas_call(
        _expert_kernel,
        grid=(rows // rb, hid // hb),
        in_specs=[
            pl.BlockSpec((rb, feat), lambda i, j: (i, 0)),
            pl.BlockSpec((rb, feat), lambda i, j: (i, 0)),
            pl.BlockSpec((feat, hb), lambda i, j: (0, j)),
            pl.BlockSpec((feat, hb), lambda i, j: (0, j)),
            pl.BlockSpec((hb, feat), lambda i, j: (j, 0)),
        ],
        out_specs=[
            pl.BlockSpec((rb, feat), lambda i, j: (i, 0)),
            pl.BlockSpec((rb, feat), lambda i, j: (i, 0)),
        ],
        out_shape=[jax.ShapeDtypeStruct((rows, feat), jnp.bfloat16)] * 2,
        scratch_shapes=[pltpu.VMEM((rb, feat), jnp.float32)] * 2,
        compiler_params=pltpu.CompilerParams(
            dimension_semantics=("arbitrary", "arbitrary"), vmem_limit_bytes=56 * 1024 * 1024
        ),
    )(x, y, gw, uw, dw)


def _pair_kernel(
    first_ref, a_ref, p_ref, g_ref, u_ref, d_ref, both_ref, xs, ys, acc_o, acc_b
):
    j = pl.program_id(0)
    first = first_ref[0] == 1

    @pl.when(j == 0)
    def _():
        xs[...] = jnp.where(first, a_ref[...], p_ref[...])
        ys[...] = jnp.where(first, p_ref[...], a_ref[...])
        acc_o[...] = jnp.zeros_like(acc_o)
        acc_b[...] = jnp.zeros_like(acc_b)

    x = xs[...]
    y = ys[...]
    gw = g_ref[...]
    uw = u_ref[...]
    dw = d_ref[...]
    nt = (((1,), (1,)), ((), ()))
    g = jnp.dot(x, gw, preferred_element_type=jnp.float32)
    u = jnp.dot(x, uw, preferred_element_type=jnp.float32)
    sig = jax.nn.sigmoid(g)
    hidden = (g * sig * u).astype(jnp.bfloat16)
    bh = lax.dot_general(y, dw, nt, preferred_element_type=jnp.float32)
    back_up = (bh * g * sig).astype(jnp.bfloat16)
    back_gate = (bh * u * sig * (1.0 + g * (1.0 - sig))).astype(jnp.bfloat16)
    acc_o[...] += jnp.dot(hidden, dw, preferred_element_type=jnp.float32)
    acc_b[...] += lax.dot_general(
        back_gate, gw, nt, preferred_element_type=jnp.float32
    ) + lax.dot_general(back_up, uw, nt, preferred_element_type=jnp.float32)

    @pl.when(j == pl.num_programs(0) - 1)
    def _():
        both_ref[0] = acc_o[...].astype(both_ref.dtype)
        both_ref[1] = acc_b[...].astype(both_ref.dtype)


def expert_pair(first, arrived, partner, gw, uw, dw):
    rows, feat = arrived.shape
    hid = gw.shape[1]
    hb = min(hid, 256)
    full = pl.BlockSpec((rows, feat), lambda j, f: (0, 0))
    grid_spec = pltpu.PrefetchScalarGridSpec(
        num_scalar_prefetch=1,
        grid=(hid // hb,),
        in_specs=[
            full,
            full,
            pl.BlockSpec((feat, hb), lambda j, f: (0, j)),
            pl.BlockSpec((feat, hb), lambda j, f: (0, j)),
            pl.BlockSpec((hb, feat), lambda j, f: (j, 0)),
        ],
        out_specs=pl.BlockSpec((2, rows, feat), lambda j, f: (0, 0, 0)),
        scratch_shapes=[pltpu.VMEM((rows, feat), arrived.dtype)] * 2
        + [pltpu.VMEM((rows, feat), jnp.float32)] * 2,
    )
    return pl.pallas_call(
        _pair_kernel,
        grid_spec=grid_spec,
        out_shape=jax.ShapeDtypeStruct((2, rows, feat), jnp.bfloat16),
        compiler_params=pltpu.CompilerParams(
            dimension_semantics=("arbitrary",), vmem_limit_bytes=56 * 1024 * 1024
        ),
    )(first, arrived, partner, gw, uw, dw)


def apply_combine(combine, partial_sums):
    return jnp.dot(combine, partial_sums, precision=lax.Precision.HIGHEST)


def group_perm(expert_count, group_size, shift):
    return [
        (d, (d // group_size) * group_size + (d % group_size + shift) % group_size)
        for d in range(expert_count)
    ]


def group_gather(piece, member, expert_count, group_size):
    got = [piece]
    for shift in range(1, group_size):
        got.append(lax.ppermute(piece, "expert", group_perm(expert_count, group_size, shift)))
    stacked = jnp.stack(got)
    order = (member - jnp.arange(group_size, dtype=jnp.int32)) % group_size
    return jnp.take(stacked, order, axis=0)


def group_reduce_scatter(pieces, member, expert_count, group_size, axis):
    total = lax.dynamic_index_in_dim(pieces, member, axis, keepdims=False).astype(jnp.float32)
    for shift in range(1, group_size):
        target = (member + shift) % group_size
        part = lax.dynamic_index_in_dim(pieces, target, axis, keepdims=False)
        moved = lax.ppermute(part, "expert", group_perm(expert_count, group_size, shift))
        total = total + moved.astype(jnp.float32)
    return total


def butterfly_sum(value, steps):
    done = {}
    for axis, limit in steps:
        size = lax.axis_size(axis)
        if size & (size - 1):
            if axis not in done:
                value = lax.psum(value, axis)
                done[axis] = size
            continue
        bit = done.get(axis, 1)
        while bit < size and (limit is None or bit < 2 * limit):
            value = value + lax.ppermute(value, axis, [(i, i ^ bit) for i in range(size)])
            bit *= 2
        done[axis] = bit
    return value


def by_features(
    normed, out_grad, slot_table, filled, gate_weight, up_weight, down_weight,
    member, expert_count, group_size,
):
    flight, capacity = slot_table.shape
    feature_count = normed.shape[1]
    piece = feature_count // group_size
    packed = jnp.stack(
        [dispatch_rows(normed, slot_table, filled), dispatch_rows(out_grad, slot_table, filled)],
        axis=1,
    )
    sending = (
        packed.reshape(flight, 2, capacity, group_size, piece)
        .transpose(0, 3, 1, 2, 4)
        .reshape(expert_count, 2, capacity, piece)
    )
    arrived = lax.all_to_all(sending, "expert", split_axis=0, concat_axis=0, tiled=True)
    whole = group_gather(arrived, member, expert_count, group_size)
    rows = whole.transpose(1, 2, 3, 0, 4).reshape(expert_count, 2, capacity, feature_count)
    local_rows = rows[:, 0].reshape(expert_count * capacity, feature_count)
    local_grads = rows[:, 1].reshape(expert_count * capacity, feature_count)
    forward, backward = expert_share(local_rows, local_grads, gate_weight, up_weight, down_weight)
    both = jnp.stack(
        [
            forward.reshape(expert_count, capacity, feature_count),
            backward.reshape(expert_count, capacity, feature_count),
        ],
        axis=1,
    ).reshape(expert_count, 2, capacity, group_size, piece)
    summed = group_reduce_scatter(both, member, expert_count, group_size, 3)
    came = lax.all_to_all(
        summed.astype(jnp.bfloat16), "expert", split_axis=0, concat_axis=0, tiled=True
    )
    sums = (
        came.reshape(flight, group_size, 2, capacity, piece)
        .transpose(0, 2, 3, 1, 4)
        .reshape(flight, 2, capacity * feature_count)
        .astype(jnp.float32)
    )
    out_sums = sums[:, 0].reshape(flight * capacity, feature_count)
    grad_sums = sums[:, 1].reshape(flight * capacity, feature_count)
    return out_sums, grad_sums


def exchange(chunks, axis):
    size = lax.axis_size(axis)
    me = lax.axis_index(axis)
    moved = [lax.dynamic_index_in_dim(chunks, me, 0, keepdims=False)]
    for shift in range(1, size):
        part = lax.dynamic_index_in_dim(chunks, (me + shift) % size, 0, keepdims=False)
        moved.append(lax.ppermute(part, axis, [(i, (i + shift) % size) for i in range(size)]))
    stacked = jnp.stack(moved)
    order = (me - jnp.arange(size, dtype=jnp.int32)) % size
    return jnp.take(stacked, order, axis=0)


def pick_rows(values, slot_table, filled):
    token_range = jnp.arange(values.shape[0], dtype=jnp.int32)
    onehot = (slot_table[:, :, None] == token_range[None, None, :]) & filled[:, :, None]
    picked = jnp.einsum(
        "fct,td->fcd", onehot.astype(values.dtype), values, preferred_element_type=jnp.float32
    )
    return picked.astype(values.dtype)


def exchange_relative(chunks, first):
    size = lax.axis_size("expert")
    me = lax.axis_index("expert")
    moved = [lax.dynamic_index_in_dim(chunks, me, 0, keepdims=False)]
    for shift in range(1, size):
        part = lax.dynamic_index_in_dim(chunks, (me + shift) % size, 0, keepdims=False)
        moved.append(lax.ppermute(part, "expert", [(i, (i + shift) % size) for i in range(size)]))
    return jnp.where(first, jnp.stack(moved), jnp.stack(moved[1:] + moved[:1]))


def by_parity(chunks, odd, flight, group_size):
    size = lax.axis_size("expert")
    me = lax.axis_index("expert")
    moved = []
    for shift in range(odd, size, group_size):
        block = (size - me % group_size - shift) % size
        part = lax.dynamic_index_in_dim(chunks, block, 0, keepdims=False)
        if shift == 0:
            moved.append(part)
        else:
            moved.append(lax.ppermute(part, "expert", [(i, (i + shift) % size) for i in range(size)]))
    stacked = jnp.stack(moved)
    chip = me // group_size
    order = (chip + odd * (me % group_size - 1) - jnp.arange(flight, dtype=jnp.int32)) % flight
    return stacked.reshape(flight * chunks.shape[1], chunks.shape[2]), order


def by_pair(
    normed, out_grad, slot_table, filled, gate_weight, up_weight, down_weight,
    member, expert_count, group_size,
):
    flight, capacity = slot_table.shape
    feature_count = normed.shape[1]
    sending = jnp.stack(
        [pick_rows(normed, slot_table, filled), pick_rows(out_grad, slot_table, filled)],
        axis=1,
    ).reshape(expert_count, capacity, feature_count)
    arrived = exchange_relative(sending, member == 0)
    swap = group_perm(expert_count, group_size, 1)
    partner = lax.ppermute(arrived, "expert", swap)
    first = (member == 0).astype(jnp.int32).reshape(1)
    both = expert_pair(
        first,
        arrived.reshape(expert_count * capacity, feature_count),
        partner.reshape(expert_count * capacity, feature_count),
        gate_weight,
        up_weight,
        down_weight,
    )
    sums = both.astype(jnp.float32) + lax.ppermute(both, "expert", swap).astype(jnp.float32)
    sums = sums.astype(jnp.bfloat16).reshape(2, expert_count, capacity, feature_count)
    grad_sums, grad_order = by_parity(sums[1], 0, flight, group_size)
    out_sums, out_order = by_parity(sums[0], 1, flight, group_size)
    return out_sums.astype(jnp.float32), grad_sums.astype(jnp.float32), out_order, grad_order


def shards(
    tokens,
    steering,
    norm_gain,
    route_ids,
    route_gates,
    gate_weight,
    up_weight,
    down_weight,
    out_grad,
):
    expert_count = lax.axis_size("expert")
    flight = EXP_FLIGHT
    group_size = expert_count // flight
    capacity = CAP
    feature_count = tokens.shape[1]
    piece = feature_count // group_size
    member = lax.axis_index("expert") % group_size
    residual, inverse, normed = normalize(tokens, steering, norm_gain)
    slot_table, filled, combine = slot_tables(route_ids, route_gates, flight, capacity)
    out_combine = combine
    grad_combine = combine
    if group_size == 2:
        out_sums, grad_sums, out_order, grad_order = by_pair(
            normed, out_grad, slot_table, filled, gate_weight, up_weight, down_weight,
            member, expert_count, group_size,
        )
        by_expert = combine.reshape(combine.shape[0], flight, capacity)
        out_combine = jnp.take(by_expert, out_order, axis=1).reshape(combine.shape)
        grad_combine = jnp.take(by_expert, grad_order, axis=1).reshape(combine.shape)
    else:
        out_sums, grad_sums = by_features(
            normed, out_grad, slot_table, filled, gate_weight, up_weight, down_weight,
            member, expert_count, group_size,
        )
    mixture = apply_combine(out_combine, out_sums)
    back_normed = apply_combine(grad_combine, grad_sums)
    layer_out = (residual + mixture).astype(jnp.bfloat16)
    total_grad = norm_backward(residual, inverse, norm_gain, back_normed, out_grad)
    steer_grad = butterfly_sum(
        jnp.sum(total_grad, axis=0), (("expert", 1), ("dp", None), ("expert", None))
    )
    return (layer_out, total_grad.astype(jnp.bfloat16), steer_grad)


def solution(mesh):
    in_specs = (
        P(("dp", "expert"), None),
        P(),
        P(),
        P(("dp", "expert"), None),
        P(("dp", "expert"), None),
        P(None, "expert"),
        P(None, "expert"),
        P("expert", None),
        P(("dp", "expert"), None),
    )
    out_specs = (P(("dp", "expert"), None), P(("dp", "expert"), None), P())
    return jax.shard_map(shards, mesh=mesh, in_specs=in_specs, out_specs=out_specs, check_vma=False)
```

```python
import jax
import jax.numpy as jnp
from jax import lax
from jax.sharding import PartitionSpec as P
from jax.experimental import pallas as pl
from jax.experimental.pallas import tpu as pltpu

EXP_FLIGHT = 4
CAP = 8


EPSILON = 1e-06
GATE_UNIT = 1.0 / 65536.0


def slot_tables(route_ids, route_gates, flight, capacity):
    count_rows = route_ids.shape[0]
    expert_range = jnp.arange(flight, dtype=jnp.int32)
    hit_mask = route_ids[:, :, None] == expert_range[None, None, :]
    member = jnp.any(hit_mask, axis=1)
    scaled = route_gates.astype(jnp.float32) * GATE_UNIT
    weights = jnp.sum(jnp.where(hit_mask, scaled[:, :, None], 0.0), axis=1)
    position = jnp.cumsum(member.astype(jnp.int32), axis=0) - 1
    slot_of = jnp.where(member, position, capacity)
    slot_range = jnp.arange(capacity, dtype=jnp.int32)
    matches = slot_of[:, :, None] == slot_range[None, None, :]
    row_range = jnp.arange(count_rows, dtype=jnp.int32)
    slot_table = jnp.sum(jnp.where(matches, row_range[:, None, None], 0), axis=0)
    filled = jnp.any(matches, axis=0)
    combine = jnp.where(matches, weights[:, :, None], 0.0).reshape(count_rows, flight * capacity)
    return (slot_table, filled, combine)


def dispatch_rows(values, slot_table, filled):
    picked = values[slot_table]
    return jnp.where(filled[:, :, None], picked, jnp.zeros((), values.dtype))


def normalize(tokens, steering, norm_gain):
    residual = tokens.astype(jnp.float32) + steering
    inverse = lax.rsqrt(jnp.mean(residual * residual, axis=-1, keepdims=True) + EPSILON)
    normed = (residual * inverse * norm_gain).astype(jnp.bfloat16)
    return (residual, inverse, normed)


def norm_backward(residual, inverse, norm_gain, back_normed, out_grad):
    scaled = back_normed * norm_gain
    inner_mean = jnp.mean(scaled * residual, axis=-1, keepdims=True)
    cubed = inverse * inverse * inverse
    return out_grad.astype(jnp.float32) + inverse * scaled - residual * cubed * inner_mean


def share_forward(token_rows, gate_cols, up_cols, down_rows):
    gate_pre = jnp.dot(token_rows, gate_cols, preferred_element_type=jnp.float32)
    up_pre = jnp.dot(token_rows, up_cols, preferred_element_type=jnp.float32)
    hidden = (jax.nn.silu(gate_pre) * up_pre).astype(jnp.bfloat16)
    forward = jnp.dot(hidden, down_rows, preferred_element_type=jnp.float32).astype(jnp.bfloat16)
    return (forward, gate_pre, up_pre)


def share_backward(grad_rows, gate_pre, up_pre, gate_cols, up_cols, down_rows):
    contract = (((1,), (1,)), ((), ()))
    back_hidden = lax.dot_general(
        grad_rows, down_rows, contract, preferred_element_type=jnp.float32
    )
    sigmoid = jax.nn.sigmoid(gate_pre)
    back_up = (back_hidden * gate_pre * sigmoid).astype(jnp.bfloat16)
    back_gate = (back_hidden * up_pre * sigmoid * (1.0 + gate_pre * (1.0 - sigmoid))).astype(
        jnp.bfloat16
    )
    backward = lax.dot_general(back_gate, gate_cols, contract, preferred_element_type=jnp.float32)
    backward = backward + lax.dot_general(
        back_up, up_cols, contract, preferred_element_type=jnp.float32
    )
    return backward.astype(jnp.bfloat16)


def _expert_kernel(x_ref, y_ref, g_ref, u_ref, d_ref, out_ref, back_ref, acc_o, acc_b):
    j = pl.program_id(1)
    @pl.when(j == 0)
    def _():
        acc_o[...] = jnp.zeros_like(acc_o)
        acc_b[...] = jnp.zeros_like(acc_b)
    x = x_ref[...]
    y = y_ref[...]
    gw = g_ref[...]
    uw = u_ref[...]
    dw = d_ref[...]
    nt = (((1,), (1,)), ((), ()))
    g = jnp.dot(x, gw, preferred_element_type=jnp.float32)
    u = jnp.dot(x, uw, preferred_element_type=jnp.float32)
    sig = jax.nn.sigmoid(g)
    hidden = (g * sig * u).astype(jnp.bfloat16)
    bh = lax.dot_general(y, dw, nt, preferred_element_type=jnp.float32)
    back_up = (bh * g * sig).astype(jnp.bfloat16)
    back_gate = (bh * u * sig * (1.0 + g * (1.0 - sig))).astype(jnp.bfloat16)
    acc_o[...] += jnp.dot(hidden, dw, preferred_element_type=jnp.float32)
    acc_b[...] += (lax.dot_general(back_gate, gw, nt, preferred_element_type=jnp.float32)
                   + lax.dot_general(back_up, uw, nt, preferred_element_type=jnp.float32))
    @pl.when(j == pl.num_programs(1) - 1)
    def _():
        out_ref[...] = acc_o[...].astype(out_ref.dtype)
        back_ref[...] = acc_b[...].astype(back_ref.dtype)

def expert_share(x, y, gw, uw, dw):
    rows, feat = x.shape
    hid = gw.shape[1]
    rb = min(rows, 128)
    hb = min(hid, 256)
    return pl.pallas_call(
        _expert_kernel,
        grid=(rows // rb, hid // hb),
        in_specs=[
            pl.BlockSpec((rb, feat), lambda i, j: (i, 0)),
            pl.BlockSpec((rb, feat), lambda i, j: (i, 0)),
            pl.BlockSpec((feat, hb), lambda i, j: (0, j)),
            pl.BlockSpec((feat, hb), lambda i, j: (0, j)),
            pl.BlockSpec((hb, feat), lambda i, j: (j, 0)),
        ],
        out_specs=[
            pl.BlockSpec((rb, feat), lambda i, j: (i, 0)),
            pl.BlockSpec((rb, feat), lambda i, j: (i, 0)),
        ],
        out_shape=[jax.ShapeDtypeStruct((rows, feat), jnp.bfloat16)] * 2,
        scratch_shapes=[pltpu.VMEM((rb, feat), jnp.float32)] * 2,
        compiler_params=pltpu.CompilerParams(
            dimension_semantics=("arbitrary", "arbitrary"), vmem_limit_bytes=56 * 1024 * 1024
        ),
    )(x, y, gw, uw, dw)


def _pair_kernel(
    first_ref, a_ref, p_ref, g_ref, u_ref, d_ref, fwd_ref, bwd_ref, xs, ys, acc_o, acc_b
):
    j = pl.program_id(0)
    first = first_ref[0] == 1

    @pl.when(j == 0)
    def _():
        xs[...] = jnp.where(first, a_ref[...], p_ref[...])
        ys[...] = jnp.where(first, p_ref[...], a_ref[...])
        acc_o[...] = jnp.zeros_like(acc_o)
        acc_b[...] = jnp.zeros_like(acc_b)

    x = xs[...]
    y = ys[...]
    gw = g_ref[...]
    uw = u_ref[...]
    dw = d_ref[...]
    nt = (((1,), (1,)), ((), ()))
    g = jnp.dot(x, gw, preferred_element_type=jnp.float32)
    u = jnp.dot(x, uw, preferred_element_type=jnp.float32)
    sig = jax.nn.sigmoid(g)
    hidden = (g * sig * u).astype(jnp.bfloat16)
    bh = lax.dot_general(y, dw, nt, preferred_element_type=jnp.float32)
    back_up = (bh * g * sig).astype(jnp.bfloat16)
    back_gate = (bh * u * sig * (1.0 + g * (1.0 - sig))).astype(jnp.bfloat16)
    acc_o[...] += jnp.dot(hidden, dw, preferred_element_type=jnp.float32)
    acc_b[...] += lax.dot_general(
        back_gate, gw, nt, preferred_element_type=jnp.float32
    ) + lax.dot_general(back_up, uw, nt, preferred_element_type=jnp.float32)

    @pl.when(j == pl.num_programs(0) - 1)
    def _():
        fwd_ref[...] = acc_o[...].astype(fwd_ref.dtype)
        bwd_ref[...] = acc_b[...].astype(bwd_ref.dtype)


def expert_pair(first, arrived, partner, gw, uw, dw):
    rows, feat = arrived.shape
    hid = gw.shape[1]
    hb = min(hid, 256)
    full = pl.BlockSpec((rows, feat), lambda j, f: (0, 0))
    grid_spec = pltpu.PrefetchScalarGridSpec(
        num_scalar_prefetch=1,
        grid=(hid // hb,),
        in_specs=[
            full,
            full,
            pl.BlockSpec((feat, hb), lambda j, f: (0, j)),
            pl.BlockSpec((feat, hb), lambda j, f: (0, j)),
            pl.BlockSpec((hb, feat), lambda j, f: (j, 0)),
        ],
        out_specs=[full, full],
        scratch_shapes=[pltpu.VMEM((rows, feat), arrived.dtype)] * 2
        + [pltpu.VMEM((rows, feat), jnp.float32)] * 2,
    )
    return pl.pallas_call(
        _pair_kernel,
        grid_spec=grid_spec,
        out_shape=[jax.ShapeDtypeStruct((rows, feat), jnp.bfloat16)] * 2,
        compiler_params=pltpu.CompilerParams(
            dimension_semantics=("arbitrary",), vmem_limit_bytes=56 * 1024 * 1024
        ),
    )(first, arrived, partner, gw, uw, dw)


def apply_combine(combine, partial_sums):
    return jnp.dot(combine, partial_sums, precision=lax.Precision.HIGHEST)


def group_perm(expert_count, group_size, shift):
    return [
        (d, (d // group_size) * group_size + (d % group_size + shift) % group_size)
        for d in range(expert_count)
    ]


def group_gather(piece, member, expert_count, group_size):
    got = [piece]
    for shift in range(1, group_size):
        got.append(lax.ppermute(piece, "expert", group_perm(expert_count, group_size, shift)))
    stacked = jnp.stack(got)
    order = (member - jnp.arange(group_size, dtype=jnp.int32)) % group_size
    return jnp.take(stacked, order, axis=0)


def group_reduce_scatter(pieces, member, expert_count, group_size, axis):
    total = lax.dynamic_index_in_dim(pieces, member, axis, keepdims=False).astype(jnp.float32)
    for shift in range(1, group_size):
        target = (member + shift) % group_size
        part = lax.dynamic_index_in_dim(pieces, target, axis, keepdims=False)
        moved = lax.ppermute(part, "expert", group_perm(expert_count, group_size, shift))
        total = total + moved.astype(jnp.float32)
    return total


def butterfly_sum(value, steps):
    done = {}
    for axis, limit in steps:
        size = lax.axis_size(axis)
        if size & (size - 1):
            if axis not in done:
                value = lax.psum(value, axis)
                done[axis] = size
            continue
        bit = done.get(axis, 1)
        while bit < size and (limit is None or bit < 2 * limit):
            value = value + lax.ppermute(value, axis, [(i, i ^ bit) for i in range(size)])
            bit *= 2
        done[axis] = bit
    return value


def by_features(
    normed, out_grad, slot_table, filled, gate_weight, up_weight, down_weight,
    member, expert_count, group_size,
):
    flight, capacity = slot_table.shape
    feature_count = normed.shape[1]
    piece = feature_count // group_size
    packed = jnp.stack(
        [dispatch_rows(normed, slot_table, filled), dispatch_rows(out_grad, slot_table, filled)],
        axis=1,
    )
    sending = (
        packed.reshape(flight, 2, capacity, group_size, piece)
        .transpose(0, 3, 1, 2, 4)
        .reshape(expert_count, 2, capacity, piece)
    )
    arrived = lax.all_to_all(sending, "expert", split_axis=0, concat_axis=0, tiled=True)
    whole = group_gather(arrived, member, expert_count, group_size)
    rows = whole.transpose(1, 2, 3, 0, 4).reshape(expert_count, 2, capacity, feature_count)
    local_rows = rows[:, 0].reshape(expert_count * capacity, feature_count)
    local_grads = rows[:, 1].reshape(expert_count * capacity, feature_count)
    forward, backward = expert_share(local_rows, local_grads, gate_weight, up_weight, down_weight)
    both = jnp.stack(
        [
            forward.reshape(expert_count, capacity, feature_count),
            backward.reshape(expert_count, capacity, feature_count),
        ],
        axis=1,
    ).reshape(expert_count, 2, capacity, group_size, piece)
    summed = group_reduce_scatter(both, member, expert_count, group_size, 3)
    came = lax.all_to_all(
        summed.astype(jnp.bfloat16), "expert", split_axis=0, concat_axis=0, tiled=True
    )
    sums = (
        came.reshape(flight, group_size, 2, capacity, piece)
        .transpose(0, 2, 3, 1, 4)
        .reshape(flight, 2, capacity * feature_count)
        .astype(jnp.float32)
    )
    out_sums = sums[:, 0].reshape(flight * capacity, feature_count)
    grad_sums = sums[:, 1].reshape(flight * capacity, feature_count)
    return out_sums, grad_sums


def exchange(chunks, axis):
    size = lax.axis_size(axis)
    me = lax.axis_index(axis)
    moved = [lax.dynamic_index_in_dim(chunks, me, 0, keepdims=False)]
    for shift in range(1, size):
        part = lax.dynamic_index_in_dim(chunks, (me + shift) % size, 0, keepdims=False)
        moved.append(lax.ppermute(part, axis, [(i, (i + shift) % size) for i in range(size)]))
    stacked = jnp.stack(moved)
    order = (me - jnp.arange(size, dtype=jnp.int32)) % size
    return jnp.take(stacked, order, axis=0)


def pick_rows(values, slot_table, filled):
    token_range = jnp.arange(values.shape[0], dtype=jnp.int32)
    onehot = (slot_table[:, :, None] == token_range[None, None, :]) & filled[:, :, None]
    picked = jnp.einsum(
        "fct,td->fcd", onehot.astype(values.dtype), values, preferred_element_type=jnp.float32
    )
    return picked.astype(values.dtype)


def exchange_relative(chunks, first):
    size = lax.axis_size("expert")
    me = lax.axis_index("expert")
    moved = [lax.dynamic_index_in_dim(chunks, me, 0, keepdims=False)]
    for shift in range(1, size):
        part = lax.dynamic_index_in_dim(chunks, (me + shift) % size, 0, keepdims=False)
        moved.append(lax.ppermute(part, "expert", [(i, (i + shift) % size) for i in range(size)]))
    return jnp.where(first, jnp.stack(moved), jnp.stack(moved[1:] + moved[:1]))


def by_parity(chunks, odd, flight, group_size):
    size = lax.axis_size("expert")
    me = lax.axis_index("expert")
    moved = []
    for shift in range(odd, size, group_size):
        block = (size - me % group_size - shift) % size
        part = lax.dynamic_index_in_dim(chunks, block, 0, keepdims=False)
        if shift == 0:
            moved.append(part)
        else:
            moved.append(lax.ppermute(part, "expert", [(i, (i + shift) % size) for i in range(size)]))
    stacked = jnp.stack(moved)
    chip = me // group_size
    order = (chip + odd * (me % group_size - 1) - jnp.arange(flight, dtype=jnp.int32)) % flight
    return stacked.reshape(flight * chunks.shape[1], chunks.shape[2]), order


def by_pair(
    normed, out_grad, slot_table, filled, gate_weight, up_weight, down_weight,
    member, expert_count, group_size,
):
    flight, capacity = slot_table.shape
    feature_count = normed.shape[1]
    sending = jnp.stack(
        [pick_rows(normed, slot_table, filled), pick_rows(out_grad, slot_table, filled)],
        axis=1,
    ).reshape(expert_count, capacity, feature_count)
    arrived = exchange_relative(sending, member == 0)
    swap = group_perm(expert_count, group_size, 1)
    partner = lax.ppermute(arrived, "expert", swap)
    first = (member == 0).astype(jnp.int32).reshape(1)
    forward, backward = expert_pair(
        first,
        arrived.reshape(expert_count * capacity, feature_count),
        partner.reshape(expert_count * capacity, feature_count),
        gate_weight,
        up_weight,
        down_weight,
    )
    shape = (expert_count, capacity, feature_count)
    grad_total = backward.astype(jnp.float32) + lax.ppermute(backward, "expert", swap).astype(
        jnp.float32
    )
    grad_sums, grad_order = by_parity(
        grad_total.astype(jnp.bfloat16).reshape(shape), 0, flight, group_size
    )
    out_total = forward.astype(jnp.float32) + lax.ppermute(forward, "expert", swap).astype(
        jnp.float32
    )
    out_sums, out_order = by_parity(
        out_total.astype(jnp.bfloat16).reshape(shape), 1, flight, group_size
    )
    return out_sums.astype(jnp.float32), grad_sums.astype(jnp.float32), out_order, grad_order


def shards(
    tokens,
    steering,
    norm_gain,
    route_ids,
    route_gates,
    gate_weight,
    up_weight,
    down_weight,
    out_grad,
):
    expert_count = lax.axis_size("expert")
    flight = EXP_FLIGHT
    group_size = expert_count // flight
    capacity = CAP
    feature_count = tokens.shape[1]
    piece = feature_count // group_size
    member = lax.axis_index("expert") % group_size
    residual, inverse, normed = normalize(tokens, steering, norm_gain)
    slot_table, filled, combine = slot_tables(route_ids, route_gates, flight, capacity)
    out_combine = combine
    grad_combine = combine
    if group_size == 2:
        out_sums, grad_sums, out_order, grad_order = by_pair(
            normed, out_grad, slot_table, filled, gate_weight, up_weight, down_weight,
            member, expert_count, group_size,
        )
        by_expert = combine.reshape(combine.shape[0], flight, capacity)
        out_combine = jnp.take(by_expert, out_order, axis=1).reshape(combine.shape)
        grad_combine = jnp.take(by_expert, grad_order, axis=1).reshape(combine.shape)
    else:
        out_sums, grad_sums = by_features(
            normed, out_grad, slot_table, filled, gate_weight, up_weight, down_weight,
            member, expert_count, group_size,
        )
    mixture = apply_combine(out_combine, out_sums)
    back_normed = apply_combine(grad_combine, grad_sums)
    layer_out = (residual + mixture).astype(jnp.bfloat16)
    total_grad = norm_backward(residual, inverse, norm_gain, back_normed, out_grad)
    steer_grad = butterfly_sum(
        jnp.sum(total_grad, axis=0), (("expert", 1), ("dp", None), ("expert", None))
    )
    return (layer_out, total_grad.astype(jnp.bfloat16), steer_grad)


def solution(mesh):
    in_specs = (
        P(("dp", "expert"), None),
        P(),
        P(),
        P(("dp", "expert"), None),
        P(("dp", "expert"), None),
        P(None, "expert"),
        P(None, "expert"),
        P("expert", None),
        P(("dp", "expert"), None),
    )
    out_specs = (P(("dp", "expert"), None), P(("dp", "expert"), None), P())
    return jax.shard_map(shards, mesh=mesh, in_specs=in_specs, out_specs=out_specs, check_vma=False)
```

```python
import jax
import jax.numpy as jnp
from jax import lax
from jax.sharding import PartitionSpec as P
from jax.experimental import pallas as pl
from jax.experimental.pallas import tpu as pltpu

EXP_FLIGHT = 4
CAP = 8


EPSILON = 1e-06
GATE_UNIT = 1.0 / 65536.0


def slot_tables(route_ids, route_gates, flight, capacity):
    count_rows = route_ids.shape[0]
    expert_range = jnp.arange(flight, dtype=jnp.int32)
    hit_mask = route_ids[:, :, None] == expert_range[None, None, :]
    member = jnp.any(hit_mask, axis=1)
    scaled = route_gates.astype(jnp.float32) * GATE_UNIT
    weights = jnp.sum(jnp.where(hit_mask, scaled[:, :, None], 0.0), axis=1)
    position = jnp.cumsum(member.astype(jnp.int32), axis=0) - 1
    slot_of = jnp.where(member, position, capacity)
    slot_range = jnp.arange(capacity, dtype=jnp.int32)
    matches = slot_of[:, :, None] == slot_range[None, None, :]
    row_range = jnp.arange(count_rows, dtype=jnp.int32)
    slot_table = jnp.sum(jnp.where(matches, row_range[:, None, None], 0), axis=0)
    filled = jnp.any(matches, axis=0)
    combine = jnp.where(matches, weights[:, :, None], 0.0).reshape(count_rows, flight * capacity)
    return (slot_table, filled, combine)


def dispatch_rows(values, slot_table, filled):
    picked = values[slot_table]
    return jnp.where(filled[:, :, None], picked, jnp.zeros((), values.dtype))


def normalize(tokens, steering, norm_gain):
    residual = tokens.astype(jnp.float32) + steering
    inverse = lax.rsqrt(jnp.mean(residual * residual, axis=-1, keepdims=True) + EPSILON)
    normed = (residual * inverse * norm_gain).astype(jnp.bfloat16)
    return (residual, inverse, normed)


def norm_backward(residual, inverse, norm_gain, back_normed, out_grad):
    scaled = back_normed * norm_gain
    inner_mean = jnp.mean(scaled * residual, axis=-1, keepdims=True)
    cubed = inverse * inverse * inverse
    return out_grad.astype(jnp.float32) + inverse * scaled - residual * cubed * inner_mean


def share_forward(token_rows, gate_cols, up_cols, down_rows):
    gate_pre = jnp.dot(token_rows, gate_cols, preferred_element_type=jnp.float32)
    up_pre = jnp.dot(token_rows, up_cols, preferred_element_type=jnp.float32)
    hidden = (jax.nn.silu(gate_pre) * up_pre).astype(jnp.bfloat16)
    forward = jnp.dot(hidden, down_rows, preferred_element_type=jnp.float32).astype(jnp.bfloat16)
    return (forward, gate_pre, up_pre)


def share_backward(grad_rows, gate_pre, up_pre, gate_cols, up_cols, down_rows):
    contract = (((1,), (1,)), ((), ()))
    back_hidden = lax.dot_general(
        grad_rows, down_rows, contract, preferred_element_type=jnp.float32
    )
    sigmoid = jax.nn.sigmoid(gate_pre)
    back_up = (back_hidden * gate_pre * sigmoid).astype(jnp.bfloat16)
    back_gate = (back_hidden * up_pre * sigmoid * (1.0 + gate_pre * (1.0 - sigmoid))).astype(
        jnp.bfloat16
    )
    backward = lax.dot_general(back_gate, gate_cols, contract, preferred_element_type=jnp.float32)
    backward = backward + lax.dot_general(
        back_up, up_cols, contract, preferred_element_type=jnp.float32
    )
    return backward.astype(jnp.bfloat16)


def _expert_kernel(x_ref, y_ref, g_ref, u_ref, d_ref, out_ref, back_ref, acc_o, acc_b):
    j = pl.program_id(1)
    @pl.when(j == 0)
    def _():
        acc_o[...] = jnp.zeros_like(acc_o)
        acc_b[...] = jnp.zeros_like(acc_b)
    x = x_ref[...]
    y = y_ref[...]
    gw = g_ref[...]
    uw = u_ref[...]
    dw = d_ref[...]
    nt = (((1,), (1,)), ((), ()))
    g = jnp.dot(x, gw, preferred_element_type=jnp.float32)
    u = jnp.dot(x, uw, preferred_element_type=jnp.float32)
    sig = jax.nn.sigmoid(g)
    hidden = (g * sig * u).astype(jnp.bfloat16)
    bh = lax.dot_general(y, dw, nt, preferred_element_type=jnp.float32)
    back_up = (bh * g * sig).astype(jnp.bfloat16)
    back_gate = (bh * u * sig * (1.0 + g * (1.0 - sig))).astype(jnp.bfloat16)
    acc_o[...] += jnp.dot(hidden, dw, preferred_element_type=jnp.float32)
    acc_b[...] += (lax.dot_general(back_gate, gw, nt, preferred_element_type=jnp.float32)
                   + lax.dot_general(back_up, uw, nt, preferred_element_type=jnp.float32))
    @pl.when(j == pl.num_programs(1) - 1)
    def _():
        out_ref[...] = acc_o[...].astype(out_ref.dtype)
        back_ref[...] = acc_b[...].astype(back_ref.dtype)

def expert_share(x, y, gw, uw, dw):
    rows, feat = x.shape
    hid = gw.shape[1]
    rb = min(rows, 128)
    hb = min(hid, 256)
    return pl.pallas_call(
        _expert_kernel,
        grid=(rows // rb, hid // hb),
        in_specs=[
            pl.BlockSpec((rb, feat), lambda i, j: (i, 0)),
            pl.BlockSpec((rb, feat), lambda i, j: (i, 0)),
            pl.BlockSpec((feat, hb), lambda i, j: (0, j)),
            pl.BlockSpec((feat, hb), lambda i, j: (0, j)),
            pl.BlockSpec((hb, feat), lambda i, j: (j, 0)),
        ],
        out_specs=[
            pl.BlockSpec((rb, feat), lambda i, j: (i, 0)),
            pl.BlockSpec((rb, feat), lambda i, j: (i, 0)),
        ],
        out_shape=[jax.ShapeDtypeStruct((rows, feat), jnp.bfloat16)] * 2,
        scratch_shapes=[pltpu.VMEM((rb, feat), jnp.float32)] * 2,
        compiler_params=pltpu.CompilerParams(
            dimension_semantics=("arbitrary", "arbitrary"), vmem_limit_bytes=56 * 1024 * 1024
        ),
    )(x, y, gw, uw, dw)


def _pair_kernel(
    first_ref, a_ref, p_ref, g_ref, u_ref, d_ref, fwd_ref, bwd_ref, xs, ys, acc_o, acc_b
):
    j = pl.program_id(0)
    first = first_ref[0] == 1

    @pl.when(j == 0)
    def _():
        xs[...] = jnp.where(first, a_ref[...], p_ref[...])
        ys[...] = jnp.where(first, p_ref[...], a_ref[...])
        acc_o[...] = jnp.zeros_like(acc_o)
        acc_b[...] = jnp.zeros_like(acc_b)

    x = xs[...]
    y = ys[...]
    gw = g_ref[...]
    uw = u_ref[...]
    dw = d_ref[...]
    nt = (((1,), (1,)), ((), ()))
    g = jnp.dot(x, gw, preferred_element_type=jnp.float32)
    u = jnp.dot(x, uw, preferred_element_type=jnp.float32)
    sig = jax.nn.sigmoid(g)
    hidden = (g * sig * u).astype(jnp.bfloat16)
    bh = lax.dot_general(y, dw, nt, preferred_element_type=jnp.float32)
    back_up = (bh * g * sig).astype(jnp.bfloat16)
    back_gate = (bh * u * sig * (1.0 + g * (1.0 - sig))).astype(jnp.bfloat16)
    acc_o[...] += jnp.dot(hidden, dw, preferred_element_type=jnp.float32)
    acc_b[...] += lax.dot_general(
        back_gate, gw, nt, preferred_element_type=jnp.float32
    ) + lax.dot_general(back_up, uw, nt, preferred_element_type=jnp.float32)

    @pl.when(j == pl.num_programs(0) - 1)
    def _():
        fwd_ref[...] = acc_o[...].astype(fwd_ref.dtype)
        bwd_ref[...] = acc_b[...].astype(bwd_ref.dtype)


def expert_pair(first, arrived, partner, gw, uw, dw):
    rows, feat = arrived.shape
    hid = gw.shape[1]
    hb = min(hid, 256)
    full = pl.BlockSpec((rows, feat), lambda j, f: (0, 0))
    grid_spec = pltpu.PrefetchScalarGridSpec(
        num_scalar_prefetch=1,
        grid=(hid // hb,),
        in_specs=[
            full,
            full,
            pl.BlockSpec((feat, hb), lambda j, f: (0, j)),
            pl.BlockSpec((feat, hb), lambda j, f: (0, j)),
            pl.BlockSpec((hb, feat), lambda j, f: (j, 0)),
        ],
        out_specs=[full, full],
        scratch_shapes=[pltpu.VMEM((rows, feat), arrived.dtype)] * 2
        + [pltpu.VMEM((rows, feat), jnp.float32)] * 2,
    )
    return pl.pallas_call(
        _pair_kernel,
        grid_spec=grid_spec,
        out_shape=[jax.ShapeDtypeStruct((rows, feat), jnp.bfloat16)] * 2,
        compiler_params=pltpu.CompilerParams(
            dimension_semantics=("arbitrary",), vmem_limit_bytes=56 * 1024 * 1024
        ),
    )(first, arrived, partner, gw, uw, dw)


def apply_combine(combine, partial_sums):
    return jnp.dot(combine, partial_sums, precision=lax.Precision.HIGHEST)


def group_perm(expert_count, group_size, shift):
    return [
        (d, (d // group_size) * group_size + (d % group_size + shift) % group_size)
        for d in range(expert_count)
    ]


def group_gather(piece, member, expert_count, group_size):
    got = [piece]
    for shift in range(1, group_size):
        got.append(lax.ppermute(piece, "expert", group_perm(expert_count, group_size, shift)))
    stacked = jnp.stack(got)
    order = (member - jnp.arange(group_size, dtype=jnp.int32)) % group_size
    return jnp.take(stacked, order, axis=0)


def group_reduce_scatter(pieces, member, expert_count, group_size, axis):
    total = lax.dynamic_index_in_dim(pieces, member, axis, keepdims=False).astype(jnp.float32)
    for shift in range(1, group_size):
        target = (member + shift) % group_size
        part = lax.dynamic_index_in_dim(pieces, target, axis, keepdims=False)
        moved = lax.ppermute(part, "expert", group_perm(expert_count, group_size, shift))
        total = total + moved.astype(jnp.float32)
    return total


def butterfly_sum(value, steps):
    done = {}
    for axis, limit in steps:
        size = lax.axis_size(axis)
        if size & (size - 1):
            if axis not in done:
                value = lax.psum(value, axis)
                done[axis] = size
            continue
        bit = done.get(axis, 1)
        while bit < size and (limit is None or bit < 2 * limit):
            value = value + lax.ppermute(value, axis, [(i, i ^ bit) for i in range(size)])
            bit *= 2
        done[axis] = bit
    return value


def by_features(
    normed, out_grad, slot_table, filled, gate_weight, up_weight, down_weight,
    member, expert_count, group_size,
):
    flight, capacity = slot_table.shape
    feature_count = normed.shape[1]
    piece = feature_count // group_size
    packed = jnp.stack(
        [dispatch_rows(normed, slot_table, filled), dispatch_rows(out_grad, slot_table, filled)],
        axis=1,
    )
    sending = (
        packed.reshape(flight, 2, capacity, group_size, piece)
        .transpose(0, 3, 1, 2, 4)
        .reshape(expert_count, 2, capacity, piece)
    )
    arrived = lax.all_to_all(sending, "expert", split_axis=0, concat_axis=0, tiled=True)
    whole = group_gather(arrived, member, expert_count, group_size)
    rows = whole.transpose(1, 2, 3, 0, 4).reshape(expert_count, 2, capacity, feature_count)
    local_rows = rows[:, 0].reshape(expert_count * capacity, feature_count)
    local_grads = rows[:, 1].reshape(expert_count * capacity, feature_count)
    forward, backward = expert_share(local_rows, local_grads, gate_weight, up_weight, down_weight)
    both = jnp.stack(
        [
            forward.reshape(expert_count, capacity, feature_count),
            backward.reshape(expert_count, capacity, feature_count),
        ],
        axis=1,
    ).reshape(expert_count, 2, capacity, group_size, piece)
    summed = group_reduce_scatter(both, member, expert_count, group_size, 3)
    came = lax.all_to_all(
        summed.astype(jnp.bfloat16), "expert", split_axis=0, concat_axis=0, tiled=True
    )
    sums = (
        came.reshape(flight, group_size, 2, capacity, piece)
        .transpose(0, 2, 3, 1, 4)
        .reshape(flight, 2, capacity * feature_count)
        .astype(jnp.float32)
    )
    out_sums = sums[:, 0].reshape(flight * capacity, feature_count)
    grad_sums = sums[:, 1].reshape(flight * capacity, feature_count)
    return out_sums, grad_sums


def exchange(chunks, axis):
    size = lax.axis_size(axis)
    me = lax.axis_index(axis)
    moved = [lax.dynamic_index_in_dim(chunks, me, 0, keepdims=False)]
    for shift in range(1, size):
        part = lax.dynamic_index_in_dim(chunks, (me + shift) % size, 0, keepdims=False)
        moved.append(lax.ppermute(part, axis, [(i, (i + shift) % size) for i in range(size)]))
    stacked = jnp.stack(moved)
    order = (me - jnp.arange(size, dtype=jnp.int32)) % size
    return jnp.take(stacked, order, axis=0)


def pick_rows(values, slot_table, filled):
    token_range = jnp.arange(values.shape[0], dtype=jnp.int32)
    onehot = (slot_table[:, :, None] == token_range[None, None, :]) & filled[:, :, None]
    picked = jnp.einsum(
        "fct,td->fcd", onehot.astype(values.dtype), values, preferred_element_type=jnp.float32
    )
    return picked.astype(values.dtype)


def exchange_relative(chunks, first):
    size = lax.axis_size("expert")
    me = lax.axis_index("expert")
    moved = [lax.dynamic_index_in_dim(chunks, me, 0, keepdims=False)]
    for shift in range(1, size):
        part = lax.dynamic_index_in_dim(chunks, (me + shift) % size, 0, keepdims=False)
        moved.append(lax.ppermute(part, "expert", [(i, (i + shift) % size) for i in range(size)]))
    return jnp.where(first, jnp.stack(moved), jnp.stack(moved[1:] + moved[:1]))


def by_parity(chunks, odd, flight, group_size):
    size = lax.axis_size("expert")
    me = lax.axis_index("expert")
    moved = []
    for shift in range(odd, size, group_size):
        block = (size - me % group_size - shift) % size
        part = lax.dynamic_index_in_dim(chunks, block, 0, keepdims=False)
        if shift == 0:
            moved.append(part)
        else:
            moved.append(lax.ppermute(part, "expert", [(i, (i + shift) % size) for i in range(size)]))
    stacked = jnp.stack(moved)
    chip = me // group_size
    order = (chip + odd * (me % group_size - 1) - jnp.arange(flight, dtype=jnp.int32)) % flight
    return stacked.reshape(flight * chunks.shape[1], chunks.shape[2]), order


def by_pair(
    normed, out_grad, slot_table, filled, gate_weight, up_weight, down_weight,
    member, expert_count, group_size,
):
    flight, capacity = slot_table.shape
    feature_count = normed.shape[1]
    picked = (pick_rows(normed, slot_table, filled), pick_rows(out_grad, slot_table, filled))
    me = lax.axis_index("expert")
    own = []
    for shift in range(expert_count):
        expert = ((me + shift) % expert_count) // group_size
        part = lax.dynamic_index_in_dim(picked[shift % 2], expert, 0, keepdims=False)
        if shift:
            pairs = [(i, (i + shift) % expert_count) for i in range(expert_count)]
            part = lax.ppermute(part, "expert", pairs)
        own.append(part)
    own = jnp.stack(own)
    swap = group_perm(expert_count, group_size, 1)
    partner = lax.ppermute(own, "expert", swap)
    first = member == 0
    even = jnp.where(first, own, partner)
    odd = jnp.where(first, partner, own)
    blocks = range(0, expert_count, 2)
    rows_x = jnp.stack(sum([[even[k], odd[(k + 2) % expert_count]] for k in blocks], []))
    rows_y = jnp.stack(sum([[odd[k + 1], even[k + 1]] for k in blocks], []))
    forward, backward = expert_pair(
        jnp.ones((1,), jnp.int32),
        rows_x.reshape(expert_count * capacity, feature_count),
        rows_y.reshape(expert_count * capacity, feature_count),
        gate_weight,
        up_weight,
        down_weight,
    )
    shape = (expert_count, capacity, feature_count)
    grad_total = backward.astype(jnp.float32) + lax.ppermute(backward, "expert", swap).astype(
        jnp.float32
    )
    grad_sums, grad_order = by_parity(
        grad_total.astype(jnp.bfloat16).reshape(shape), 0, flight, group_size
    )
    out_total = forward.astype(jnp.float32) + lax.ppermute(forward, "expert", swap).astype(
        jnp.float32
    )
    out_sums, out_order = by_parity(
        out_total.astype(jnp.bfloat16).reshape(shape), 1, flight, group_size
    )
    return out_sums.astype(jnp.float32), grad_sums.astype(jnp.float32), out_order, grad_order


def shards(
    tokens,
    steering,
    norm_gain,
    route_ids,
    route_gates,
    gate_weight,
    up_weight,
    down_weight,
    out_grad,
):
    expert_count = lax.axis_size("expert")
    flight = EXP_FLIGHT
    group_size = expert_count // flight
    capacity = CAP
    feature_count = tokens.shape[1]
    piece = feature_count // group_size
    member = lax.axis_index("expert") % group_size
    residual, inverse, normed = normalize(tokens, steering, norm_gain)
    slot_table, filled, combine = slot_tables(route_ids, route_gates, flight, capacity)
    out_combine = combine
    grad_combine = combine
    if group_size == 2:
        out_sums, grad_sums, out_order, grad_order = by_pair(
            normed, out_grad, slot_table, filled, gate_weight, up_weight, down_weight,
            member, expert_count, group_size,
        )
        by_expert = combine.reshape(combine.shape[0], flight, capacity)
        out_combine = jnp.take(by_expert, out_order, axis=1).reshape(combine.shape)
        grad_combine = jnp.take(by_expert, grad_order, axis=1).reshape(combine.shape)
    else:
        out_sums, grad_sums = by_features(
            normed, out_grad, slot_table, filled, gate_weight, up_weight, down_weight,
            member, expert_count, group_size,
        )
    mixture = apply_combine(out_combine, out_sums)
    back_normed = apply_combine(grad_combine, grad_sums)
    layer_out = (residual + mixture).astype(jnp.bfloat16)
    total_grad = norm_backward(residual, inverse, norm_gain, back_normed, out_grad)
    steer_grad = butterfly_sum(
        jnp.sum(total_grad, axis=0), (("expert", 1), ("dp", None), ("expert", None))
    )
    return (layer_out, total_grad.astype(jnp.bfloat16), steer_grad)


def solution(mesh):
    in_specs = (
        P(("dp", "expert"), None),
        P(),
        P(),
        P(("dp", "expert"), None),
        P(("dp", "expert"), None),
        P(None, "expert"),
        P(None, "expert"),
        P("expert", None),
        P(("dp", "expert"), None),
    )
    out_specs = (P(("dp", "expert"), None), P(("dp", "expert"), None), P())
    return jax.shard_map(shards, mesh=mesh, in_specs=in_specs, out_specs=out_specs, check_vma=False)
```

```python
import jax
import jax.numpy as jnp
from jax import lax
from jax.sharding import PartitionSpec as P
from jax.experimental import pallas as pl
from jax.experimental.pallas import tpu as pltpu

EXP_FLIGHT = 4
CAP = 8


EPSILON = 1e-06
GATE_UNIT = 1.0 / 65536.0


def slot_tables(route_ids, route_gates, flight, capacity):
    count_rows = route_ids.shape[0]
    expert_range = jnp.arange(flight, dtype=jnp.int32)
    hit_mask = route_ids[:, :, None] == expert_range[None, None, :]
    member = jnp.any(hit_mask, axis=1)
    scaled = route_gates.astype(jnp.float32) * GATE_UNIT
    weights = jnp.sum(jnp.where(hit_mask, scaled[:, :, None], 0.0), axis=1)
    position = jnp.cumsum(member.astype(jnp.int32), axis=0) - 1
    slot_of = jnp.where(member, position, capacity)
    slot_range = jnp.arange(capacity, dtype=jnp.int32)
    matches = slot_of[:, :, None] == slot_range[None, None, :]
    row_range = jnp.arange(count_rows, dtype=jnp.int32)
    slot_table = jnp.sum(jnp.where(matches, row_range[:, None, None], 0), axis=0)
    filled = jnp.any(matches, axis=0)
    combine = jnp.where(matches, weights[:, :, None], 0.0).reshape(count_rows, flight * capacity)
    return (slot_table, filled, combine)


def dispatch_rows(values, slot_table, filled):
    picked = values[slot_table]
    return jnp.where(filled[:, :, None], picked, jnp.zeros((), values.dtype))


def normalize(tokens, steering, norm_gain):
    residual = tokens.astype(jnp.float32) + steering
    inverse = lax.rsqrt(jnp.mean(residual * residual, axis=-1, keepdims=True) + EPSILON)
    normed = (residual * inverse * norm_gain).astype(jnp.bfloat16)
    return (residual, inverse, normed)


def norm_backward(residual, inverse, norm_gain, back_normed, out_grad):
    scaled = back_normed * norm_gain
    inner_mean = jnp.mean(scaled * residual, axis=-1, keepdims=True)
    cubed = inverse * inverse * inverse
    return out_grad.astype(jnp.float32) + inverse * scaled - residual * cubed * inner_mean


def share_forward(token_rows, gate_cols, up_cols, down_rows):
    gate_pre = jnp.dot(token_rows, gate_cols, preferred_element_type=jnp.float32)
    up_pre = jnp.dot(token_rows, up_cols, preferred_element_type=jnp.float32)
    hidden = (jax.nn.silu(gate_pre) * up_pre).astype(jnp.bfloat16)
    forward = jnp.dot(hidden, down_rows, preferred_element_type=jnp.float32).astype(jnp.bfloat16)
    return (forward, gate_pre, up_pre)


def share_backward(grad_rows, gate_pre, up_pre, gate_cols, up_cols, down_rows):
    contract = (((1,), (1,)), ((), ()))
    back_hidden = lax.dot_general(
        grad_rows, down_rows, contract, preferred_element_type=jnp.float32
    )
    sigmoid = jax.nn.sigmoid(gate_pre)
    back_up = (back_hidden * gate_pre * sigmoid).astype(jnp.bfloat16)
    back_gate = (back_hidden * up_pre * sigmoid * (1.0 + gate_pre * (1.0 - sigmoid))).astype(
        jnp.bfloat16
    )
    backward = lax.dot_general(back_gate, gate_cols, contract, preferred_element_type=jnp.float32)
    backward = backward + lax.dot_general(
        back_up, up_cols, contract, preferred_element_type=jnp.float32
    )
    return backward.astype(jnp.bfloat16)


def _expert_kernel(x_ref, y_ref, g_ref, u_ref, d_ref, out_ref, back_ref, acc_o, acc_b):
    j = pl.program_id(1)
    @pl.when(j == 0)
    def _():
        acc_o[...] = jnp.zeros_like(acc_o)
        acc_b[...] = jnp.zeros_like(acc_b)
    x = x_ref[...]
    y = y_ref[...]
    gw = g_ref[...]
    uw = u_ref[...]
    dw = d_ref[...]
    nt = (((1,), (1,)), ((), ()))
    g = jnp.dot(x, gw, preferred_element_type=jnp.float32)
    u = jnp.dot(x, uw, preferred_element_type=jnp.float32)
    sig = jax.nn.sigmoid(g)
    hidden = (g * sig * u).astype(jnp.bfloat16)
    bh = lax.dot_general(y, dw, nt, preferred_element_type=jnp.float32)
    back_up = (bh * g * sig).astype(jnp.bfloat16)
    back_gate = (bh * u * sig * (1.0 + g * (1.0 - sig))).astype(jnp.bfloat16)
    acc_o[...] += jnp.dot(hidden, dw, preferred_element_type=jnp.float32)
    acc_b[...] += (lax.dot_general(back_gate, gw, nt, preferred_element_type=jnp.float32)
                   + lax.dot_general(back_up, uw, nt, preferred_element_type=jnp.float32))
    @pl.when(j == pl.num_programs(1) - 1)
    def _():
        out_ref[...] = acc_o[...].astype(out_ref.dtype)
        back_ref[...] = acc_b[...].astype(back_ref.dtype)

def expert_share(x, y, gw, uw, dw):
    rows, feat = x.shape
    hid = gw.shape[1]
    rb = min(rows, 128)
    hb = min(hid, 256)
    return pl.pallas_call(
        _expert_kernel,
        grid=(rows // rb, hid // hb),
        in_specs=[
            pl.BlockSpec((rb, feat), lambda i, j: (i, 0)),
            pl.BlockSpec((rb, feat), lambda i, j: (i, 0)),
            pl.BlockSpec((feat, hb), lambda i, j: (0, j)),
            pl.BlockSpec((feat, hb), lambda i, j: (0, j)),
            pl.BlockSpec((hb, feat), lambda i, j: (j, 0)),
        ],
        out_specs=[
            pl.BlockSpec((rb, feat), lambda i, j: (i, 0)),
            pl.BlockSpec((rb, feat), lambda i, j: (i, 0)),
        ],
        out_shape=[jax.ShapeDtypeStruct((rows, feat), jnp.bfloat16)] * 2,
        scratch_shapes=[pltpu.VMEM((rb, feat), jnp.float32)] * 2,
        compiler_params=pltpu.CompilerParams(
            dimension_semantics=("arbitrary", "arbitrary"), vmem_limit_bytes=56 * 1024 * 1024
        ),
    )(x, y, gw, uw, dw)


def _pair_kernel(
    first_ref, a_ref, p_ref, g_ref, u_ref, d_ref, fwd_ref, bwd_ref, xs, ys, acc_o, acc_b
):
    j = pl.program_id(0)
    first = first_ref[0] == 1

    @pl.when(j == 0)
    def _():
        xs[...] = jnp.where(first, a_ref[...], p_ref[...])
        ys[...] = jnp.where(first, p_ref[...], a_ref[...])
        acc_o[...] = jnp.zeros_like(acc_o)
        acc_b[...] = jnp.zeros_like(acc_b)

    x = xs[...]
    y = ys[...]
    gw = g_ref[...]
    uw = u_ref[...]
    dw = d_ref[...]
    nt = (((1,), (1,)), ((), ()))
    g = jnp.dot(x, gw, preferred_element_type=jnp.float32)
    u = jnp.dot(x, uw, preferred_element_type=jnp.float32)
    sig = jax.nn.sigmoid(g)
    hidden = (g * sig * u).astype(jnp.bfloat16)
    bh = lax.dot_general(y, dw, nt, preferred_element_type=jnp.float32)
    back_up = (bh * g * sig).astype(jnp.bfloat16)
    back_gate = (bh * u * sig * (1.0 + g * (1.0 - sig))).astype(jnp.bfloat16)
    acc_o[...] += jnp.dot(hidden, dw, preferred_element_type=jnp.float32)
    acc_b[...] += lax.dot_general(
        back_gate, gw, nt, preferred_element_type=jnp.float32
    ) + lax.dot_general(back_up, uw, nt, preferred_element_type=jnp.float32)

    @pl.when(j == pl.num_programs(0) - 1)
    def _():
        fwd_ref[...] = acc_o[...].astype(fwd_ref.dtype)
        bwd_ref[...] = acc_b[...].astype(bwd_ref.dtype)


def expert_pair(first, arrived, partner, gw, uw, dw):
    rows, feat = arrived.shape
    hid = gw.shape[1]
    hb = min(hid, 256)
    full = pl.BlockSpec((rows, feat), lambda j, f: (0, 0))
    grid_spec = pltpu.PrefetchScalarGridSpec(
        num_scalar_prefetch=1,
        grid=(hid // hb,),
        in_specs=[
            full,
            full,
            pl.BlockSpec((feat, hb), lambda j, f: (0, j)),
            pl.BlockSpec((feat, hb), lambda j, f: (0, j)),
            pl.BlockSpec((hb, feat), lambda j, f: (j, 0)),
        ],
        out_specs=[full, full],
        scratch_shapes=[pltpu.VMEM((rows, feat), arrived.dtype)] * 2
        + [pltpu.VMEM((rows, feat), jnp.float32)] * 2,
    )
    return pl.pallas_call(
        _pair_kernel,
        grid_spec=grid_spec,
        out_shape=[jax.ShapeDtypeStruct((rows, feat), jnp.bfloat16)] * 2,
        compiler_params=pltpu.CompilerParams(
            dimension_semantics=("arbitrary",), vmem_limit_bytes=56 * 1024 * 1024
        ),
    )(first, arrived, partner, gw, uw, dw)


def split_combine(combine, rows):
    high = combine.astype(jnp.bfloat16)
    rest = combine - high.astype(jnp.float32)
    mid = rest.astype(jnp.bfloat16)
    low = (rest - mid.astype(jnp.float32)).astype(jnp.bfloat16)
    total = jnp.dot(high, rows, preferred_element_type=jnp.float32)
    total = total + jnp.dot(mid, rows, preferred_element_type=jnp.float32)
    return total + jnp.dot(low, rows, preferred_element_type=jnp.float32)


def apply_combine(combine, partial_sums):
    return jnp.dot(combine, partial_sums, precision=lax.Precision.HIGHEST)


def group_perm(expert_count, group_size, shift):
    return [
        (d, (d // group_size) * group_size + (d % group_size + shift) % group_size)
        for d in range(expert_count)
    ]


def group_gather(piece, member, expert_count, group_size):
    got = [piece]
    for shift in range(1, group_size):
        got.append(lax.ppermute(piece, "expert", group_perm(expert_count, group_size, shift)))
    stacked = jnp.stack(got)
    order = (member - jnp.arange(group_size, dtype=jnp.int32)) % group_size
    return jnp.take(stacked, order, axis=0)


def group_reduce_scatter(pieces, member, expert_count, group_size, axis):
    total = lax.dynamic_index_in_dim(pieces, member, axis, keepdims=False).astype(jnp.float32)
    for shift in range(1, group_size):
        target = (member + shift) % group_size
        part = lax.dynamic_index_in_dim(pieces, target, axis, keepdims=False)
        moved = lax.ppermute(part, "expert", group_perm(expert_count, group_size, shift))
        total = total + moved.astype(jnp.float32)
    return total


def butterfly_sum(value, steps):
    done = {}
    for axis, limit in steps:
        size = lax.axis_size(axis)
        if size & (size - 1):
            if axis not in done:
                value = lax.psum(value, axis)
                done[axis] = size
            continue
        bit = done.get(axis, 1)
        while bit < size and (limit is None or bit < 2 * limit):
            value = value + lax.ppermute(value, axis, [(i, i ^ bit) for i in range(size)])
            bit *= 2
        done[axis] = bit
    return value


def by_features(
    normed, out_grad, slot_table, filled, gate_weight, up_weight, down_weight,
    member, expert_count, group_size,
):
    flight, capacity = slot_table.shape
    feature_count = normed.shape[1]
    piece = feature_count // group_size
    packed = jnp.stack(
        [dispatch_rows(normed, slot_table, filled), dispatch_rows(out_grad, slot_table, filled)],
        axis=1,
    )
    sending = (
        packed.reshape(flight, 2, capacity, group_size, piece)
        .transpose(0, 3, 1, 2, 4)
        .reshape(expert_count, 2, capacity, piece)
    )
    arrived = lax.all_to_all(sending, "expert", split_axis=0, concat_axis=0, tiled=True)
    whole = group_gather(arrived, member, expert_count, group_size)
    rows = whole.transpose(1, 2, 3, 0, 4).reshape(expert_count, 2, capacity, feature_count)
    local_rows = rows[:, 0].reshape(expert_count * capacity, feature_count)
    local_grads = rows[:, 1].reshape(expert_count * capacity, feature_count)
    forward, backward = expert_share(local_rows, local_grads, gate_weight, up_weight, down_weight)
    both = jnp.stack(
        [
            forward.reshape(expert_count, capacity, feature_count),
            backward.reshape(expert_count, capacity, feature_count),
        ],
        axis=1,
    ).reshape(expert_count, 2, capacity, group_size, piece)
    summed = group_reduce_scatter(both, member, expert_count, group_size, 3)
    came = lax.all_to_all(
        summed.astype(jnp.bfloat16), "expert", split_axis=0, concat_axis=0, tiled=True
    )
    sums = (
        came.reshape(flight, group_size, 2, capacity, piece)
        .transpose(0, 2, 3, 1, 4)
        .reshape(flight, 2, capacity * feature_count)
        .astype(jnp.float32)
    )
    out_sums = sums[:, 0].reshape(flight * capacity, feature_count)
    grad_sums = sums[:, 1].reshape(flight * capacity, feature_count)
    return out_sums, grad_sums


def exchange(chunks, axis):
    size = lax.axis_size(axis)
    me = lax.axis_index(axis)
    moved = [lax.dynamic_index_in_dim(chunks, me, 0, keepdims=False)]
    for shift in range(1, size):
        part = lax.dynamic_index_in_dim(chunks, (me + shift) % size, 0, keepdims=False)
        moved.append(lax.ppermute(part, axis, [(i, (i + shift) % size) for i in range(size)]))
    stacked = jnp.stack(moved)
    order = (me - jnp.arange(size, dtype=jnp.int32)) % size
    return jnp.take(stacked, order, axis=0)


def pick_rows(values, slot_table, filled):
    token_range = jnp.arange(values.shape[0], dtype=jnp.int32)
    onehot = (slot_table[:, :, None] == token_range[None, None, :]) & filled[:, :, None]
    picked = jnp.einsum(
        "fct,td->fcd", onehot.astype(values.dtype), values, preferred_element_type=jnp.float32
    )
    return picked.astype(values.dtype)


def exchange_relative(chunks, first):
    size = lax.axis_size("expert")
    me = lax.axis_index("expert")
    moved = [lax.dynamic_index_in_dim(chunks, me, 0, keepdims=False)]
    for shift in range(1, size):
        part = lax.dynamic_index_in_dim(chunks, (me + shift) % size, 0, keepdims=False)
        moved.append(lax.ppermute(part, "expert", [(i, (i + shift) % size) for i in range(size)]))
    return jnp.where(first, jnp.stack(moved), jnp.stack(moved[1:] + moved[:1]))


def by_parity(chunks, odd, flight, group_size):
    size = lax.axis_size("expert")
    me = lax.axis_index("expert")
    moved = []
    for shift in range(odd, size, group_size):
        block = (size - me % group_size - shift) % size
        part = lax.dynamic_index_in_dim(chunks, block, 0, keepdims=False)
        if shift == 0:
            moved.append(part)
        else:
            moved.append(lax.ppermute(part, "expert", [(i, (i + shift) % size) for i in range(size)]))
    stacked = jnp.stack(moved)
    chip = me // group_size
    order = (chip + odd * (me % group_size - 1) - jnp.arange(flight, dtype=jnp.int32)) % flight
    return stacked.reshape(flight * chunks.shape[1], chunks.shape[2]), order


def by_pair(
    normed, out_grad, slot_table, filled, gate_weight, up_weight, down_weight,
    member, expert_count, group_size,
):
    flight, capacity = slot_table.shape
    feature_count = normed.shape[1]
    picked = (pick_rows(normed, slot_table, filled), pick_rows(out_grad, slot_table, filled))
    me = lax.axis_index("expert")
    own = []
    for shift in range(expert_count):
        expert = ((me + shift) % expert_count) // group_size
        part = lax.dynamic_index_in_dim(picked[shift % 2], expert, 0, keepdims=False)
        if shift:
            pairs = [(i, (i + shift) % expert_count) for i in range(expert_count)]
            part = lax.ppermute(part, "expert", pairs)
        own.append(part)
    own = jnp.stack(own)
    swap = group_perm(expert_count, group_size, 1)
    partner = lax.ppermute(own, "expert", swap)
    first = member == 0
    even = jnp.where(first, own, partner)
    odd = jnp.where(first, partner, own)
    blocks = range(0, expert_count, 2)
    rows_x = jnp.stack(sum([[even[k], odd[(k + 2) % expert_count]] for k in blocks], []))
    rows_y = jnp.stack(sum([[odd[k + 1], even[k + 1]] for k in blocks], []))
    forward, backward = expert_pair(
        jnp.ones((1,), jnp.int32),
        rows_x.reshape(expert_count * capacity, feature_count),
        rows_y.reshape(expert_count * capacity, feature_count),
        gate_weight,
        up_weight,
        down_weight,
    )
    shape = (expert_count, capacity, feature_count)
    grad_total = backward.astype(jnp.float32) + lax.ppermute(backward, "expert", swap).astype(
        jnp.float32
    )
    grad_sums, grad_order = by_parity(
        grad_total.astype(jnp.bfloat16).reshape(shape), 0, flight, group_size
    )
    out_total = forward.astype(jnp.float32) + lax.ppermute(forward, "expert", swap).astype(
        jnp.float32
    )
    out_sums, out_order = by_parity(
        out_total.astype(jnp.bfloat16).reshape(shape), 1, flight, group_size
    )
    return out_sums, grad_sums, out_order, grad_order


def shards(
    tokens,
    steering,
    norm_gain,
    route_ids,
    route_gates,
    gate_weight,
    up_weight,
    down_weight,
    out_grad,
):
    expert_count = lax.axis_size("expert")
    flight = EXP_FLIGHT
    group_size = expert_count // flight
    capacity = CAP
    feature_count = tokens.shape[1]
    piece = feature_count // group_size
    member = lax.axis_index("expert") % group_size
    residual, inverse, normed = normalize(tokens, steering, norm_gain)
    slot_table, filled, combine = slot_tables(route_ids, route_gates, flight, capacity)
    out_combine = combine
    grad_combine = combine
    if group_size == 2:
        out_sums, grad_sums, out_order, grad_order = by_pair(
            normed, out_grad, slot_table, filled, gate_weight, up_weight, down_weight,
            member, expert_count, group_size,
        )
        by_expert = combine.reshape(combine.shape[0], flight, capacity)
        out_combine = jnp.take(by_expert, out_order, axis=1).reshape(combine.shape)
        grad_combine = jnp.take(by_expert, grad_order, axis=1).reshape(combine.shape)
        mixture = split_combine(out_combine, out_sums)
        back_normed = split_combine(grad_combine, grad_sums)
    else:
        out_sums, grad_sums = by_features(
            normed, out_grad, slot_table, filled, gate_weight, up_weight, down_weight,
            member, expert_count, group_size,
        )
        mixture = apply_combine(out_combine, out_sums)
        back_normed = apply_combine(grad_combine, grad_sums)
    layer_out = (residual + mixture).astype(jnp.bfloat16)
    total_grad = norm_backward(residual, inverse, norm_gain, back_normed, out_grad)
    steer_grad = butterfly_sum(
        jnp.sum(total_grad, axis=0), (("expert", 1), ("dp", None), ("expert", None))
    )
    return (layer_out, total_grad.astype(jnp.bfloat16), steer_grad)


def solution(mesh):
    in_specs = (
        P(("dp", "expert"), None),
        P(),
        P(),
        P(("dp", "expert"), None),
        P(("dp", "expert"), None),
        P(None, "expert"),
        P(None, "expert"),
        P("expert", None),
        P(("dp", "expert"), None),
    )
    out_specs = (P(("dp", "expert"), None), P(("dp", "expert"), None), P())
    return jax.shard_map(shards, mesh=mesh, in_specs=in_specs, out_specs=out_specs, check_vma=False)
```

```python
import jax
import jax.numpy as jnp
from jax import lax
from jax.sharding import PartitionSpec as P
from jax.experimental import pallas as pl
from jax.experimental.pallas import tpu as pltpu


EXP_FLIGHT = 4
CAP = 8


EPSILON = 1e-06
GATE_UNIT = 1.0 / 65536.0


def slot_tables(route_ids, route_gates, flight, capacity):
    count_rows = route_ids.shape[0]
    expert_range = jnp.arange(flight, dtype=jnp.int32)
    hit_mask = route_ids[:, :, None] == expert_range[None, None, :]
    member = jnp.any(hit_mask, axis=1)
    scaled = route_gates.astype(jnp.float32) * GATE_UNIT
    weights = jnp.sum(jnp.where(hit_mask, scaled[:, :, None], 0.0), axis=1)
    position = jnp.cumsum(member.astype(jnp.int32), axis=0) - 1
    slot_of = jnp.where(member, position, capacity)
    slot_range = jnp.arange(capacity, dtype=jnp.int32)
    matches = slot_of[:, :, None] == slot_range[None, None, :]
    row_range = jnp.arange(count_rows, dtype=jnp.int32)
    slot_table = jnp.sum(jnp.where(matches, row_range[:, None, None], 0), axis=0)
    filled = jnp.any(matches, axis=0)
    combine = jnp.where(matches, weights[:, :, None], 0.0).reshape(count_rows, flight * capacity)
    return (slot_table, filled, combine)


def dispatch_rows(values, slot_table, filled):
    picked = values[slot_table]
    return jnp.where(filled[:, :, None], picked, jnp.zeros((), values.dtype))


def normalize(tokens, steering, norm_gain):
    residual = tokens.astype(jnp.float32) + steering
    inverse = lax.rsqrt(jnp.mean(residual * residual, axis=-1, keepdims=True) + EPSILON)
    normed = (residual * inverse * norm_gain).astype(jnp.bfloat16)
    return (residual, inverse, normed)


def norm_backward(residual, inverse, norm_gain, back_normed, out_grad):
    scaled = back_normed * norm_gain
    inner_mean = jnp.mean(scaled * residual, axis=-1, keepdims=True)
    cubed = inverse * inverse * inverse
    return out_grad.astype(jnp.float32) + inverse * scaled - residual * cubed * inner_mean


def share_forward(token_rows, gate_cols, up_cols, down_rows):
    gate_pre = jnp.dot(token_rows, gate_cols, preferred_element_type=jnp.float32)
    up_pre = jnp.dot(token_rows, up_cols, preferred_element_type=jnp.float32)
    hidden = (jax.nn.silu(gate_pre) * up_pre).astype(jnp.bfloat16)
    forward = jnp.dot(hidden, down_rows, preferred_element_type=jnp.float32).astype(jnp.bfloat16)
    return (forward, gate_pre, up_pre)


def share_backward(grad_rows, gate_pre, up_pre, gate_cols, up_cols, down_rows):
    contract = (((1,), (1,)), ((), ()))
    back_hidden = lax.dot_general(
        grad_rows, down_rows, contract, preferred_element_type=jnp.float32
    )
    sigmoid = jax.nn.sigmoid(gate_pre)
    back_up = (back_hidden * gate_pre * sigmoid).astype(jnp.bfloat16)
    back_gate = (back_hidden * up_pre * sigmoid * (1.0 + gate_pre * (1.0 - sigmoid))).astype(
        jnp.bfloat16
    )
    backward = lax.dot_general(back_gate, gate_cols, contract, preferred_element_type=jnp.float32)
    backward = backward + lax.dot_general(
        back_up, up_cols, contract, preferred_element_type=jnp.float32
    )
    return backward.astype(jnp.bfloat16)


def _expert_kernel(x_ref, y_ref, g_ref, u_ref, d_ref, out_ref, back_ref, acc_o, acc_b):
    j = pl.program_id(1)
    @pl.when(j == 0)
    def _():
        acc_o[...] = jnp.zeros_like(acc_o)
        acc_b[...] = jnp.zeros_like(acc_b)
    x = x_ref[...]
    y = y_ref[...]
    gw = g_ref[...]
    uw = u_ref[...]
    dw = d_ref[...]
    nt = (((1,), (1,)), ((), ()))
    g = jnp.dot(x, gw, preferred_element_type=jnp.float32)
    u = jnp.dot(x, uw, preferred_element_type=jnp.float32)
    sig = jax.nn.sigmoid(g)
    hidden = (g * sig * u).astype(jnp.bfloat16)
    bh = lax.dot_general(y, dw, nt, preferred_element_type=jnp.float32)
    back_up = (bh * g * sig).astype(jnp.bfloat16)
    back_gate = (bh * u * sig * (1.0 + g * (1.0 - sig))).astype(jnp.bfloat16)
    acc_o[...] += jnp.dot(hidden, dw, preferred_element_type=jnp.float32)
    acc_b[...] += (lax.dot_general(back_gate, gw, nt, preferred_element_type=jnp.float32)
                   + lax.dot_general(back_up, uw, nt, preferred_element_type=jnp.float32))
    @pl.when(j == pl.num_programs(1) - 1)
    def _():
        out_ref[...] = acc_o[...].astype(out_ref.dtype)
        back_ref[...] = acc_b[...].astype(back_ref.dtype)

def expert_share(x, y, gw, uw, dw):
    rows, feat = x.shape
    hid = gw.shape[1]
    rb = min(rows, 128)
    hb = min(hid, 256)
    return pl.pallas_call(
        _expert_kernel,
        grid=(rows // rb, hid // hb),
        in_specs=[
            pl.BlockSpec((rb, feat), lambda i, j: (i, 0)),
            pl.BlockSpec((rb, feat), lambda i, j: (i, 0)),
            pl.BlockSpec((feat, hb), lambda i, j: (0, j)),
            pl.BlockSpec((feat, hb), lambda i, j: (0, j)),
            pl.BlockSpec((hb, feat), lambda i, j: (j, 0)),
        ],
        out_specs=[
            pl.BlockSpec((rb, feat), lambda i, j: (i, 0)),
            pl.BlockSpec((rb, feat), lambda i, j: (i, 0)),
        ],
        out_shape=[jax.ShapeDtypeStruct((rows, feat), jnp.bfloat16)] * 2,
        scratch_shapes=[pltpu.VMEM((rb, feat), jnp.float32)] * 2,
        compiler_params=pltpu.CompilerParams(
            dimension_semantics=("arbitrary", "arbitrary"), vmem_limit_bytes=56 * 1024 * 1024
        ),
    )(x, y, gw, uw, dw)


def _pair_kernel(
    first_ref, a_ref, p_ref, g_ref, u_ref, d_ref, fwd_ref, bwd_ref, xs, ys, acc_o, acc_b
):
    j = pl.program_id(0)
    first = first_ref[0] == 1

    @pl.when(j == 0)
    def _():
        xs[...] = jnp.where(first, a_ref[...], p_ref[...])
        ys[...] = jnp.where(first, p_ref[...], a_ref[...])
        acc_o[...] = jnp.zeros_like(acc_o)
        acc_b[...] = jnp.zeros_like(acc_b)

    x = xs[...]
    y = ys[...]
    gw = g_ref[...]
    uw = u_ref[...]
    dw = d_ref[...]
    nt = (((1,), (1,)), ((), ()))
    g = jnp.dot(x, gw, preferred_element_type=jnp.float32)
    u = jnp.dot(x, uw, preferred_element_type=jnp.float32)
    sig = jax.nn.sigmoid(g)
    hidden = (g * sig * u).astype(jnp.bfloat16)
    bh = lax.dot_general(y, dw, nt, preferred_element_type=jnp.float32)
    back_up = (bh * g * sig).astype(jnp.bfloat16)
    back_gate = (bh * u * sig * (1.0 + g * (1.0 - sig))).astype(jnp.bfloat16)
    acc_o[...] += jnp.dot(hidden, dw, preferred_element_type=jnp.float32)
    acc_b[...] += lax.dot_general(
        back_gate, gw, nt, preferred_element_type=jnp.float32
    ) + lax.dot_general(back_up, uw, nt, preferred_element_type=jnp.float32)

    @pl.when(j == pl.num_programs(0) - 1)
    def _():
        fwd_ref[...] = acc_o[...].astype(fwd_ref.dtype)
        bwd_ref[...] = acc_b[...].astype(bwd_ref.dtype)


def expert_pair(first, arrived, partner, gw, uw, dw):
    rows, feat = arrived.shape
    hid = gw.shape[1]
    hb = min(hid, 256)
    full = pl.BlockSpec((rows, feat), lambda j, f: (0, 0))
    grid_spec = pltpu.PrefetchScalarGridSpec(
        num_scalar_prefetch=1,
        grid=(hid // hb,),
        in_specs=[
            full,
            full,
            pl.BlockSpec((feat, hb), lambda j, f: (0, j)),
            pl.BlockSpec((feat, hb), lambda j, f: (0, j)),
            pl.BlockSpec((hb, feat), lambda j, f: (j, 0)),
        ],
        out_specs=[full, full],
        scratch_shapes=[pltpu.VMEM((rows, feat), arrived.dtype)] * 2
        + [pltpu.VMEM((rows, feat), jnp.float32)] * 2,
    )
    return pl.pallas_call(
        _pair_kernel,
        grid_spec=grid_spec,
        out_shape=[jax.ShapeDtypeStruct((rows, feat), jnp.bfloat16)] * 2,
        compiler_params=pltpu.CompilerParams(
            dimension_semantics=("arbitrary",), vmem_limit_bytes=56 * 1024 * 1024
        ),
    )(first, arrived, partner, gw, uw, dw)


def apply_combine(combine, partial_sums):
    return jnp.dot(combine, partial_sums, precision=lax.Precision.HIGHEST)


def group_perm(expert_count, group_size, shift):
    return [
        (d, (d // group_size) * group_size + (d % group_size + shift) % group_size)
        for d in range(expert_count)
    ]


def group_gather(piece, member, expert_count, group_size):
    got = [piece]
    for shift in range(1, group_size):
        got.append(lax.ppermute(piece, "expert", group_perm(expert_count, group_size, shift)))
    stacked = jnp.stack(got)
    order = (member - jnp.arange(group_size, dtype=jnp.int32)) % group_size
    return jnp.take(stacked, order, axis=0)


def group_reduce_scatter(pieces, member, expert_count, group_size, axis):
    total = lax.dynamic_index_in_dim(pieces, member, axis, keepdims=False).astype(jnp.float32)
    for shift in range(1, group_size):
        target = (member + shift) % group_size
        part = lax.dynamic_index_in_dim(pieces, target, axis, keepdims=False)
        moved = lax.ppermute(part, "expert", group_perm(expert_count, group_size, shift))
        total = total + moved.astype(jnp.float32)
    return total


def butterfly_sum(value, steps):
    done = {}
    for axis, limit in steps:
        size = lax.axis_size(axis)
        if size & (size - 1):
            if axis not in done:
                value = lax.psum(value, axis)
                done[axis] = size
            continue
        bit = done.get(axis, 1)
        while bit < size and (limit is None or bit < 2 * limit):
            value = value + lax.ppermute(value, axis, [(i, i ^ bit) for i in range(size)])
            bit *= 2
        done[axis] = bit
    return value


def by_features(
    normed, out_grad, slot_table, filled, gate_weight, up_weight, down_weight,
    member, expert_count, group_size,
):
    flight, capacity = slot_table.shape
    feature_count = normed.shape[1]
    piece = feature_count // group_size
    packed = jnp.stack(
        [dispatch_rows(normed, slot_table, filled), dispatch_rows(out_grad, slot_table, filled)],
        axis=1,
    )
    sending = (
        packed.reshape(flight, 2, capacity, group_size, piece)
        .transpose(0, 3, 1, 2, 4)
        .reshape(expert_count, 2, capacity, piece)
    )
    arrived = lax.all_to_all(sending, "expert", split_axis=0, concat_axis=0, tiled=True)
    whole = group_gather(arrived, member, expert_count, group_size)
    rows = whole.transpose(1, 2, 3, 0, 4).reshape(expert_count, 2, capacity, feature_count)
    local_rows = rows[:, 0].reshape(expert_count * capacity, feature_count)
    local_grads = rows[:, 1].reshape(expert_count * capacity, feature_count)
    forward, backward = expert_share(local_rows, local_grads, gate_weight, up_weight, down_weight)
    both = jnp.stack(
        [
            forward.reshape(expert_count, capacity, feature_count),
            backward.reshape(expert_count, capacity, feature_count),
        ],
        axis=1,
    ).reshape(expert_count, 2, capacity, group_size, piece)
    summed = group_reduce_scatter(both, member, expert_count, group_size, 3)
    came = lax.all_to_all(
        summed.astype(jnp.bfloat16), "expert", split_axis=0, concat_axis=0, tiled=True
    )
    sums = (
        came.reshape(flight, group_size, 2, capacity, piece)
        .transpose(0, 2, 3, 1, 4)
        .reshape(flight, 2, capacity * feature_count)
        .astype(jnp.float32)
    )
    out_sums = sums[:, 0].reshape(flight * capacity, feature_count)
    grad_sums = sums[:, 1].reshape(flight * capacity, feature_count)
    return out_sums, grad_sums


def exchange(chunks, axis):
    size = lax.axis_size(axis)
    me = lax.axis_index(axis)
    moved = [lax.dynamic_index_in_dim(chunks, me, 0, keepdims=False)]
    for shift in range(1, size):
        part = lax.dynamic_index_in_dim(chunks, (me + shift) % size, 0, keepdims=False)
        moved.append(lax.ppermute(part, axis, [(i, (i + shift) % size) for i in range(size)]))
    stacked = jnp.stack(moved)
    order = (me - jnp.arange(size, dtype=jnp.int32)) % size
    return jnp.take(stacked, order, axis=0)


def pick_rows(values, slot_table, filled):
    token_range = jnp.arange(values.shape[0], dtype=jnp.int32)
    onehot = (slot_table[:, :, None] == token_range[None, None, :]) & filled[:, :, None]
    picked = jnp.einsum(
        "fct,td->fcd", onehot.astype(values.dtype), values, preferred_element_type=jnp.float32
    )
    return picked.astype(values.dtype)


def exchange_relative(chunks, first):
    size = lax.axis_size("expert")
    me = lax.axis_index("expert")
    moved = [lax.dynamic_index_in_dim(chunks, me, 0, keepdims=False)]
    for shift in range(1, size):
        part = lax.dynamic_index_in_dim(chunks, (me + shift) % size, 0, keepdims=False)
        moved.append(lax.ppermute(part, "expert", [(i, (i + shift) % size) for i in range(size)]))
    return jnp.where(first, jnp.stack(moved), jnp.stack(moved[1:] + moved[:1]))


def by_parity(chunks, odd, flight, group_size):
    size = lax.axis_size("expert")
    me = lax.axis_index("expert")
    moved = []
    for shift in range(odd, size, group_size):
        block = (size - me % group_size - shift) % size
        part = lax.dynamic_index_in_dim(chunks, block, 0, keepdims=False)
        if shift == 0:
            moved.append(part)
        else:
            moved.append(lax.ppermute(part, "expert", [(i, (i + shift) % size) for i in range(size)]))
    stacked = jnp.stack(moved)
    chip = me // group_size
    order = (chip + odd * (me % group_size - 1) - jnp.arange(flight, dtype=jnp.int32)) % flight
    return stacked.reshape(flight * chunks.shape[1], chunks.shape[2]), order


def by_pair(
    normed, out_grad, slot_table, filled, gate_weight, up_weight, down_weight,
    member, expert_count, group_size,
):
    flight, capacity = slot_table.shape
    feature_count = out_grad.shape[1]
    token_rows = pick_rows(normed[0], slot_table, filled).astype(jnp.float32) + normed[1]
    scale = jnp.take(normed[2][:, 0], slot_table, axis=0)[:, :, None]
    normed_rows = jnp.where(filled[:, :, None], token_rows * scale * normed[3], 0.0)
    picked = (normed_rows.astype(jnp.bfloat16), pick_rows(out_grad, slot_table, filled))
    me = lax.axis_index("expert")
    own = []
    for shift in range(expert_count):
        expert = ((me + shift) % expert_count) // group_size
        part = lax.dynamic_index_in_dim(picked[shift % 2], expert, 0, keepdims=False)
        if shift:
            pairs = [(i, (i + shift) % expert_count) for i in range(expert_count)]
            part = lax.ppermute(part, "expert", pairs)
        own.append(part)
    own = jnp.stack(own)
    swap = group_perm(expert_count, group_size, 1)
    partner = lax.ppermute(own, "expert", swap)
    first = member == 0
    even = jnp.where(first, own, partner)
    odd = jnp.where(first, partner, own)
    blocks = range(0, expert_count, 2)
    rows_x = jnp.stack(sum([[even[k], odd[(k + 2) % expert_count]] for k in blocks], []))
    rows_y = jnp.stack(sum([[odd[k + 1], even[k + 1]] for k in blocks], []))
    forward, backward = expert_pair(
        jnp.ones((1,), jnp.int32),
        rows_x.reshape(expert_count * capacity, feature_count),
        rows_y.reshape(expert_count * capacity, feature_count),
        gate_weight,
        up_weight,
        down_weight,
    )
    shape = (expert_count, capacity, feature_count)
    grad_total = backward.astype(jnp.float32) + lax.ppermute(backward, "expert", swap).astype(
        jnp.float32
    )
    grad_sums, grad_order = by_parity(
        grad_total.astype(jnp.bfloat16).reshape(shape), 0, flight, group_size
    )
    out_total = forward.astype(jnp.float32) + lax.ppermute(forward, "expert", swap).astype(
        jnp.float32
    )
    out_sums, out_order = by_parity(
        out_total.astype(jnp.bfloat16).reshape(shape), 1, flight, group_size
    )
    return out_sums.astype(jnp.float32), grad_sums.astype(jnp.float32), out_order, grad_order


def shards(
    tokens,
    steering,
    norm_gain,
    route_ids,
    route_gates,
    gate_weight,
    up_weight,
    down_weight,
    out_grad,
):
    expert_count = lax.axis_size("expert")
    flight = EXP_FLIGHT
    group_size = expert_count // flight
    capacity = CAP
    feature_count = tokens.shape[1]
    piece = feature_count // group_size
    member = lax.axis_index("expert") % group_size
    residual, inverse, normed = normalize(tokens, steering, norm_gain)
    slot_table, filled, combine = slot_tables(route_ids, route_gates, flight, capacity)
    out_combine = combine
    grad_combine = combine
    if group_size == 2:
        out_sums, grad_sums, out_order, grad_order = by_pair(
            (tokens, steering, inverse, norm_gain), out_grad, slot_table, filled, gate_weight, up_weight, down_weight,
            member, expert_count, group_size,
        )
        by_expert = combine.reshape(combine.shape[0], flight, capacity)
        out_combine = jnp.take(by_expert, out_order, axis=1).reshape(combine.shape)
        grad_combine = jnp.take(by_expert, grad_order, axis=1).reshape(combine.shape)
    else:
        out_sums, grad_sums = by_features(
            normed, out_grad, slot_table, filled, gate_weight, up_weight, down_weight,
            member, expert_count, group_size,
        )
    mixture = apply_combine(out_combine, out_sums)
    back_normed = apply_combine(grad_combine, grad_sums)
    layer_out = (residual + mixture).astype(jnp.bfloat16)
    total_grad = norm_backward(residual, inverse, norm_gain, back_normed, out_grad)
    steer_grad = butterfly_sum(
        jnp.sum(total_grad, axis=0), (("expert", 1), ("dp", None), ("expert", None))
    )
    return (layer_out, total_grad.astype(jnp.bfloat16), steer_grad)


def solution(mesh):
    in_specs = (
        P(("dp", "expert"), None),
        P(),
        P(),
        P(("dp", "expert"), None),
        P(("dp", "expert"), None),
        P(None, "expert"),
        P(None, "expert"),
        P("expert", None),
        P(("dp", "expert"), None),
    )
    out_specs = (P(("dp", "expert"), None), P(("dp", "expert"), None), P())
    return jax.shard_map(shards, mesh=mesh, in_specs=in_specs, out_specs=out_specs, check_vma=False)
```

```python
import jax
import jax.numpy as jnp
from jax import lax
from jax.sharding import PartitionSpec as P
from jax.experimental import pallas as pl
from jax.experimental.pallas import tpu as pltpu

EXP_FLIGHT = 4
CAP = 8


EPSILON = 1e-06
GATE_UNIT = 1.0 / 65536.0


def slot_tables(route_ids, route_gates, flight, capacity):
    count_rows = route_ids.shape[0]
    expert_range = jnp.arange(flight, dtype=jnp.int32)
    hit_mask = route_ids[:, :, None] == expert_range[None, None, :]
    member = jnp.any(hit_mask, axis=1)
    scaled = route_gates.astype(jnp.float32) * GATE_UNIT
    weights = jnp.sum(jnp.where(hit_mask, scaled[:, :, None], 0.0), axis=1)
    position = jnp.cumsum(member.astype(jnp.int32), axis=0) - 1
    slot_of = jnp.where(member, position, capacity)
    slot_range = jnp.arange(capacity, dtype=jnp.int32)
    matches = slot_of[:, :, None] == slot_range[None, None, :]
    row_range = jnp.arange(count_rows, dtype=jnp.int32)
    slot_table = jnp.sum(jnp.where(matches, row_range[:, None, None], 0), axis=0)
    filled = jnp.any(matches, axis=0)
    combine = jnp.where(matches, weights[:, :, None], 0.0).reshape(count_rows, flight * capacity)
    return (slot_table, filled, combine)


def dispatch_rows(values, slot_table, filled):
    picked = values[slot_table]
    return jnp.where(filled[:, :, None], picked, jnp.zeros((), values.dtype))


def normalize(tokens, steering, norm_gain):
    residual = tokens.astype(jnp.float32) + steering
    inverse = lax.rsqrt(jnp.mean(residual * residual, axis=-1, keepdims=True) + EPSILON)
    normed = (residual * inverse * norm_gain).astype(jnp.bfloat16)
    return (residual, inverse, normed)


def norm_backward(residual, inverse, norm_gain, back_normed, out_grad):
    scaled = back_normed * norm_gain
    inner_mean = jnp.mean(scaled * residual, axis=-1, keepdims=True)
    cubed = inverse * inverse * inverse
    return out_grad.astype(jnp.float32) + inverse * scaled - residual * cubed * inner_mean


def share_forward(token_rows, gate_cols, up_cols, down_rows):
    gate_pre = jnp.dot(token_rows, gate_cols, preferred_element_type=jnp.float32)
    up_pre = jnp.dot(token_rows, up_cols, preferred_element_type=jnp.float32)
    hidden = (jax.nn.silu(gate_pre) * up_pre).astype(jnp.bfloat16)
    forward = jnp.dot(hidden, down_rows, preferred_element_type=jnp.float32).astype(jnp.bfloat16)
    return (forward, gate_pre, up_pre)


def share_backward(grad_rows, gate_pre, up_pre, gate_cols, up_cols, down_rows):
    contract = (((1,), (1,)), ((), ()))
    back_hidden = lax.dot_general(
        grad_rows, down_rows, contract, preferred_element_type=jnp.float32
    )
    sigmoid = jax.nn.sigmoid(gate_pre)
    back_up = (back_hidden * gate_pre * sigmoid).astype(jnp.bfloat16)
    back_gate = (back_hidden * up_pre * sigmoid * (1.0 + gate_pre * (1.0 - sigmoid))).astype(
        jnp.bfloat16
    )
    backward = lax.dot_general(back_gate, gate_cols, contract, preferred_element_type=jnp.float32)
    backward = backward + lax.dot_general(
        back_up, up_cols, contract, preferred_element_type=jnp.float32
    )
    return backward.astype(jnp.bfloat16)


def _expert_kernel(x_ref, y_ref, g_ref, u_ref, d_ref, out_ref, back_ref, acc_o, acc_b):
    j = pl.program_id(1)
    @pl.when(j == 0)
    def _():
        acc_o[...] = jnp.zeros_like(acc_o)
        acc_b[...] = jnp.zeros_like(acc_b)
    x = x_ref[...]
    y = y_ref[...]
    gw = g_ref[...]
    uw = u_ref[...]
    dw = d_ref[...]
    nt = (((1,), (1,)), ((), ()))
    g = jnp.dot(x, gw, preferred_element_type=jnp.float32)
    u = jnp.dot(x, uw, preferred_element_type=jnp.float32)
    sig = jax.nn.sigmoid(g)
    hidden = (g * sig * u).astype(jnp.bfloat16)
    bh = lax.dot_general(y, dw, nt, preferred_element_type=jnp.float32)
    back_up = (bh * g * sig).astype(jnp.bfloat16)
    back_gate = (bh * u * sig * (1.0 + g * (1.0 - sig))).astype(jnp.bfloat16)
    acc_o[...] += jnp.dot(hidden, dw, preferred_element_type=jnp.float32)
    acc_b[...] += (lax.dot_general(back_gate, gw, nt, preferred_element_type=jnp.float32)
                   + lax.dot_general(back_up, uw, nt, preferred_element_type=jnp.float32))
    @pl.when(j == pl.num_programs(1) - 1)
    def _():
        out_ref[...] = acc_o[...].astype(out_ref.dtype)
        back_ref[...] = acc_b[...].astype(back_ref.dtype)

def expert_share(x, y, gw, uw, dw):
    rows, feat = x.shape
    hid = gw.shape[1]
    rb = min(rows, 128)
    hb = min(hid, 256)
    return pl.pallas_call(
        _expert_kernel,
        grid=(rows // rb, hid // hb),
        in_specs=[
            pl.BlockSpec((rb, feat), lambda i, j: (i, 0)),
            pl.BlockSpec((rb, feat), lambda i, j: (i, 0)),
            pl.BlockSpec((feat, hb), lambda i, j: (0, j)),
            pl.BlockSpec((feat, hb), lambda i, j: (0, j)),
            pl.BlockSpec((hb, feat), lambda i, j: (j, 0)),
        ],
        out_specs=[
            pl.BlockSpec((rb, feat), lambda i, j: (i, 0)),
            pl.BlockSpec((rb, feat), lambda i, j: (i, 0)),
        ],
        out_shape=[jax.ShapeDtypeStruct((rows, feat), jnp.bfloat16)] * 2,
        scratch_shapes=[pltpu.VMEM((rb, feat), jnp.float32)] * 2,
        compiler_params=pltpu.CompilerParams(
            dimension_semantics=("arbitrary", "arbitrary"), vmem_limit_bytes=56 * 1024 * 1024
        ),
    )(x, y, gw, uw, dw)


def _pair_kernel(
    first_ref, a_ref, p_ref, g_ref, u_ref, d_ref, fwd_ref, bwd_ref, acc_o, acc_b
):
    j = pl.program_id(0)

    @pl.when(j == 0)
    def _():
        acc_o[...] = jnp.zeros_like(acc_o)
        acc_b[...] = jnp.zeros_like(acc_b)

    x = a_ref[...]
    y = p_ref[...]
    gw = g_ref[...]
    uw = u_ref[...]
    dw = d_ref[...]
    nt = (((1,), (1,)), ((), ()))
    g = jnp.dot(x, gw, preferred_element_type=jnp.float32)
    u = jnp.dot(x, uw, preferred_element_type=jnp.float32)
    sig = jax.nn.sigmoid(g)
    hidden = (g * sig * u).astype(jnp.bfloat16)
    bh = lax.dot_general(y, dw, nt, preferred_element_type=jnp.float32)
    back_up = (bh * g * sig).astype(jnp.bfloat16)
    back_gate = (bh * u * sig * (1.0 + g * (1.0 - sig))).astype(jnp.bfloat16)
    acc_o[...] += jnp.dot(hidden, dw, preferred_element_type=jnp.float32)
    acc_b[...] += lax.dot_general(
        back_gate, gw, nt, preferred_element_type=jnp.float32
    ) + lax.dot_general(back_up, uw, nt, preferred_element_type=jnp.float32)

    @pl.when(j == pl.num_programs(0) - 1)
    def _():
        fwd_ref[...] = acc_o[...].astype(fwd_ref.dtype)
        bwd_ref[...] = acc_b[...].astype(bwd_ref.dtype)


def expert_pair(first, arrived, partner, gw, uw, dw):
    rows, feat = arrived.shape
    hid = gw.shape[1]
    hb = min(hid, 256)
    full = pl.BlockSpec((rows, feat), lambda j, f: (0, 0))
    grid_spec = pltpu.PrefetchScalarGridSpec(
        num_scalar_prefetch=1,
        grid=(hid // hb,),
        in_specs=[
            full,
            full,
            pl.BlockSpec((feat, hb), lambda j, f: (0, j)),
            pl.BlockSpec((feat, hb), lambda j, f: (0, j)),
            pl.BlockSpec((hb, feat), lambda j, f: (j, 0)),
        ],
        out_specs=[full, full],
        scratch_shapes=[pltpu.VMEM((rows, feat), jnp.float32)] * 2,
    )
    return pl.pallas_call(
        _pair_kernel,
        grid_spec=grid_spec,
        out_shape=[jax.ShapeDtypeStruct((rows, feat), jnp.bfloat16)] * 2,
        compiler_params=pltpu.CompilerParams(
            dimension_semantics=("arbitrary",), vmem_limit_bytes=56 * 1024 * 1024
        ),
    )(first, arrived, partner, gw, uw, dw)


def apply_combine(combine, partial_sums):
    return jnp.dot(combine, partial_sums, precision=lax.Precision.HIGHEST)


def group_perm(expert_count, group_size, shift):
    return [
        (d, (d // group_size) * group_size + (d % group_size + shift) % group_size)
        for d in range(expert_count)
    ]


def group_gather(piece, member, expert_count, group_size):
    got = [piece]
    for shift in range(1, group_size):
        got.append(lax.ppermute(piece, "expert", group_perm(expert_count, group_size, shift)))
    stacked = jnp.stack(got)
    order = (member - jnp.arange(group_size, dtype=jnp.int32)) % group_size
    return jnp.take(stacked, order, axis=0)


def group_reduce_scatter(pieces, member, expert_count, group_size, axis):
    total = lax.dynamic_index_in_dim(pieces, member, axis, keepdims=False).astype(jnp.float32)
    for shift in range(1, group_size):
        target = (member + shift) % group_size
        part = lax.dynamic_index_in_dim(pieces, target, axis, keepdims=False)
        moved = lax.ppermute(part, "expert", group_perm(expert_count, group_size, shift))
        total = total + moved.astype(jnp.float32)
    return total


def butterfly_sum(value, steps):
    done = {}
    for axis, limit in steps:
        size = lax.axis_size(axis)
        if size & (size - 1):
            if axis not in done:
                value = lax.psum(value, axis)
                done[axis] = size
            continue
        bit = done.get(axis, 1)
        while bit < size and (limit is None or bit < 2 * limit):
            value = value + lax.ppermute(value, axis, [(i, i ^ bit) for i in range(size)])
            bit *= 2
        done[axis] = bit
    return value


def by_features(
    normed, out_grad, slot_table, filled, gate_weight, up_weight, down_weight,
    member, expert_count, group_size,
):
    flight, capacity = slot_table.shape
    feature_count = normed.shape[1]
    piece = feature_count // group_size
    packed = jnp.stack(
        [dispatch_rows(normed, slot_table, filled), dispatch_rows(out_grad, slot_table, filled)],
        axis=1,
    )
    sending = (
        packed.reshape(flight, 2, capacity, group_size, piece)
        .transpose(0, 3, 1, 2, 4)
        .reshape(expert_count, 2, capacity, piece)
    )
    arrived = lax.all_to_all(sending, "expert", split_axis=0, concat_axis=0, tiled=True)
    whole = group_gather(arrived, member, expert_count, group_size)
    rows = whole.transpose(1, 2, 3, 0, 4).reshape(expert_count, 2, capacity, feature_count)
    local_rows = rows[:, 0].reshape(expert_count * capacity, feature_count)
    local_grads = rows[:, 1].reshape(expert_count * capacity, feature_count)
    forward, backward = expert_share(local_rows, local_grads, gate_weight, up_weight, down_weight)
    both = jnp.stack(
        [
            forward.reshape(expert_count, capacity, feature_count),
            backward.reshape(expert_count, capacity, feature_count),
        ],
        axis=1,
    ).reshape(expert_count, 2, capacity, group_size, piece)
    summed = group_reduce_scatter(both, member, expert_count, group_size, 3)
    came = lax.all_to_all(
        summed.astype(jnp.bfloat16), "expert", split_axis=0, concat_axis=0, tiled=True
    )
    sums = (
        came.reshape(flight, group_size, 2, capacity, piece)
        .transpose(0, 2, 3, 1, 4)
        .reshape(flight, 2, capacity * feature_count)
        .astype(jnp.float32)
    )
    out_sums = sums[:, 0].reshape(flight * capacity, feature_count)
    grad_sums = sums[:, 1].reshape(flight * capacity, feature_count)
    return out_sums, grad_sums


def exchange(chunks, axis):
    size = lax.axis_size(axis)
    me = lax.axis_index(axis)
    moved = [lax.dynamic_index_in_dim(chunks, me, 0, keepdims=False)]
    for shift in range(1, size):
        part = lax.dynamic_index_in_dim(chunks, (me + shift) % size, 0, keepdims=False)
        moved.append(lax.ppermute(part, axis, [(i, (i + shift) % size) for i in range(size)]))
    stacked = jnp.stack(moved)
    order = (me - jnp.arange(size, dtype=jnp.int32)) % size
    return jnp.take(stacked, order, axis=0)


def pick_rows(values, slot_table, filled):
    token_range = jnp.arange(values.shape[0], dtype=jnp.int32)
    onehot = (slot_table[:, :, None] == token_range[None, None, :]) & filled[:, :, None]
    picked = jnp.einsum(
        "fct,td->fcd", onehot.astype(values.dtype), values, preferred_element_type=jnp.float32
    )
    return picked.astype(values.dtype)


def exchange_relative(chunks, first):
    size = lax.axis_size("expert")
    me = lax.axis_index("expert")
    moved = [lax.dynamic_index_in_dim(chunks, me, 0, keepdims=False)]
    for shift in range(1, size):
        part = lax.dynamic_index_in_dim(chunks, (me + shift) % size, 0, keepdims=False)
        moved.append(lax.ppermute(part, "expert", [(i, (i + shift) % size) for i in range(size)]))
    return jnp.where(first, jnp.stack(moved), jnp.stack(moved[1:] + moved[:1]))


def by_parity(chunks, odd, flight, group_size):
    size = lax.axis_size("expert")
    me = lax.axis_index("expert")
    moved = []
    for shift in range(odd, size, group_size):
        block = (size - me % group_size - shift) % size
        part = lax.dynamic_index_in_dim(chunks, block, 0, keepdims=False)
        if shift == 0:
            moved.append(part)
        else:
            moved.append(lax.ppermute(part, "expert", [(i, (i + shift) % size) for i in range(size)]))
    stacked = jnp.stack(moved)
    chip = me // group_size
    order = (chip + odd * (me % group_size - 1) - jnp.arange(flight, dtype=jnp.int32)) % flight
    return stacked.reshape(flight * chunks.shape[1], chunks.shape[2]), order


def by_pair(
    normed, out_grad, slot_table, filled, gate_weight, up_weight, down_weight,
    member, expert_count, group_size,
):
    flight, capacity = slot_table.shape
    feature_count = normed.shape[1]
    picked = (pick_rows(normed, slot_table, filled), pick_rows(out_grad, slot_table, filled))
    me = lax.axis_index("expert")
    own = []
    for shift in range(expert_count):
        expert = ((me + shift) % expert_count) // group_size
        part = lax.dynamic_index_in_dim(picked[shift % 2], expert, 0, keepdims=False)
        if shift:
            pairs = [(i, (i + shift) % expert_count) for i in range(expert_count)]
            part = lax.ppermute(part, "expert", pairs)
        own.append(part)
    own = jnp.stack(own)
    swap = group_perm(expert_count, group_size, 1)
    partner = lax.ppermute(own, "expert", swap)
    first = member == 0
    even = jnp.where(first, own, partner)
    odd = jnp.where(first, partner, own)
    blocks = range(0, expert_count, 2)
    rows_x = jnp.stack(sum([[even[k], odd[(k + 2) % expert_count]] for k in blocks], []))
    rows_y = jnp.stack(sum([[odd[k + 1], even[k + 1]] for k in blocks], []))
    forward, backward = expert_pair(
        jnp.ones((1,), jnp.int32),
        rows_x.reshape(expert_count * capacity, feature_count),
        rows_y.reshape(expert_count * capacity, feature_count),
        gate_weight,
        up_weight,
        down_weight,
    )
    shape = (expert_count, capacity, feature_count)
    grad_total = backward.astype(jnp.float32) + lax.ppermute(backward, "expert", swap).astype(
        jnp.float32
    )
    grad_sums, grad_order = by_parity(
        grad_total.astype(jnp.bfloat16).reshape(shape), 0, flight, group_size
    )
    out_total = forward.astype(jnp.float32) + lax.ppermute(forward, "expert", swap).astype(
        jnp.float32
    )
    out_sums, out_order = by_parity(
        out_total.astype(jnp.bfloat16).reshape(shape), 1, flight, group_size
    )
    return out_sums.astype(jnp.float32), grad_sums.astype(jnp.float32), out_order, grad_order


def shards(
    tokens,
    steering,
    norm_gain,
    route_ids,
    route_gates,
    gate_weight,
    up_weight,
    down_weight,
    out_grad,
):
    expert_count = lax.axis_size("expert")
    flight = EXP_FLIGHT
    group_size = expert_count // flight
    capacity = CAP
    feature_count = tokens.shape[1]
    piece = feature_count // group_size
    member = lax.axis_index("expert") % group_size
    residual, inverse, normed = normalize(tokens, steering, norm_gain)
    slot_table, filled, combine = slot_tables(route_ids, route_gates, flight, capacity)
    out_combine = combine
    grad_combine = combine
    if group_size == 2:
        out_sums, grad_sums, out_order, grad_order = by_pair(
            normed, out_grad, slot_table, filled, gate_weight, up_weight, down_weight,
            member, expert_count, group_size,
        )
        by_expert = combine.reshape(combine.shape[0], flight, capacity)
        out_combine = jnp.take(by_expert, out_order, axis=1).reshape(combine.shape)
        grad_combine = jnp.take(by_expert, grad_order, axis=1).reshape(combine.shape)
    else:
        out_sums, grad_sums = by_features(
            normed, out_grad, slot_table, filled, gate_weight, up_weight, down_weight,
            member, expert_count, group_size,
        )
    mixture = apply_combine(out_combine, out_sums)
    back_normed = apply_combine(grad_combine, grad_sums)
    layer_out = (residual + mixture).astype(jnp.bfloat16)
    total_grad = norm_backward(residual, inverse, norm_gain, back_normed, out_grad)
    steer_grad = butterfly_sum(
        jnp.sum(total_grad, axis=0), (("expert", 1), ("dp", None), ("expert", None))
    )
    return (layer_out, total_grad.astype(jnp.bfloat16), steer_grad)


def solution(mesh):
    in_specs = (
        P(("dp", "expert"), None),
        P(),
        P(),
        P(("dp", "expert"), None),
        P(("dp", "expert"), None),
        P(None, "expert"),
        P(None, "expert"),
        P("expert", None),
        P(("dp", "expert"), None),
    )
    out_specs = (P(("dp", "expert"), None), P(("dp", "expert"), None), P())
    return jax.shard_map(shards, mesh=mesh, in_specs=in_specs, out_specs=out_specs, check_vma=False)
```
